256 devices in a mesh: pool: 32 (over y, z), tp: 8 (over x, core).
Axes of the slice: x: 4, y: 4, z: 8, core: 2. Of those that a mesh axis runs over, the one named last changes fastest.
Arguments:
- pool_kv: bfloat16 [8192, 8, 2, 16, 128], P('pool', 'tp')
- span_pages: int32 [64, 128], replicated, may hold values from 0 to 8191, as said below
- req_spans: int32 [64, 4], replicated, may hold values from 0 to 63, as said below
- span_offsets: int32 [64, 4], replicated, may hold values from 0 to 6144, as said below
- recompute_rows: int32 [64, 4, 104], replicated, may hold values from 0 to 2047, as said below
- question_lengths: int32 [64], replicated, may hold values from 32 to 64
- question_q: bfloat16 [64, 64, 40, 128], P('pool', None, 'tp')
- question_kv: bfloat16 [64, 64, 2, 8, 128], P('pool', None, None, 'tp')
- recompute_hidden: bfloat16 [64, 4, 104, 5120], P('pool', None, None, 'tp')
- w_kv: bfloat16 [5120, 2, 8, 128], P(None, None, 'tp'), may hold values from -0.25 to 0.25
- w_out: bfloat16 [5120, 5120], P('tp'), may hold values from -0.078125 to 0.078125
Outputs:
- attn_out: bfloat16 [64, 64, 5120], P('pool', None, 'tp')
The draws below stay inside these ranges and needn't reach their ends.
Inputs may be any that keep to these rules, and one draw needn't show every extreme that they name: `span_pages`: page ids are distinct; page p is slot p mod 256 of pool index p // 256; every span has exactly 4 of its pages on each pool index. `req_spans`: the spans of one request are distinct. `span_offsets`: each request's offsets are 2048 times 0 to 3 in some order. `recompute_rows`: the rows of one request's slot are distinct.
All inputs are finite; a program needn't handle non-finite values.
Results may differ from the reference program's by a relative error of at most 0.012.
Values may be sent and summed in bfloat16 or wider, within the bound.
No kernel may reach another device: no remote copies, remote signals or barrier semaphores. Data moves between devices by JAX's collectives and lax.ppermute only.
A program may use at most 192 MiB of HBM per device.

```python
import math
import jax
import jax.numpy as jnp
from jax import lax

D = 5120
H = 40
KVH = 8
HD = 128
PAGE = 16
PAGES_SPAN = 128
SPAN_LEN = 2048
SPANS_REQ = 4
RECOMP = 104
QLEN = 64
SPANS_DEV = 2
REQ = 64
SPANS_POOL = 64
PAGES_DEV = 256
POOL_PAGES = 8192
PAGES_PEER = 4
N_POOL = 32


def page_layout(key):
    base = jax.random.fold_in(key, 101)
    devices = PAGES_SPAN // PAGES_PEER
    order = jax.vmap(lambda each: jax.random.permutation(each, PAGES_SPAN))(jax.random.split(jax.random.fold_in(base, 1), SPANS_POOL))
    owner = order // PAGES_PEER
    within = order % PAGES_PEER
    slots = jax.vmap(lambda each: jax.random.permutation(each, PAGES_DEV))(jax.random.split(jax.random.fold_in(base, 2), devices))
    local = jnp.arange(SPANS_POOL, dtype=jnp.int32)[:, None] * PAGES_PEER + within
    return (owner * PAGES_DEV + slots[owner, local]).astype(jnp.int32)


def draw_span_pages(key, part):
    return page_layout(key)


def draw_req_spans(key, part):
    base = jax.random.fold_in(key, 202)
    popular = jax.random.randint(jax.random.fold_in(base, 1), (SPANS_POOL,), 0, 4) * 4096
    noise = jax.random.randint(jax.random.fold_in(base, 2), (REQ, SPANS_POOL), 0, 12288)
    column_ids = jnp.arange(SPANS_POOL, dtype=jnp.int32)
    score = (popular[None, :] + noise) * SPANS_POOL + column_ids[None, :]
    row_ids = jnp.arange(REQ, dtype=jnp.int32)
    forced = (row_ids[:, None] == 0) & ((column_ids[None, :] == 0) | (column_ids[None, :] == SPANS_POOL - 1))
    score = jnp.where(forced, 1073741824 + column_ids[None, :], score)
    picked = lax.top_k(score, SPANS_REQ)[1]
    return picked.astype(jnp.int32)


def draw_span_offsets(key, part):
    base = jax.random.fold_in(key, 303)
    order = jax.vmap(lambda each: jax.random.permutation(each, SPANS_REQ))(jax.random.split(base, REQ))
    return (order * SPAN_LEN).astype(jnp.int32)


def draw_recompute_rows(key, part):
    base = jax.random.fold_in(key, 404)
    order = jax.vmap(lambda each: jax.random.permutation(each, SPAN_LEN))(jax.random.split(base, REQ * SPANS_REQ))
    drawn = order[:, :RECOMP]
    inner = jax.random.permutation(jax.random.fold_in(base, 7), SPAN_LEN - 2) + 1
    special = jnp.concatenate([jnp.array([0, SPAN_LEN - 1], jnp.int32), inner[:RECOMP - 2].astype(jnp.int32)])
    first = jnp.arange(REQ * SPANS_REQ, dtype=jnp.int32)[:, None] == 0
    rows = jnp.where(first, special[None, :], drawn.astype(jnp.int32))
    return rows.reshape(REQ, SPANS_REQ, RECOMP).astype(jnp.int32)


def draw_question_lengths(key, part):
    base = jax.random.fold_in(key, 505)
    lengths = jax.random.randint(jax.random.fold_in(base, 1), (REQ,), QLEN // 2, QLEN + 1)
    spots = jax.random.permutation(jax.random.fold_in(base, 2), REQ)
    lengths = lengths.at[spots[0]].set(QLEN).at[spots[1]].set(QLEN // 2)
    return lengths.astype(jnp.int32)


def draw_pool_kv(key, part):
    base = jax.random.fold_in(key, 606)
    shape = (POOL_PAGES, KVH, 2, PAGE, HD)
    raw = jnp.clip(jax.random.normal(base, shape, jnp.float32), -6.0, 6.0)
    factor = jnp.array([2.5, 1.0], jnp.float32).reshape(1, 1, 2, 1, 1)
    return (raw * factor).astype(jnp.bfloat16)


def question_keys(key):
    base = jax.random.fold_in(key, 707)
    shape = (REQ, QLEN, 2, KVH, HD)
    raw = jnp.clip(jax.random.normal(base, shape, jnp.float32), -6.0, 6.0)
    raw = raw * jnp.array([4.5, 1.0], jnp.float32).reshape(1, 1, 2, 1, 1)
    return raw


def draw_question_kv(key, part):
    return question_keys(key).astype(jnp.bfloat16)


def draw_question_q(key, part):
    base = jax.random.fold_in(key, 808)
    shape = (REQ, QLEN, H, HD)
    raw = jnp.clip(jax.random.normal(base, shape, jnp.float32), -6.0, 6.0)
    return raw.astype(jnp.bfloat16)


def draw_recompute_hidden(key, part):
    base = jax.random.fold_in(key, 909)
    shape = (REQ, SPANS_REQ, RECOMP, D)
    row_scale = jnp.exp(jax.random.uniform(jax.random.fold_in(base, 1), (REQ, SPANS_REQ, RECOMP, 1), jnp.float32, 0.0, math.log(10.0)))
    column_scale = jnp.exp(jax.random.uniform(jax.random.fold_in(base, 2), (D,), jnp.float32, 0.0, math.log(10.0)))
    raw = jnp.clip(jax.random.normal(jax.random.fold_in(base, 3), shape, jnp.float32), -6.0, 6.0)
    return (raw * row_scale * column_scale).astype(jnp.bfloat16)


def block_levels(key, dims, cuts, low, largest):
    loudness, own = 1.0, jax.random.fold_in(key, 6)
    for axis_at, blocks in cuts:
        draws = jnp.exp(jax.random.uniform(jax.random.fold_in(own, axis_at), (blocks,), jnp.float32, low / len(cuts), largest / len(cuts)))
        loudness = loudness * jnp.repeat(draws, dims[axis_at] // blocks).reshape([-1 if axis == axis_at else 1 for axis in range(len(dims))])
    return loudness


def centred(rng, extent, deviation, most, shards=(), kind=jnp.bfloat16):
    entries = jax.random.normal(rng, extent, jnp.float32) * deviation
    if len(shards) > 0:
        entries = block_levels(rng, extent, shards, -0.22, 0.18) * entries
    return jnp.clip(entries, min=-most, max=most).astype(kind)


def setup_inputs(seed: int = 0) -> dict:
    splits = jax.random.split(jax.random.key(seed), 12)
    pool_kv = draw_pool_kv(jax.random.fold_in(splits[11], 71), 0)
    span_pages = draw_span_pages(jax.random.fold_in(splits[11], 71), 0)
    req_spans = draw_req_spans(jax.random.fold_in(splits[11], 71), 0)
    span_offsets = draw_span_offsets(jax.random.fold_in(splits[11], 71), 0)
    recompute_rows = draw_recompute_rows(jax.random.fold_in(splits[11], 71), 0)
    question_lengths = draw_question_lengths(jax.random.fold_in(splits[11], 71), 0)
    question_q = draw_question_q(jax.random.fold_in(splits[11], 71), 0)
    question_kv = draw_question_kv(jax.random.fold_in(splits[11], 71), 0)
    recompute_hidden = draw_recompute_hidden(jax.random.fold_in(splits[11], 71), 0)
    w_kv = centred(splits[9], (D, 2, KVH, HD), (D // 9) ** -0.5, 0.25, ((2, 8),))
    w_out = centred(splits[10], (H * HD, D), (H * HD) ** -0.5, 0.078125, ((0, 8),))
    return dict(pool_kv=pool_kv, span_pages=span_pages, req_spans=req_spans, span_offsets=span_offsets, recompute_rows=recompute_rows, question_lengths=question_lengths, question_q=question_q, question_kv=question_kv, recompute_hidden=recompute_hidden, w_kv=w_kv, w_out=w_out)


THETA = 1000000.0
NEGATIVE = -1e+30

def rotate(vectors, position):
    halfway = vectors.shape[-1] // 2
    frequency = THETA ** (-(jnp.arange(halfway, dtype=jnp.float32) * 2.0) / vectors.shape[-1])
    angles = position[..., None] * frequency
    cosine_part = jnp.cos(angles)
    sine_part = jnp.sin(angles)
    leading = vectors[..., :halfway]
    trailing = vectors[..., halfway:]
    return jnp.concatenate([leading * cosine_part - trailing * sine_part, trailing * cosine_part + leading * sine_part], axis=-1)

def stored(values):
    return lax.optimization_barrier(values.astype(jnp.bfloat16)).astype(jnp.float32)

def reference(pool_kv, span_pages, req_spans, span_offsets, recompute_rows, question_lengths, question_q, question_kv, recompute_hidden, w_kv, w_out):
    group_size = H // KVH
    span_rows = PAGES_SPAN * PAGE
    peer_pages = PAGES_SPAN // N_POOL
    pages_dev = SPANS_DEV * PAGES_SPAN
    score_scale = HD ** (-0.5)
    qpos = (SPANS_REQ * span_rows + jnp.arange(QLEN, dtype=jnp.int32)).astype(jnp.float32)
    steps_q = jnp.arange(QLEN, dtype=jnp.int32)
    highest = lax.Precision.HIGHEST

    def one_request(request):
        pages = span_pages[req_spans[request]]
        owner = pages // pages_dev
        order = jnp.argsort(owner, axis=-1, stable=True).astype(jnp.int32)
        sorted_pages = jnp.take_along_axis(pages, order, axis=-1)
        cached = pool_kv[sorted_pages].reshape(SPANS_REQ, N_POOL, peer_pages, KVH, 2, PAGE, HD)
        offsets = span_offsets[request].astype(jnp.float32)
        cached_key = stored(rotate(cached[:, :, :, :, 0].astype(jnp.float32), offsets[:, None, None, None, None]))
        cached_value = cached[:, :, :, :, 1].astype(jnp.float32)
        row_ids = order[:, :, None] * PAGE + jnp.arange(PAGE, dtype=jnp.int32)[None, None, :]
        row_ids = row_ids.reshape(SPANS_REQ, N_POOL, peer_pages, PAGE)
        chosen = recompute_rows[request]
        replaced = jnp.any(row_ids[..., None] == chosen[:, None, None, None, :], axis=-1)
        hidden = recompute_hidden[request].astype(jnp.float32)
        normed = stored(hidden * lax.rsqrt(lax.optimization_barrier(jnp.mean(hidden * hidden, axis=-1, keepdims=True)) + 1e-06))
        fresh = jnp.einsum('cnd,dskh->cnskh', normed, w_kv.astype(jnp.float32), precision=highest)
        fresh_pos = offsets[:, None] + chosen.astype(jnp.float32)
        fresh_key = stored(rotate(fresh[:, :, 0], fresh_pos[:, :, None]))
        fresh_value = stored(fresh[:, :, 1])
        query = stored(rotate(question_q[request].astype(jnp.float32), qpos[:, None]))
        own_key = stored(rotate(question_kv[request, :, 0].astype(jnp.float32), qpos[:, None]))
        own_value = question_kv[request, :, 1].astype(jnp.float32)
        grouped = query.reshape(QLEN, KVH, group_size, HD)
        valid = jnp.logical_not(replaced)[None, None, None]
        first_scores = jnp.einsum('qkgd,cepktd->qkgcept', grouped, cached_key, precision=highest) * score_scale
        first_scores = jnp.where(valid, first_scores, NEGATIVE)
        first_peak = lax.optimization_barrier(jnp.max(first_scores, axis=(3, 5, 6)))
        first_exp = jnp.where(valid, jnp.exp(first_scores - first_peak[:, :, :, None, :, None, None]), 0.0)
        first_sum = lax.optimization_barrier(jnp.sum(first_exp, axis=(3, 5, 6)))
        first_num = jnp.einsum('qkgcept,cepktd->qkged', stored(first_exp), cached_value, precision=highest)
        normalised = stored(first_num / jnp.maximum(first_sum, 1.0)[..., None])
        second_scores = jnp.einsum('qkgd,cnkd->qkgcn', grouped, fresh_key, precision=highest) * score_scale
        second_peak = lax.optimization_barrier(jnp.max(second_scores, axis=(3, 4)))
        second_exp = jnp.exp(second_scores - second_peak[:, :, :, None, None])
        second_sum = lax.optimization_barrier(jnp.sum(second_exp, axis=(3, 4)))
        second_num = jnp.einsum('qkgcn,cnkd->qkgd', stored(second_exp), fresh_value, precision=highest)
        third_scores = jnp.einsum('qkgd,jkd->qkgj', grouped, own_key, precision=highest) * score_scale
        length = question_lengths[request]
        visible = ((steps_q[None, :] <= steps_q[:, None]) & (steps_q[None, :] < length))[:, None, None, :]
        third_scores = jnp.where(visible, third_scores, NEGATIVE)
        third_peak = lax.optimization_barrier(jnp.max(third_scores, axis=3))
        third_exp = jnp.where(visible, jnp.exp(third_scores - third_peak[..., None]), 0.0)
        third_sum = lax.optimization_barrier(jnp.sum(third_exp, axis=3))
        third_num = jnp.einsum('qkgj,jkd->qkgd', stored(third_exp), own_value, precision=highest)
        peak = jnp.maximum(jnp.maximum(lax.optimization_barrier(jnp.max(first_peak, axis=3)), second_peak), third_peak)
        first_factor = first_sum * jnp.exp(first_peak - peak[..., None])
        second_factor = jnp.exp(second_peak - peak)
        third_factor = jnp.exp(third_peak - peak)
        weight_sum = lax.optimization_barrier(jnp.sum(first_factor, axis=3)) + second_sum * second_factor + third_sum * third_factor
        numerator = lax.optimization_barrier(jnp.sum(normalised * first_factor[..., None], axis=3)) + second_num * second_factor[..., None] + third_num * third_factor[..., None]
        attn = numerator / weight_sum[..., None]
        attn = jnp.where((steps_q < length)[:, None, None, None], attn, 0.0)
        attn = attn.astype(jnp.bfloat16).reshape(QLEN, H * HD)
        return jnp.dot(attn, w_out, preferred_element_type=jnp.float32).astype(jnp.bfloat16)
    return lax.map(one_request, jnp.arange(REQ, dtype=jnp.int32))
```

```python
import jax
import jax.numpy as jnp
from jax import lax
from jax.sharding import PartitionSpec as P

THETA = 1000000.0
NEGATIVE = -1e30


def rotate(vectors, position):
    halfway = vectors.shape[-1] // 2
    frequency = THETA ** (-(jnp.arange(halfway, dtype=jnp.float32) * 2.0) / vectors.shape[-1])
    angles = position[..., None] * frequency
    cosine_part = jnp.cos(angles)
    sine_part = jnp.sin(angles)
    leading = vectors[..., :halfway]
    trailing = vectors[..., halfway:]
    return jnp.concatenate(
        [
            leading * cosine_part - trailing * sine_part,
            trailing * cosine_part + leading * sine_part,
        ],
        axis=-1,
    )


def summarize(scores, valid):
    masked = jnp.where(valid, scores, NEGATIVE)
    peak = jnp.max(masked, axis=-1)
    powers = jnp.where(valid, jnp.exp(masked - peak[..., None]), 0.0)
    return (peak, jnp.sum(powers, axis=-1), powers.astype(jnp.bfloat16))


def local_pages(pages, device, pages_dev, peer_pages):
    here = pages // pages_dev == device
    ranking = jnp.cumsum(here.astype(jnp.int32), axis=-1) - 1
    picks = here[..., None, :] & (
        ranking[..., None, :] == jnp.arange(peer_pages, dtype=jnp.int32)[:, None]
    )
    slot_ids = jnp.sum(jnp.where(picks, (pages % pages_dev)[..., None, :], 0), axis=-1)
    page_index = jnp.sum(jnp.where(picks, jnp.arange(pages.shape[-1], dtype=jnp.int32), 0), axis=-1)
    return (slot_ids, page_index)


def shards(
    pool_kv,
    span_pages,
    req_spans,
    span_offsets,
    recompute_rows,
    question_lengths,
    question_q,
    question_kv,
    recompute_hidden,
    w_kv,
    w_out,
):
    pool_count = lax.axis_size("pool")
    device = lax.axis_index("pool")
    req_dev = question_q.shape[0]
    qlen = question_q.shape[1]
    heads = question_q.shape[2]
    head_dim = question_q.shape[3]
    pages_dev = pool_kv.shape[0]
    kv_heads = pool_kv.shape[1]
    page_rows = pool_kv.shape[3]
    group_size = heads // kv_heads
    n_req = req_spans.shape[0]
    n_slots = req_spans.shape[1]
    pages_span = span_pages.shape[1]
    span_rows = pages_span * page_rows
    peer_pages = pages_span // pool_count
    score_scale = head_dim ** (-0.5)
    first_request = device * req_dev
    own_offsets = lax.dynamic_slice_in_dim(span_offsets, first_request, req_dev, 0).astype(
        jnp.float32
    )
    own_rows = lax.dynamic_slice_in_dim(recompute_rows, first_request, req_dev, 0)
    own_lengths = lax.dynamic_slice_in_dim(question_lengths, first_request, req_dev, 0)
    steps_q = jnp.arange(qlen, dtype=jnp.int32)
    qpos = (n_slots * span_rows + steps_q).astype(jnp.float32)
    queries = rotate(question_q.astype(jnp.float32), qpos[None, :, None]).astype(jnp.bfloat16)
    grouped = queries.reshape(req_dev, qlen, kv_heads, group_size, head_dim)
    all_queries = lax.all_gather(queries, "pool", axis=0, tiled=True)

    all_pages = span_pages[req_spans]
    slot_ids, page_index = local_pages(all_pages, device, pages_dev, peer_pages)
    local_kv = pool_kv[slot_ids][:, :, :, 0]
    all_offsets = span_offsets.astype(jnp.float32)
    local_keys = rotate(
        local_kv[:, :, :, 0].astype(jnp.float32), all_offsets[:, :, None, None]
    ).astype(jnp.bfloat16)
    local_keys = local_keys.reshape(n_req, -1, head_dim)
    local_values = local_kv[:, :, :, 1].reshape(n_req, -1, head_dim)
    marks = jnp.zeros((n_req, n_slots, span_rows), jnp.bool_)
    marks = marks.at[
        jnp.arange(n_req)[:, None, None], jnp.arange(n_slots)[None, :, None], recompute_rows
    ].set(True)
    row_ids = page_index[..., None] * page_rows + jnp.arange(page_rows, dtype=jnp.int32)
    replaced = jnp.take_along_axis(
        marks, row_ids.reshape(n_req, n_slots, -1), axis=2
    ).reshape(n_req, 1, 1, -1)
    cached_scores = (
        jnp.einsum("rqhd,rkd->rqhk", all_queries, local_keys, preferred_element_type=jnp.float32)
        * score_scale
    )
    part_peak, part_sum, part_weights = summarize(cached_scores, jnp.logical_not(replaced))
    part_acc = jnp.einsum(
        "rqhk,rkd->rqhd", part_weights, local_values, preferred_element_type=jnp.float32
    )
    part_norm = (part_acc / jnp.maximum(part_sum, 1.0)[..., None]).astype(jnp.bfloat16)
    cached_peak = lax.pmax(part_peak, "pool")
    part_weight = part_sum * jnp.exp(part_peak - cached_peak)
    part_num = part_norm.astype(jnp.float32) * part_weight[..., None]
    cached_num = lax.psum_scatter(part_num, "pool", scatter_dimension=0, tiled=True)
    cached_sum = lax.psum_scatter(part_weight, "pool", scatter_dimension=0, tiled=True)
    cached_peak = lax.dynamic_slice_in_dim(cached_peak, first_request, req_dev, 0)
    cached = (
        cached_peak.reshape(req_dev, qlen, kv_heads, group_size),
        cached_sum.reshape(req_dev, qlen, kv_heads, group_size),
        cached_num.reshape(req_dev, qlen, kv_heads, group_size, head_dim),
    )

    own_keys = rotate(question_kv[:, :, 0].astype(jnp.float32), qpos[None, :, None]).astype(
        jnp.bfloat16
    )
    own_values = question_kv[:, :, 1]
    hidden = lax.all_gather(recompute_hidden, "tp", axis=3, tiled=True)
    widened = hidden.astype(jnp.float32)
    normed = (
        widened * lax.rsqrt(jnp.mean(widened * widened, axis=-1, keepdims=True) + 1e-06)
    ).astype(jnp.bfloat16)
    fresh = jnp.einsum("rcnd,dskh->rcnskh", normed, w_kv, preferred_element_type=jnp.float32)
    fresh_pos = own_offsets[:, :, None] + own_rows.astype(jnp.float32)
    fresh_keys = rotate(fresh[:, :, :, 0], fresh_pos[..., None]).astype(jnp.bfloat16)
    fresh_values = fresh[:, :, :, 1].astype(jnp.bfloat16)
    fresh_scores = (
        jnp.einsum("rqkgd,rcnkd->rqkgcn", grouped, fresh_keys, preferred_element_type=jnp.float32)
        * score_scale
    )
    fresh_scores = fresh_scores.reshape(req_dev, qlen, kv_heads, group_size, -1)
    fresh_peak, fresh_sum, fresh_weights = summarize(fresh_scores, True)
    fresh_acc = jnp.einsum(
        "rqkgn,rnkd->rqkgd",
        fresh_weights,
        fresh_values.reshape(req_dev, -1, kv_heads, head_dim),
        preferred_element_type=jnp.float32,
    )
    visible = (steps_q[None, None, :] <= steps_q[None, :, None]) & (
        steps_q[None, None, :] < own_lengths[:, None, None]
    )
    own_scores = (
        jnp.einsum("rqkgd,rjkd->rqkgj", grouped, own_keys, preferred_element_type=jnp.float32)
        * score_scale
    )
    own_peak, own_sum, own_weights = summarize(own_scores, visible[:, :, None, None, :])
    own_acc = jnp.einsum(
        "rqkgj,rjkd->rqkgd", own_weights, own_values, preferred_element_type=jnp.float32
    )

    peak = jnp.maximum(jnp.maximum(cached[0], fresh_peak), own_peak)
    cached_factor = jnp.exp(cached[0] - peak)
    fresh_factor = jnp.exp(fresh_peak - peak)
    own_factor = jnp.exp(own_peak - peak)
    weight_sum = cached[1] * cached_factor + fresh_sum * fresh_factor + own_sum * own_factor
    numerator = (
        cached[2] * cached_factor[..., None]
        + fresh_acc * fresh_factor[..., None]
        + own_acc * own_factor[..., None]
    )
    attn = numerator / weight_sum[..., None]
    live = steps_q[None, :] < own_lengths[:, None]
    attn = (
        jnp.where(live[:, :, None, None, None], attn, 0.0)
        .astype(jnp.bfloat16)
        .reshape(req_dev, qlen, heads * head_dim)
    )
    partial_out = jnp.einsum("rqh,hm->rqm", attn, w_out, preferred_element_type=jnp.float32)
    return lax.psum_scatter(partial_out, "tp", scatter_dimension=2, tiled=True).astype(jnp.bfloat16)


def solution(mesh):
    return jax.shard_map(
        shards,
        mesh=mesh,
        in_specs=(
            P("pool", "tp", None, None, None),
            P(),
            P(),
            P(),
            P(),
            P(),
            P("pool", None, "tp", None),
            P("pool", None, None, "tp", None),
            P("pool", None, None, "tp"),
            P(None, None, "tp", None),
            P("tp", None),
        ),
        out_specs=P("pool", None, "tp"),
        check_vma=False,
    )
```

```python
import functools

import jax
import jax.numpy as jnp
from jax import lax
from jax.experimental import pallas as pl
from jax.experimental.pallas import tpu as pltpu
from jax.sharding import PartitionSpec as P

THETA = 1000000.0
NEGATIVE = -1e30


def rotate(vectors, position):
    halfway = vectors.shape[-1] // 2
    frequency = THETA ** (-(jnp.arange(halfway, dtype=jnp.float32) * 2.0) / vectors.shape[-1])
    angles = position[..., None] * frequency
    cosine_part = jnp.cos(angles)
    sine_part = jnp.sin(angles)
    leading = vectors[..., :halfway]
    trailing = vectors[..., halfway:]
    return jnp.concatenate(
        [
            leading * cosine_part - trailing * sine_part,
            trailing * cosine_part + leading * sine_part,
        ],
        axis=-1,
    )


def summarize(scores, valid):
    masked = jnp.where(valid, scores, NEGATIVE)
    peak = jnp.max(masked, axis=-1)
    powers = jnp.where(valid, jnp.exp(masked - peak[..., None]), 0.0)
    return (peak, jnp.sum(powers, axis=-1), powers.astype(jnp.bfloat16))


def combine(former, latter):
    peak = jnp.maximum(former[0], latter[0])
    former_factor = jnp.exp(former[0] - peak)
    latter_factor = jnp.exp(latter[0] - peak)
    return (
        peak,
        former[1] * former_factor + latter[1] * latter_factor,
        former[2] * former_factor[..., None] + latter[2] * latter_factor[..., None],
    )


def merge_normalised(peaks, sums, normalised, axis):
    merged_peak = jnp.max(peaks, axis=axis)
    weight = sums * jnp.exp(peaks - jnp.expand_dims(merged_peak, axis))
    return (
        merged_peak,
        jnp.sum(weight, axis=axis),
        jnp.sum(normalised.astype(jnp.float32) * weight[..., None], axis=axis),
    )


def local_pages(pages, device, pages_dev, peer_pages):
    here = pages // pages_dev == device
    ranking = jnp.cumsum(here.astype(jnp.int32), axis=-1) - 1
    picks = here[..., None, :] & (
        ranking[..., None, :] == jnp.arange(peer_pages, dtype=jnp.int32)[:, None]
    )
    slot_ids = jnp.sum(jnp.where(picks, (pages % pages_dev)[..., None, :], 0), axis=-1)
    page_index = jnp.sum(jnp.where(picks, jnp.arange(pages.shape[-1], dtype=jnp.int32), 0), axis=-1)
    return (slot_ids, page_index)


def frequencies(head_dim):
    halfway = head_dim // 2
    return THETA ** (-(jnp.arange(halfway, dtype=jnp.float32) * 2.0) / head_dim)


SET_BLOCK = 8


def cached_kernel(scale, q_ref, kv_ref, valid_ref, table_ref, peak_ref, sum_ref, num_ref, m_acc, w_acc, n_acc):
    block = pl.program_id(1)
    n_blocks = pl.num_programs(1)
    n_pages = kv_ref.shape[2]
    page_rows = kv_ref.shape[4]
    head_dim = kv_ref.shape[5]
    n_slots = table_ref.shape[1] // 2
    slot_rows = (n_pages // n_slots) * page_rows

    @pl.when(block == 0)
    def _():
        m_acc[...] = jnp.full(m_acc.shape, NEGATIVE, jnp.float32)
        w_acc[...] = jnp.zeros(w_acc.shape, jnp.float32)
        n_acc[...] = jnp.zeros(n_acc.shape, jnp.float32)

    query = q_ref[0]
    table = table_ref[0]
    cosine = jnp.concatenate(
        [jnp.broadcast_to(table[2 * c : 2 * c + 1], (slot_rows, head_dim)) for c in range(n_slots)], axis=0
    )
    sine = jnp.concatenate(
        [jnp.broadcast_to(table[2 * c + 1 : 2 * c + 2], (slot_rows, head_dim)) for c in range(n_slots)], axis=0
    )

    def one_set(i, carry):
        keys = kv_ref[i, 0, :, 0].reshape(n_pages * page_rows, head_dim).astype(jnp.float32)
        values = kv_ref[i, 0, :, 1].reshape(n_pages * page_rows, head_dim)
        keys = (keys * cosine + pltpu.roll(keys, head_dim // 2, 1) * sine).astype(jnp.bfloat16)
        scores = lax.dot_general(
            query, keys, (((1,), (1,)), ((), ())), preferred_element_type=jnp.float32
        ) * scale
        valid = valid_ref[0, pl.ds(i, 1), :] > 0.5
        masked = jnp.where(valid, scores, NEGATIVE)
        peak = jnp.max(masked, axis=1, keepdims=True)
        powers = jnp.where(valid, jnp.exp(masked - peak), 0.0)
        total = jnp.sum(powers, axis=1, keepdims=True)
        acc = jnp.dot(powers.astype(jnp.bfloat16), values, preferred_element_type=jnp.float32)
        normalised = (acc / jnp.maximum(total, 1.0)).astype(jnp.bfloat16).astype(jnp.float32)
        old = m_acc[...]
        merged = jnp.maximum(old, peak)
        rescale = jnp.exp(old - merged)
        weight = total * jnp.exp(peak - merged)
        m_acc[...] = merged
        w_acc[...] = w_acc[...] * rescale + weight
        n_acc[...] = n_acc[...] * rescale + normalised * weight
        return carry

    lax.fori_loop(0, kv_ref.shape[0], one_set, 0)

    @pl.when(block == n_blocks - 1)
    def _():
        peak_ref[0] = m_acc[...]
        sum_ref[0] = w_acc[...]
        num_ref[0] = n_acc[...]


def cached_attention(queries, arrived, valid, tables, scale):
    req_dev, rows, head_dim = queries.shape
    pool_count = arrived.shape[0]
    kv_block = (SET_BLOCK,) + (1,) + arrived.shape[2:]
    return pl.pallas_call(
        functools.partial(cached_kernel, scale),
        grid=(req_dev, pool_count // SET_BLOCK),
        in_specs=[
            pl.BlockSpec((1, rows, head_dim), lambda r, j: (r, 0, 0)),
            pl.BlockSpec(kv_block, lambda r, j: (j, r, 0, 0, 0, 0)),
            pl.BlockSpec((1, SET_BLOCK, valid.shape[2]), lambda r, j: (r, j, 0)),
            pl.BlockSpec((1,) + tables.shape[1:], lambda r, j: (r, 0, 0)),
        ],
        out_specs=[
            pl.BlockSpec((1, rows, 1), lambda r, j: (r, 0, 0)),
            pl.BlockSpec((1, rows, 1), lambda r, j: (r, 0, 0)),
            pl.BlockSpec((1, rows, head_dim), lambda r, j: (r, 0, 0)),
        ],
        out_shape=[
            jax.ShapeDtypeStruct((req_dev, rows, 1), jnp.float32),
            jax.ShapeDtypeStruct((req_dev, rows, 1), jnp.float32),
            jax.ShapeDtypeStruct((req_dev, rows, head_dim), jnp.float32),
        ],
        scratch_shapes=[
            pltpu.VMEM((rows, 1), jnp.float32),
            pltpu.VMEM((rows, 1), jnp.float32),
            pltpu.VMEM((rows, head_dim), jnp.float32),
        ],
        compiler_params=pltpu.CompilerParams(dimension_semantics=("parallel", "arbitrary")),
    )(queries, arrived, valid, tables)


def shards(
    pool_kv,
    span_pages,
    req_spans,
    span_offsets,
    recompute_rows,
    question_lengths,
    question_q,
    question_kv,
    recompute_hidden,
    w_kv,
    w_out,
):
    pool_count = lax.axis_size("pool")
    device = lax.axis_index("pool")
    req_dev = question_q.shape[0]
    qlen = question_q.shape[1]
    heads = question_q.shape[2]
    head_dim = question_q.shape[3]
    pages_dev = pool_kv.shape[0]
    kv_heads = pool_kv.shape[1]
    page_rows = pool_kv.shape[3]
    group_size = heads // kv_heads
    n_slots = req_spans.shape[1]
    pages_span = span_pages.shape[1]
    span_rows = pages_span * page_rows
    peer_pages = pages_span // pool_count
    score_scale = head_dim ** (-0.5)
    first_request = device * req_dev
    own_spans = lax.dynamic_slice_in_dim(req_spans, first_request, req_dev, 0)
    own_offsets = lax.dynamic_slice_in_dim(span_offsets, first_request, req_dev, 0).astype(
        jnp.float32
    )
    own_rows = lax.dynamic_slice_in_dim(recompute_rows, first_request, req_dev, 0)
    own_lengths = lax.dynamic_slice_in_dim(question_lengths, first_request, req_dev, 0)
    steps_q = jnp.arange(qlen, dtype=jnp.int32)
    qpos = (n_slots * span_rows + steps_q).astype(jnp.float32)
    queries = rotate(question_q.astype(jnp.float32), qpos[None, :, None]).astype(jnp.bfloat16)
    grouped = queries.reshape(req_dev, qlen, kv_heads, group_size, head_dim)
    own_keys = rotate(question_kv[:, :, 0].astype(jnp.float32), qpos[None, :, None]).astype(
        jnp.bfloat16
    )
    own_values = question_kv[:, :, 1]
    hidden = lax.all_gather(recompute_hidden, "tp", axis=3, tiled=True)
    widened = hidden.astype(jnp.float32)
    normed = (
        widened * lax.rsqrt(jnp.mean(widened * widened, axis=-1, keepdims=True) + 1e-06)
    ).astype(jnp.bfloat16)
    fresh = jnp.einsum("rcnd,dskh->rcnskh", normed, w_kv, preferred_element_type=jnp.float32)
    fresh_pos = own_offsets[:, :, None] + own_rows.astype(jnp.float32)
    fresh_keys = rotate(fresh[:, :, :, 0], fresh_pos[..., None]).astype(jnp.bfloat16)
    fresh_values = fresh[:, :, :, 1].astype(jnp.bfloat16)
    fresh_scores = (
        jnp.einsum("rqkgd,rcnkd->rqkgcn", grouped, fresh_keys, preferred_element_type=jnp.float32)
        * score_scale
    )
    fresh_scores = fresh_scores.reshape(req_dev, qlen, kv_heads, group_size, -1)
    fresh_peak, fresh_sum, fresh_weights = summarize(fresh_scores, True)
    fresh_acc = jnp.einsum(
        "rqkgn,rnkd->rqkgd",
        fresh_weights,
        fresh_values.reshape(req_dev, -1, kv_heads, head_dim),
        preferred_element_type=jnp.float32,
    )
    visible = (steps_q[None, None, :] <= steps_q[None, :, None]) & (
        steps_q[None, None, :] < own_lengths[:, None, None]
    )
    own_scores = (
        jnp.einsum("rqkgd,rjkd->rqkgj", grouped, own_keys, preferred_element_type=jnp.float32)
        * score_scale
    )
    own_peak, own_sum, own_weights = summarize(own_scores, visible[:, :, None, None, :])
    own_acc = jnp.einsum(
        "rqkgj,rjkd->rqkgd", own_weights, own_values, preferred_element_type=jnp.float32
    )
    all_pages = span_pages[req_spans]
    slot_ids, unused_index = local_pages(all_pages, device, pages_dev, peer_pages)
    outgoing = pool_kv[slot_ids]
    outgoing = outgoing.reshape((pool_count, req_dev) + outgoing.shape[1:])
    arrived = lax.all_to_all(outgoing, "pool", split_axis=0, concat_axis=0, tiled=True)
    mine = span_pages[own_spans]
    unused_slots, page_index = local_pages(
        mine[:, :, None, :], jnp.arange(pool_count, dtype=jnp.int32)[:, None], pages_dev, peer_pages
    )
    row_ids = page_index[..., None] * page_rows + jnp.arange(page_rows, dtype=jnp.int32)
    replaced = jnp.any(row_ids[..., None] == own_rows[:, :, None, None, None, :], axis=-1)
    valid = jnp.logical_not(replaced).transpose(0, 2, 1, 3, 4).reshape(req_dev, pool_count, -1)
    angles = own_offsets[..., None] * frequencies(head_dim)
    tables = jnp.stack(
        [
            jnp.concatenate([jnp.cos(angles), jnp.cos(angles)], axis=-1),
            jnp.concatenate([-jnp.sin(angles), jnp.sin(angles)], axis=-1),
        ],
        axis=2,
    ).reshape(req_dev, 2 * n_slots, head_dim)
    cached = cached_attention(
        queries.reshape(req_dev, qlen * heads, head_dim),
        arrived.reshape(pool_count, req_dev, n_slots * peer_pages, 2, page_rows, head_dim),
        valid.astype(jnp.float32),
        tables,
        score_scale,
    )
    cached = (
        cached[0].reshape(req_dev, qlen, kv_heads, group_size),
        cached[1].reshape(req_dev, qlen, kv_heads, group_size),
        cached[2].reshape(req_dev, qlen, kv_heads, group_size, head_dim),
    )
    total = combine(
        combine(cached, (fresh_peak, fresh_sum, fresh_acc)), (own_peak, own_sum, own_acc)
    )
    attn = total[2] / total[1][..., None]
    live = steps_q[None, :] < own_lengths[:, None]
    attn = (
        jnp.where(live[:, :, None, None, None], attn, 0.0)
        .astype(jnp.bfloat16)
        .reshape(req_dev, qlen, heads * head_dim)
    )
    partial_out = jnp.einsum("rqh,hm->rqm", attn, w_out, preferred_element_type=jnp.float32)
    return lax.psum_scatter(partial_out, "tp", scatter_dimension=2, tiled=True).astype(jnp.bfloat16)


def solution(mesh):
    return jax.shard_map(
        shards,
        mesh=mesh,
        in_specs=(
            P("pool", "tp", None, None, None),
            P(),
            P(),
            P(),
            P(),
            P(),
            P("pool", None, "tp", None),
            P("pool", None, None, "tp", None),
            P("pool", None, None, "tp"),
            P(None, None, "tp", None),
            P("tp", None),
        ),
        out_specs=P("pool", None, "tp"),
        check_vma=False,
    )
```

```python
import functools

import jax
import jax.numpy as jnp
from jax import lax
from jax.experimental import pallas as pl
from jax.experimental.pallas import tpu as pltpu
from jax.sharding import PartitionSpec as P

THETA = 1000000.0
NEGATIVE = -1e30


def rotate(vectors, position):
    halfway = vectors.shape[-1] // 2
    frequency = THETA ** (-(jnp.arange(halfway, dtype=jnp.float32) * 2.0) / vectors.shape[-1])
    angles = position[..., None] * frequency
    cosine_part = jnp.cos(angles)
    sine_part = jnp.sin(angles)
    leading = vectors[..., :halfway]
    trailing = vectors[..., halfway:]
    return jnp.concatenate(
        [
            leading * cosine_part - trailing * sine_part,
            trailing * cosine_part + leading * sine_part,
        ],
        axis=-1,
    )


def summarize(scores, valid):
    masked = jnp.where(valid, scores, NEGATIVE)
    peak = jnp.max(masked, axis=-1)
    powers = jnp.where(valid, jnp.exp(masked - peak[..., None]), 0.0)
    return (peak, jnp.sum(powers, axis=-1), powers.astype(jnp.bfloat16))


def combine(former, latter):
    peak = jnp.maximum(former[0], latter[0])
    former_factor = jnp.exp(former[0] - peak)
    latter_factor = jnp.exp(latter[0] - peak)
    return (
        peak,
        former[1] * former_factor + latter[1] * latter_factor,
        former[2] * former_factor[..., None] + latter[2] * latter_factor[..., None],
    )


def merge_normalised(peaks, sums, normalised, axis):
    merged_peak = jnp.max(peaks, axis=axis)
    weight = sums * jnp.exp(peaks - jnp.expand_dims(merged_peak, axis))
    return (
        merged_peak,
        jnp.sum(weight, axis=axis),
        jnp.sum(normalised.astype(jnp.float32) * weight[..., None], axis=axis),
    )


def local_pages(pages, device, pages_dev, peer_pages):
    here = pages // pages_dev == device
    ranking = jnp.cumsum(here.astype(jnp.int32), axis=-1) - 1
    picks = here[..., None, :] & (
        ranking[..., None, :] == jnp.arange(peer_pages, dtype=jnp.int32)[:, None]
    )
    slot_ids = jnp.sum(jnp.where(picks, (pages % pages_dev)[..., None, :], 0), axis=-1)
    page_index = jnp.sum(jnp.where(picks, jnp.arange(pages.shape[-1], dtype=jnp.int32), 0), axis=-1)
    return (slot_ids, page_index)


def frequencies(head_dim):
    halfway = head_dim // 2
    return THETA ** (-(jnp.arange(halfway, dtype=jnp.float32) * 2.0) / head_dim)


SET_BLOCK = 8


def cached_kernel(scale, q_ref, kv_ref, valid_ref, table_ref, peak_ref, sum_ref, num_ref, m_acc, w_acc, n_acc):
    block = pl.program_id(1)
    n_blocks = pl.num_programs(1)
    n_pages = kv_ref.shape[2]
    page_rows = kv_ref.shape[4]
    head_dim = kv_ref.shape[5]
    n_slots = table_ref.shape[1] // 2
    slot_rows = (n_pages // n_slots) * page_rows

    @pl.when(block == 0)
    def _():
        m_acc[...] = jnp.full(m_acc.shape, NEGATIVE, jnp.float32)
        w_acc[...] = jnp.zeros(w_acc.shape, jnp.float32)
        n_acc[...] = jnp.zeros(n_acc.shape, jnp.float32)

    query = q_ref[0]
    table = table_ref[0]
    cosine = jnp.concatenate(
        [jnp.broadcast_to(table[2 * c : 2 * c + 1], (slot_rows, head_dim)) for c in range(n_slots)], axis=0
    )
    sine = jnp.concatenate(
        [jnp.broadcast_to(table[2 * c + 1 : 2 * c + 2], (slot_rows, head_dim)) for c in range(n_slots)], axis=0
    )

    def one_set(i, carry):
        keys = kv_ref[i, 0, :, 0].reshape(n_pages * page_rows, head_dim).astype(jnp.float32)
        values = kv_ref[i, 0, :, 1].reshape(n_pages * page_rows, head_dim)
        keys = (keys * cosine + pltpu.roll(keys, head_dim // 2, 1) * sine).astype(jnp.bfloat16)
        scores = lax.dot_general(
            query, keys, (((1,), (1,)), ((), ())), preferred_element_type=jnp.float32
        ) * scale
        valid = valid_ref[0, pl.ds(i, 1), :] > 0.5
        masked = jnp.where(valid, scores, NEGATIVE)
        peak = jnp.max(masked, axis=1, keepdims=True)
        powers = jnp.where(valid, jnp.exp(masked - peak), 0.0)
        total = jnp.sum(powers, axis=1, keepdims=True)
        acc = jnp.dot(powers.astype(jnp.bfloat16), values, preferred_element_type=jnp.float32)
        normalised = (acc / jnp.maximum(total, 1.0)).astype(jnp.bfloat16).astype(jnp.float32)
        old = m_acc[...]
        merged = jnp.maximum(old, peak)
        rescale = jnp.exp(old - merged)
        weight = total * jnp.exp(peak - merged)
        m_acc[...] = merged
        w_acc[...] = w_acc[...] * rescale + weight
        n_acc[...] = n_acc[...] * rescale + normalised * weight
        return carry

    lax.fori_loop(0, kv_ref.shape[0], one_set, 0)

    @pl.when(block == n_blocks - 1)
    def _():
        peak_ref[0] = m_acc[...]
        sum_ref[0] = w_acc[...]
        num_ref[0] = n_acc[...]


def cached_attention(queries, arrived, valid, tables, scale):
    req_dev, rows, head_dim = queries.shape
    pool_count = arrived.shape[0]
    kv_block = (SET_BLOCK,) + (1,) + arrived.shape[2:]
    return pl.pallas_call(
        functools.partial(cached_kernel, scale),
        grid=(req_dev, pool_count // SET_BLOCK),
        in_specs=[
            pl.BlockSpec((1, rows, head_dim), lambda r, j: (r, 0, 0)),
            pl.BlockSpec(kv_block, lambda r, j: (j, r, 0, 0, 0, 0)),
            pl.BlockSpec((1, SET_BLOCK, valid.shape[2]), lambda r, j: (r, j, 0)),
            pl.BlockSpec((1,) + tables.shape[1:], lambda r, j: (r, 0, 0)),
        ],
        out_specs=[
            pl.BlockSpec((1, rows, 1), lambda r, j: (r, 0, 0)),
            pl.BlockSpec((1, rows, 1), lambda r, j: (r, 0, 0)),
            pl.BlockSpec((1, rows, head_dim), lambda r, j: (r, 0, 0)),
        ],
        out_shape=[
            jax.ShapeDtypeStruct((req_dev, rows, 1), jnp.float32),
            jax.ShapeDtypeStruct((req_dev, rows, 1), jnp.float32),
            jax.ShapeDtypeStruct((req_dev, rows, head_dim), jnp.float32),
        ],
        scratch_shapes=[
            pltpu.VMEM((rows, 1), jnp.float32),
            pltpu.VMEM((rows, 1), jnp.float32),
            pltpu.VMEM((rows, head_dim), jnp.float32),
        ],
        compiler_params=pltpu.CompilerParams(dimension_semantics=("parallel", "arbitrary")),
    )(queries, arrived, valid, tables)


def shards(
    pool_kv,
    span_pages,
    req_spans,
    span_offsets,
    recompute_rows,
    question_lengths,
    question_q,
    question_kv,
    recompute_hidden,
    w_kv,
    w_out,
):
    pool_count = lax.axis_size("pool")
    device = lax.axis_index("pool")
    req_dev = question_q.shape[0]
    qlen = question_q.shape[1]
    heads = question_q.shape[2]
    head_dim = question_q.shape[3]
    pages_dev = pool_kv.shape[0]
    kv_heads = pool_kv.shape[1]
    page_rows = pool_kv.shape[3]
    group_size = heads // kv_heads
    n_slots = req_spans.shape[1]
    pages_span = span_pages.shape[1]
    span_rows = pages_span * page_rows
    peer_pages = pages_span // pool_count
    score_scale = head_dim ** (-0.5)
    first_request = device * req_dev
    own_spans = lax.dynamic_slice_in_dim(req_spans, first_request, req_dev, 0)
    own_offsets = lax.dynamic_slice_in_dim(span_offsets, first_request, req_dev, 0).astype(
        jnp.float32
    )
    own_rows = lax.dynamic_slice_in_dim(recompute_rows, first_request, req_dev, 0)
    own_lengths = lax.dynamic_slice_in_dim(question_lengths, first_request, req_dev, 0)
    steps_q = jnp.arange(qlen, dtype=jnp.int32)
    qpos = (n_slots * span_rows + steps_q).astype(jnp.float32)
    queries = rotate(question_q.astype(jnp.float32), qpos[None, :, None]).astype(jnp.bfloat16)
    grouped = queries.reshape(req_dev, qlen, kv_heads, group_size, head_dim)
    own_keys = rotate(question_kv[:, :, 0].astype(jnp.float32), qpos[None, :, None]).astype(
        jnp.bfloat16
    )
    own_values = question_kv[:, :, 1]
    hidden = lax.all_gather(recompute_hidden, "tp", axis=3, tiled=True)
    widened = hidden.astype(jnp.float32)
    normed = (
        widened * lax.rsqrt(jnp.mean(widened * widened, axis=-1, keepdims=True) + 1e-06)
    ).astype(jnp.bfloat16)
    fresh = jnp.einsum("rcnd,dskh->rcnskh", normed, w_kv, preferred_element_type=jnp.float32)
    fresh_pos = own_offsets[:, :, None] + own_rows.astype(jnp.float32)
    fresh_keys = rotate(fresh[:, :, :, 0], fresh_pos[..., None]).astype(jnp.bfloat16)
    fresh_values = fresh[:, :, :, 1].astype(jnp.bfloat16)
    fresh_scores = (
        jnp.einsum("rqkgd,rcnkd->rqkgcn", grouped, fresh_keys, preferred_element_type=jnp.float32)
        * score_scale
    )
    fresh_scores = fresh_scores.reshape(req_dev, qlen, kv_heads, group_size, -1)
    fresh_peak, fresh_sum, fresh_weights = summarize(fresh_scores, True)
    fresh_acc = jnp.einsum(
        "rqkgn,rnkd->rqkgd",
        fresh_weights,
        fresh_values.reshape(req_dev, -1, kv_heads, head_dim),
        preferred_element_type=jnp.float32,
    )
    visible = (steps_q[None, None, :] <= steps_q[None, :, None]) & (
        steps_q[None, None, :] < own_lengths[:, None, None]
    )
    own_scores = (
        jnp.einsum("rqkgd,rjkd->rqkgj", grouped, own_keys, preferred_element_type=jnp.float32)
        * score_scale
    )
    own_peak, own_sum, own_weights = summarize(own_scores, visible[:, :, None, None, :])
    own_acc = jnp.einsum(
        "rqkgj,rjkd->rqkgd", own_weights, own_values, preferred_element_type=jnp.float32
    )
    all_pages = span_pages[req_spans]
    slot_ids, unused_index = local_pages(all_pages, device, pages_dev, peer_pages)
    slot_ids = slot_ids.reshape((pool_count, req_dev) + slot_ids.shape[1:])
    arrivals = []
    for r in range(req_dev):
        outgoing = pool_kv[slot_ids[:, r]]
        if arrivals:
            arrivals[-1], outgoing = lax.optimization_barrier((arrivals[-1], outgoing))
        arrivals.append(lax.all_to_all(outgoing, "pool", split_axis=0, concat_axis=0, tiled=True))
    mine = span_pages[own_spans]
    unused_slots, page_index = local_pages(
        mine[:, :, None, :], jnp.arange(pool_count, dtype=jnp.int32)[:, None], pages_dev, peer_pages
    )
    row_ids = page_index[..., None] * page_rows + jnp.arange(page_rows, dtype=jnp.int32)
    replaced = jnp.any(row_ids[..., None] == own_rows[:, :, None, None, None, :], axis=-1)
    valid = jnp.logical_not(replaced).transpose(0, 2, 1, 3, 4).reshape(req_dev, pool_count, -1)
    angles = own_offsets[..., None] * frequencies(head_dim)
    tables = jnp.stack(
        [
            jnp.concatenate([jnp.cos(angles), jnp.cos(angles)], axis=-1),
            jnp.concatenate([-jnp.sin(angles), jnp.sin(angles)], axis=-1),
        ],
        axis=2,
    ).reshape(req_dev, 2 * n_slots, head_dim)
    flat_queries = queries.reshape(req_dev, qlen * heads, head_dim)
    parts = [
        cached_attention(
            flat_queries[r : r + 1],
            arrivals[r].reshape(pool_count, 1, n_slots * peer_pages, 2, page_rows, head_dim),
            valid[r : r + 1].astype(jnp.float32),
            tables[r : r + 1],
            score_scale,
        )
        for r in range(req_dev)
    ]
    cached = [jnp.concatenate([part[i] for part in parts], axis=0) for i in range(3)]
    cached = (
        cached[0].reshape(req_dev, qlen, kv_heads, group_size),
        cached[1].reshape(req_dev, qlen, kv_heads, group_size),
        cached[2].reshape(req_dev, qlen, kv_heads, group_size, head_dim),
    )
    total = combine(
        combine(cached, (fresh_peak, fresh_sum, fresh_acc)), (own_peak, own_sum, own_acc)
    )
    attn = total[2] / total[1][..., None]
    live = steps_q[None, :] < own_lengths[:, None]
    attn = (
        jnp.where(live[:, :, None, None, None], attn, 0.0)
        .astype(jnp.bfloat16)
        .reshape(req_dev, qlen, heads * head_dim)
    )
    partial_out = jnp.einsum("rqh,hm->rqm", attn, w_out, preferred_element_type=jnp.float32)
    return lax.psum_scatter(partial_out, "tp", scatter_dimension=2, tiled=True).astype(jnp.bfloat16)


def solution(mesh):
    return jax.shard_map(
        shards,
        mesh=mesh,
        in_specs=(
            P("pool", "tp", None, None, None),
            P(),
            P(),
            P(),
            P(),
            P(),
            P("pool", None, "tp", None),
            P("pool", None, None, "tp", None),
            P("pool", None, None, "tp"),
            P(None, None, "tp", None),
            P("tp", None),
        ),
        out_specs=P("pool", None, "tp"),
        check_vma=False,
    )
```

```python
import functools

import jax
import jax.numpy as jnp
from jax import lax
from jax.experimental import pallas as pl
from jax.experimental.pallas import tpu as pltpu
from jax.sharding import PartitionSpec as P

THETA = 1000000.0
NEGATIVE = -1e30


def rotate(vectors, position):
    halfway = vectors.shape[-1] // 2
    frequency = THETA ** (-(jnp.arange(halfway, dtype=jnp.float32) * 2.0) / vectors.shape[-1])
    angles = position[..., None] * frequency
    cosine_part = jnp.cos(angles)
    sine_part = jnp.sin(angles)
    leading = vectors[..., :halfway]
    trailing = vectors[..., halfway:]
    return jnp.concatenate(
        [
            leading * cosine_part - trailing * sine_part,
            trailing * cosine_part + leading * sine_part,
        ],
        axis=-1,
    )


def summarize(scores, valid):
    masked = jnp.where(valid, scores, NEGATIVE)
    peak = jnp.max(masked, axis=-1)
    powers = jnp.where(valid, jnp.exp(masked - peak[..., None]), 0.0)
    return (peak, jnp.sum(powers, axis=-1), powers.astype(jnp.bfloat16))


def combine(former, latter):
    peak = jnp.maximum(former[0], latter[0])
    former_factor = jnp.exp(former[0] - peak)
    latter_factor = jnp.exp(latter[0] - peak)
    return (
        peak,
        former[1] * former_factor + latter[1] * latter_factor,
        former[2] * former_factor[..., None] + latter[2] * latter_factor[..., None],
    )


def merge_normalised(peaks, sums, normalised, axis):
    merged_peak = jnp.max(peaks, axis=axis)
    weight = sums * jnp.exp(peaks - jnp.expand_dims(merged_peak, axis))
    return (
        merged_peak,
        jnp.sum(weight, axis=axis),
        jnp.sum(normalised.astype(jnp.float32) * weight[..., None], axis=axis),
    )


def local_pages(pages, device, pages_dev, peer_pages):
    here = pages // pages_dev == device
    ranking = jnp.cumsum(here.astype(jnp.int32), axis=-1) - 1
    picks = here[..., None, :] & (
        ranking[..., None, :] == jnp.arange(peer_pages, dtype=jnp.int32)[:, None]
    )
    slot_ids = jnp.sum(jnp.where(picks, (pages % pages_dev)[..., None, :], 0), axis=-1)
    page_index = jnp.sum(jnp.where(picks, jnp.arange(pages.shape[-1], dtype=jnp.int32), 0), axis=-1)
    return (slot_ids, page_index)


def frequencies(head_dim):
    halfway = head_dim // 2
    return THETA ** (-(jnp.arange(halfway, dtype=jnp.float32) * 2.0) / head_dim)


SET_BLOCK = 8


def cached_kernel(scale, q_ref, kv_ref, valid_ref, table_ref, peak_ref, sum_ref, num_ref, m_acc, w_acc, n_acc):
    block = pl.program_id(1)
    n_blocks = pl.num_programs(1)
    n_pages = kv_ref.shape[2]
    page_rows = kv_ref.shape[4]
    head_dim = kv_ref.shape[5]
    n_slots = table_ref.shape[1] // 2
    slot_rows = (n_pages // n_slots) * page_rows

    @pl.when(block == 0)
    def _():
        m_acc[...] = jnp.full(m_acc.shape, NEGATIVE, jnp.float32)
        w_acc[...] = jnp.zeros(w_acc.shape, jnp.float32)
        n_acc[...] = jnp.zeros(n_acc.shape, jnp.float32)

    query = q_ref[0]
    table = table_ref[0]
    cosine = jnp.concatenate(
        [jnp.broadcast_to(table[2 * c : 2 * c + 1], (slot_rows, head_dim)) for c in range(n_slots)], axis=0
    )
    sine = jnp.concatenate(
        [jnp.broadcast_to(table[2 * c + 1 : 2 * c + 2], (slot_rows, head_dim)) for c in range(n_slots)], axis=0
    )

    def one_set(i, carry):
        keys = kv_ref[i, 0, :, 0].reshape(n_pages * page_rows, head_dim).astype(jnp.float32)
        values = kv_ref[i, 0, :, 1].reshape(n_pages * page_rows, head_dim)
        keys = (keys * cosine + pltpu.roll(keys, head_dim // 2, 1) * sine).astype(jnp.bfloat16)
        scores = lax.dot_general(
            query, keys, (((1,), (1,)), ((), ())), preferred_element_type=jnp.float32
        ) * scale
        valid = valid_ref[0, pl.ds(i, 1), :] > 0.5
        masked = jnp.where(valid, scores, NEGATIVE)
        peak = jnp.max(masked, axis=1, keepdims=True)
        powers = jnp.where(valid, jnp.exp(masked - peak), 0.0)
        total = jnp.sum(powers, axis=1, keepdims=True)
        acc = jnp.dot(powers.astype(jnp.bfloat16), values, preferred_element_type=jnp.float32)
        normalised = (acc / jnp.maximum(total, 1.0)).astype(jnp.bfloat16).astype(jnp.float32)
        old = m_acc[...]
        merged = jnp.maximum(old, peak)
        rescale = jnp.exp(old - merged)
        weight = total * jnp.exp(peak - merged)
        m_acc[...] = merged
        w_acc[...] = w_acc[...] * rescale + weight
        n_acc[...] = n_acc[...] * rescale + normalised * weight
        return carry

    lax.fori_loop(0, kv_ref.shape[0], one_set, 0)

    @pl.when(block == n_blocks - 1)
    def _():
        peak_ref[0] = m_acc[...]
        sum_ref[0] = w_acc[...]
        num_ref[0] = n_acc[...]


def cached_attention(queries, arrived, valid, tables, scale):
    req_dev, rows, head_dim = queries.shape
    pool_count = arrived.shape[0]
    kv_block = (SET_BLOCK,) + (1,) + arrived.shape[2:]
    return pl.pallas_call(
        functools.partial(cached_kernel, scale),
        grid=(req_dev, pool_count // SET_BLOCK),
        in_specs=[
            pl.BlockSpec((1, rows, head_dim), lambda r, j: (r, 0, 0)),
            pl.BlockSpec(kv_block, lambda r, j: (j, r, 0, 0, 0, 0)),
            pl.BlockSpec((1, SET_BLOCK, valid.shape[2]), lambda r, j: (r, j, 0)),
            pl.BlockSpec((1,) + tables.shape[1:], lambda r, j: (r, 0, 0)),
        ],
        out_specs=[
            pl.BlockSpec((1, rows, 1), lambda r, j: (r, 0, 0)),
            pl.BlockSpec((1, rows, 1), lambda r, j: (r, 0, 0)),
            pl.BlockSpec((1, rows, head_dim), lambda r, j: (r, 0, 0)),
        ],
        out_shape=[
            jax.ShapeDtypeStruct((req_dev, rows, 1), jnp.float32),
            jax.ShapeDtypeStruct((req_dev, rows, 1), jnp.float32),
            jax.ShapeDtypeStruct((req_dev, rows, head_dim), jnp.float32),
        ],
        scratch_shapes=[
            pltpu.VMEM((rows, 1), jnp.float32),
            pltpu.VMEM((rows, 1), jnp.float32),
            pltpu.VMEM((rows, head_dim), jnp.float32),
        ],
        compiler_params=pltpu.CompilerParams(dimension_semantics=("parallel", "arbitrary")),
    )(queries, arrived, valid, tables)


def shards(
    pool_kv,
    span_pages,
    req_spans,
    span_offsets,
    recompute_rows,
    question_lengths,
    question_q,
    question_kv,
    recompute_hidden,
    w_kv,
    w_out,
):
    pool_count = lax.axis_size("pool")
    device = lax.axis_index("pool")
    req_dev = question_q.shape[0]
    qlen = question_q.shape[1]
    heads = question_q.shape[2]
    head_dim = question_q.shape[3]
    pages_dev = pool_kv.shape[0]
    kv_heads = pool_kv.shape[1]
    page_rows = pool_kv.shape[3]
    group_size = heads // kv_heads
    n_slots = req_spans.shape[1]
    pages_span = span_pages.shape[1]
    span_rows = pages_span * page_rows
    peer_pages = pages_span // pool_count
    score_scale = head_dim ** (-0.5)
    first_request = device * req_dev
    own_spans = lax.dynamic_slice_in_dim(req_spans, first_request, req_dev, 0)
    own_offsets = lax.dynamic_slice_in_dim(span_offsets, first_request, req_dev, 0).astype(
        jnp.float32
    )
    own_rows = lax.dynamic_slice_in_dim(recompute_rows, first_request, req_dev, 0)
    own_lengths = lax.dynamic_slice_in_dim(question_lengths, first_request, req_dev, 0)
    steps_q = jnp.arange(qlen, dtype=jnp.int32)
    qpos = (n_slots * span_rows + steps_q).astype(jnp.float32)
    queries = rotate(question_q.astype(jnp.float32), qpos[None, :, None]).astype(jnp.bfloat16)
    grouped = queries.reshape(req_dev, qlen, kv_heads, group_size, head_dim)
    own_keys = rotate(question_kv[:, :, 0].astype(jnp.float32), qpos[None, :, None]).astype(
        jnp.bfloat16
    )
    own_values = question_kv[:, :, 1]
    hidden = lax.all_gather(recompute_hidden, "tp", axis=3, tiled=True)
    widened = hidden.astype(jnp.float32)
    normed = (
        widened * lax.rsqrt(jnp.mean(widened * widened, axis=-1, keepdims=True) + 1e-06)
    ).astype(jnp.bfloat16)
    fresh = jnp.einsum("rcnd,dskh->rcnskh", normed, w_kv, preferred_element_type=jnp.float32)
    fresh_pos = own_offsets[:, :, None] + own_rows.astype(jnp.float32)
    fresh_keys = rotate(fresh[:, :, :, 0], fresh_pos[..., None]).astype(jnp.bfloat16)
    fresh_values = fresh[:, :, :, 1].astype(jnp.bfloat16)
    fresh_scores = (
        jnp.einsum("rqkgd,rcnkd->rqkgcn", grouped, fresh_keys, preferred_element_type=jnp.float32)
        * score_scale
    )
    fresh_scores = fresh_scores.reshape(req_dev, qlen, kv_heads, group_size, -1)
    fresh_peak, fresh_sum, fresh_weights = summarize(fresh_scores, True)
    fresh_acc = jnp.einsum(
        "rqkgn,rnkd->rqkgd",
        fresh_weights,
        fresh_values.reshape(req_dev, -1, kv_heads, head_dim),
        preferred_element_type=jnp.float32,
    )
    visible = (steps_q[None, None, :] <= steps_q[None, :, None]) & (
        steps_q[None, None, :] < own_lengths[:, None, None]
    )
    own_scores = (
        jnp.einsum("rqkgd,rjkd->rqkgj", grouped, own_keys, preferred_element_type=jnp.float32)
        * score_scale
    )
    own_peak, own_sum, own_weights = summarize(own_scores, visible[:, :, None, None, :])
    own_acc = jnp.einsum(
        "rqkgj,rjkd->rqkgd", own_weights, own_values, preferred_element_type=jnp.float32
    )
    own_keys = rotate(question_kv[:, :, 0].astype(jnp.float32), qpos[None, :, None]).astype(
        jnp.bfloat16
    )
    own_values = question_kv[:, :, 1]
    hidden = lax.all_gather(recompute_hidden, "tp", axis=3, tiled=True)
    widened = hidden.astype(jnp.float32)
    normed = (
        widened * lax.rsqrt(jnp.mean(widened * widened, axis=-1, keepdims=True) + 1e-06)
    ).astype(jnp.bfloat16)
    fresh = jnp.einsum("rcnd,dskh->rcnskh", normed, w_kv, preferred_element_type=jnp.float32)
    fresh_pos = own_offsets[:, :, None] + own_rows.astype(jnp.float32)
    fresh_keys = rotate(fresh[:, :, :, 0], fresh_pos[..., None]).astype(jnp.bfloat16)
    fresh_values = fresh[:, :, :, 1].astype(jnp.bfloat16)
    fresh_scores = (
        jnp.einsum("rqkgd,rcnkd->rqkgcn", grouped, fresh_keys, preferred_element_type=jnp.float32)
        * score_scale
    )
    fresh_scores = fresh_scores.reshape(req_dev, qlen, kv_heads, group_size, -1)
    fresh_peak, fresh_sum, fresh_weights = summarize(fresh_scores, True)
    fresh_acc = jnp.einsum(
        "rqkgn,rnkd->rqkgd",
        fresh_weights,
        fresh_values.reshape(req_dev, -1, kv_heads, head_dim),
        preferred_element_type=jnp.float32,
    )
    visible = (steps_q[None, None, :] <= steps_q[None, :, None]) & (
        steps_q[None, None, :] < own_lengths[:, None, None]
    )
    own_scores = (
        jnp.einsum("rqkgd,rjkd->rqkgj", grouped, own_keys, preferred_element_type=jnp.float32)
        * score_scale
    )
    own_peak, own_sum, own_weights = summarize(own_scores, visible[:, :, None, None, :])
    own_acc = jnp.einsum(
        "rqkgj,rjkd->rqkgd", own_weights, own_values, preferred_element_type=jnp.float32
    )

    mine = span_pages[own_spans]
    unused_slots, page_index = local_pages(
        mine[:, :, None, :], jnp.arange(pool_count, dtype=jnp.int32)[:, None], pages_dev, peer_pages
    )
    row_ids = page_index[..., None] * page_rows + jnp.arange(page_rows, dtype=jnp.int32)
    replaced = jnp.any(row_ids[..., None] == own_rows[:, :, None, None, None, :], axis=-1)
    valid = jnp.logical_not(replaced).transpose(0, 2, 1, 3, 4).reshape(req_dev, pool_count, -1)
    valid = valid.astype(jnp.float32)
    angles = own_offsets[..., None] * frequencies(head_dim)
    tables = jnp.stack(
        [
            jnp.concatenate([jnp.cos(angles), jnp.cos(angles)], axis=-1),
            jnp.concatenate([-jnp.sin(angles), jnp.sin(angles)], axis=-1),
        ],
        axis=2,
    ).reshape(req_dev, 2 * n_slots, head_dim)
    local = (fresh_peak, fresh_sum, fresh_acc, own_peak, own_sum, own_acc, valid, tables)

    all_pages = span_pages[req_spans]
    slot_ids, unused_index = local_pages(all_pages, device, pages_dev, peer_pages)
    slot_ids = slot_ids.reshape((pool_count, req_dev) + slot_ids.shape[1:])
    arrivals = []
    for r in range(req_dev):
        outgoing = pool_kv[slot_ids[:, r]]
        if arrivals:
            arrivals[-1], outgoing, local = lax.optimization_barrier((arrivals[-1], outgoing, local))
        arrivals.append(lax.all_to_all(outgoing, "pool", split_axis=0, concat_axis=0, tiled=True))
    fresh_peak, fresh_sum, fresh_acc, own_peak, own_sum, own_acc, valid, tables = local

    flat_queries = queries.reshape(req_dev, qlen * heads, head_dim)
    outputs = []
    for r in range(req_dev):
        one = slice(r, r + 1)
        arrived = arrivals[r]
        if outputs:
            arrived, outputs[-1] = lax.optimization_barrier((arrived, outputs[-1]))
        cached = cached_attention(
            flat_queries[one],
            arrived.reshape(pool_count, 1, n_slots * peer_pages, 2, page_rows, head_dim),
            valid[one],
            tables[one],
            score_scale,
        )
        cached = (
            cached[0].reshape(1, qlen, kv_heads, group_size),
            cached[1].reshape(1, qlen, kv_heads, group_size),
            cached[2].reshape(1, qlen, kv_heads, group_size, head_dim),
        )
        total = combine(
            combine(cached, (fresh_peak[one], fresh_sum[one], fresh_acc[one])),
            (own_peak[one], own_sum[one], own_acc[one]),
        )
        attn = total[2] / total[1][..., None]
        live = steps_q < own_lengths[r]
        attn = (
            jnp.where(live[None, :, None, None, None], attn, 0.0)
            .astype(jnp.bfloat16)
            .reshape(1, qlen, heads * head_dim)
        )
        partial_out = jnp.einsum("rqh,hm->rqm", attn, w_out, preferred_element_type=jnp.float32)
        outputs.append(
            lax.psum_scatter(partial_out, "tp", scatter_dimension=2, tiled=True).astype(jnp.bfloat16)
        )
    return jnp.concatenate(outputs, axis=0)


def solution(mesh):
    return jax.shard_map(
        shards,
        mesh=mesh,
        in_specs=(
            P("pool", "tp", None, None, None),
            P(),
            P(),
            P(),
            P(),
            P(),
            P("pool", None, "tp", None),
            P("pool", None, None, "tp", None),
            P("pool", None, None, "tp"),
            P(None, None, "tp", None),
            P("tp", None),
        ),
        out_specs=P("pool", None, "tp"),
        check_vma=False,
    )
```

```python
import functools

import jax
import jax.numpy as jnp
from jax import lax
from jax.experimental import pallas as pl
from jax.experimental.pallas import tpu as pltpu
from jax.sharding import PartitionSpec as P

THETA = 1000000.0
NEGATIVE = -1e30


def rotate(vectors, position):
    halfway = vectors.shape[-1] // 2
    frequency = THETA ** (-(jnp.arange(halfway, dtype=jnp.float32) * 2.0) / vectors.shape[-1])
    angles = position[..., None] * frequency
    cosine_part = jnp.cos(angles)
    sine_part = jnp.sin(angles)
    leading = vectors[..., :halfway]
    trailing = vectors[..., halfway:]
    return jnp.concatenate(
        [
            leading * cosine_part - trailing * sine_part,
            trailing * cosine_part + leading * sine_part,
        ],
        axis=-1,
    )


def summarize(scores, valid):
    masked = jnp.where(valid, scores, NEGATIVE)
    peak = jnp.max(masked, axis=-1)
    powers = jnp.where(valid, jnp.exp(masked - peak[..., None]), 0.0)
    return (peak, jnp.sum(powers, axis=-1), powers.astype(jnp.bfloat16))


def combine(former, latter):
    peak = jnp.maximum(former[0], latter[0])
    former_factor = jnp.exp(former[0] - peak)
    latter_factor = jnp.exp(latter[0] - peak)
    return (
        peak,
        former[1] * former_factor + latter[1] * latter_factor,
        former[2] * former_factor[..., None] + latter[2] * latter_factor[..., None],
    )


def merge_normalised(peaks, sums, normalised, axis):
    merged_peak = jnp.max(peaks, axis=axis)
    weight = sums * jnp.exp(peaks - jnp.expand_dims(merged_peak, axis))
    return (
        merged_peak,
        jnp.sum(weight, axis=axis),
        jnp.sum(normalised.astype(jnp.float32) * weight[..., None], axis=axis),
    )


def local_pages(pages, device, pages_dev, peer_pages):
    here = pages // pages_dev == device
    ranking = jnp.cumsum(here.astype(jnp.int32), axis=-1) - 1
    picks = here[..., None, :] & (
        ranking[..., None, :] == jnp.arange(peer_pages, dtype=jnp.int32)[:, None]
    )
    slot_ids = jnp.sum(jnp.where(picks, (pages % pages_dev)[..., None, :], 0), axis=-1)
    page_index = jnp.sum(jnp.where(picks, jnp.arange(pages.shape[-1], dtype=jnp.int32), 0), axis=-1)
    return (slot_ids, page_index)


def frequencies(head_dim):
    halfway = head_dim // 2
    return THETA ** (-(jnp.arange(halfway, dtype=jnp.float32) * 2.0) / head_dim)


SET_BLOCK = 8


def cached_kernel(scale, q_ref, kv_ref, valid_ref, table_ref, peak_ref, sum_ref, num_ref, m_acc, w_acc, n_acc):
    block = pl.program_id(1)
    n_blocks = pl.num_programs(1)
    n_pages = kv_ref.shape[2]
    page_rows = kv_ref.shape[4]
    head_dim = kv_ref.shape[5]
    n_slots = table_ref.shape[1] // 2
    slot_rows = (n_pages // n_slots) * page_rows

    @pl.when(block == 0)
    def _():
        m_acc[...] = jnp.full(m_acc.shape, NEGATIVE, jnp.float32)
        w_acc[...] = jnp.zeros(w_acc.shape, jnp.float32)
        n_acc[...] = jnp.zeros(n_acc.shape, jnp.float32)

    query = q_ref[0]
    table = table_ref[0]
    cosine = jnp.concatenate(
        [jnp.broadcast_to(table[2 * c : 2 * c + 1], (slot_rows, head_dim)) for c in range(n_slots)], axis=0
    )
    sine = jnp.concatenate(
        [jnp.broadcast_to(table[2 * c + 1 : 2 * c + 2], (slot_rows, head_dim)) for c in range(n_slots)], axis=0
    )

    def one_set(i, carry):
        keys = kv_ref[i, 0, :, 0].reshape(n_pages * page_rows, head_dim).astype(jnp.float32)
        values = kv_ref[i, 0, :, 1].reshape(n_pages * page_rows, head_dim)
        keys = (keys * cosine + pltpu.roll(keys, head_dim // 2, 1) * sine).astype(jnp.bfloat16)
        scores = lax.dot_general(
            query, keys, (((1,), (1,)), ((), ())), preferred_element_type=jnp.float32
        ) * scale
        valid = valid_ref[0, pl.ds(i, 1), :] > 0.5
        masked = jnp.where(valid, scores, NEGATIVE)
        peak = jnp.max(masked, axis=1, keepdims=True)
        powers = jnp.where(valid, jnp.exp(masked - peak), 0.0)
        total = jnp.sum(powers, axis=1, keepdims=True)
        acc = jnp.dot(powers.astype(jnp.bfloat16), values, preferred_element_type=jnp.float32)
        normalised = (acc / jnp.maximum(total, 1.0)).astype(jnp.bfloat16).astype(jnp.float32)
        old = m_acc[...]
        merged = jnp.maximum(old, peak)
        rescale = jnp.exp(old - merged)
        weight = total * jnp.exp(peak - merged)
        m_acc[...] = merged
        w_acc[...] = w_acc[...] * rescale + weight
        n_acc[...] = n_acc[...] * rescale + normalised * weight
        return carry

    lax.fori_loop(0, kv_ref.shape[0], one_set, 0)

    @pl.when(block == n_blocks - 1)
    def _():
        peak_ref[0] = m_acc[...]
        sum_ref[0] = w_acc[...]
        num_ref[0] = n_acc[...]


def cached_attention(queries, arrived, valid, tables, scale):
    req_dev, rows, head_dim = queries.shape
    pool_count = arrived.shape[0]
    kv_block = (SET_BLOCK,) + (1,) + arrived.shape[2:]
    return pl.pallas_call(
        functools.partial(cached_kernel, scale),
        grid=(req_dev, pool_count // SET_BLOCK),
        in_specs=[
            pl.BlockSpec((1, rows, head_dim), lambda r, j: (r, 0, 0)),
            pl.BlockSpec(kv_block, lambda r, j: (j, r, 0, 0, 0, 0)),
            pl.BlockSpec((1, SET_BLOCK, valid.shape[2]), lambda r, j: (r, j, 0)),
            pl.BlockSpec((1,) + tables.shape[1:], lambda r, j: (r, 0, 0)),
        ],
        out_specs=[
            pl.BlockSpec((1, rows, 1), lambda r, j: (r, 0, 0)),
            pl.BlockSpec((1, rows, 1), lambda r, j: (r, 0, 0)),
            pl.BlockSpec((1, rows, head_dim), lambda r, j: (r, 0, 0)),
        ],
        out_shape=[
            jax.ShapeDtypeStruct((req_dev, rows, 1), jnp.float32),
            jax.ShapeDtypeStruct((req_dev, rows, 1), jnp.float32),
            jax.ShapeDtypeStruct((req_dev, rows, head_dim), jnp.float32),
        ],
        scratch_shapes=[
            pltpu.VMEM((rows, 1), jnp.float32),
            pltpu.VMEM((rows, 1), jnp.float32),
            pltpu.VMEM((rows, head_dim), jnp.float32),
        ],
        compiler_params=pltpu.CompilerParams(dimension_semantics=("parallel", "arbitrary")),
    )(queries, arrived, valid, tables)


def shards(
    pool_kv,
    span_pages,
    req_spans,
    span_offsets,
    recompute_rows,
    question_lengths,
    question_q,
    question_kv,
    recompute_hidden,
    w_kv,
    w_out,
):
    pool_count = lax.axis_size("pool")
    device = lax.axis_index("pool")
    req_dev = question_q.shape[0]
    qlen = question_q.shape[1]
    heads = question_q.shape[2]
    head_dim = question_q.shape[3]
    pages_dev = pool_kv.shape[0]
    kv_heads = pool_kv.shape[1]
    page_rows = pool_kv.shape[3]
    group_size = heads // kv_heads
    n_slots = req_spans.shape[1]
    pages_span = span_pages.shape[1]
    span_rows = pages_span * page_rows
    peer_pages = pages_span // pool_count
    score_scale = head_dim ** (-0.5)
    first_request = device * req_dev
    own_spans = lax.dynamic_slice_in_dim(req_spans, first_request, req_dev, 0)
    own_offsets = lax.dynamic_slice_in_dim(span_offsets, first_request, req_dev, 0).astype(
        jnp.float32
    )
    own_rows = lax.dynamic_slice_in_dim(recompute_rows, first_request, req_dev, 0)
    own_lengths = lax.dynamic_slice_in_dim(question_lengths, first_request, req_dev, 0)
    steps_q = jnp.arange(qlen, dtype=jnp.int32)
    qpos = (n_slots * span_rows + steps_q).astype(jnp.float32)
    queries = rotate(question_q.astype(jnp.float32), qpos[None, :, None]).astype(jnp.bfloat16)
    grouped = queries.reshape(req_dev, qlen, kv_heads, group_size, head_dim)
    own_keys = rotate(question_kv[:, :, 0].astype(jnp.float32), qpos[None, :, None]).astype(
        jnp.bfloat16
    )
    own_values = question_kv[:, :, 1]
    hidden = lax.all_gather(recompute_hidden, "tp", axis=3, tiled=True)
    widened = hidden.astype(jnp.float32)
    normed = (
        widened * lax.rsqrt(jnp.mean(widened * widened, axis=-1, keepdims=True) + 1e-06)
    ).astype(jnp.bfloat16)
    fresh = jnp.einsum("rcnd,dskh->rcnskh", normed, w_kv, preferred_element_type=jnp.float32)
    fresh_pos = own_offsets[:, :, None] + own_rows.astype(jnp.float32)
    fresh_keys = rotate(fresh[:, :, :, 0], fresh_pos[..., None]).astype(jnp.bfloat16)
    fresh_values = fresh[:, :, :, 1].astype(jnp.bfloat16)
    fresh_scores = (
        jnp.einsum("rqkgd,rcnkd->rqkgcn", grouped, fresh_keys, preferred_element_type=jnp.float32)
        * score_scale
    )
    fresh_scores = fresh_scores.reshape(req_dev, qlen, kv_heads, group_size, -1)
    fresh_peak, fresh_sum, fresh_weights = summarize(fresh_scores, True)
    fresh_acc = jnp.einsum(
        "rqkgn,rnkd->rqkgd",
        fresh_weights,
        fresh_values.reshape(req_dev, -1, kv_heads, head_dim),
        preferred_element_type=jnp.float32,
    )
    visible = (steps_q[None, None, :] <= steps_q[None, :, None]) & (
        steps_q[None, None, :] < own_lengths[:, None, None]
    )
    own_scores = (
        jnp.einsum("rqkgd,rjkd->rqkgj", grouped, own_keys, preferred_element_type=jnp.float32)
        * score_scale
    )
    own_peak, own_sum, own_weights = summarize(own_scores, visible[:, :, None, None, :])
    own_acc = jnp.einsum(
        "rqkgj,rjkd->rqkgd", own_weights, own_values, preferred_element_type=jnp.float32
    )
    own_keys = rotate(question_kv[:, :, 0].astype(jnp.float32), qpos[None, :, None]).astype(
        jnp.bfloat16
    )
    own_values = question_kv[:, :, 1]
    hidden = lax.all_gather(recompute_hidden, "tp", axis=3, tiled=True)
    widened = hidden.astype(jnp.float32)
    normed = (
        widened * lax.rsqrt(jnp.mean(widened * widened, axis=-1, keepdims=True) + 1e-06)
    ).astype(jnp.bfloat16)
    fresh = jnp.einsum("rcnd,dskh->rcnskh", normed, w_kv, preferred_element_type=jnp.float32)
    fresh_pos = own_offsets[:, :, None] + own_rows.astype(jnp.float32)
    fresh_keys = rotate(fresh[:, :, :, 0], fresh_pos[..., None]).astype(jnp.bfloat16)
    fresh_values = fresh[:, :, :, 1].astype(jnp.bfloat16)
    fresh_scores = (
        jnp.einsum("rqkgd,rcnkd->rqkgcn", grouped, fresh_keys, preferred_element_type=jnp.float32)
        * score_scale
    )
    fresh_scores = fresh_scores.reshape(req_dev, qlen, kv_heads, group_size, -1)
    fresh_peak, fresh_sum, fresh_weights = summarize(fresh_scores, True)
    fresh_acc = jnp.einsum(
        "rqkgn,rnkd->rqkgd",
        fresh_weights,
        fresh_values.reshape(req_dev, -1, kv_heads, head_dim),
        preferred_element_type=jnp.float32,
    )
    visible = (steps_q[None, None, :] <= steps_q[None, :, None]) & (
        steps_q[None, None, :] < own_lengths[:, None, None]
    )
    own_scores = (
        jnp.einsum("rqkgd,rjkd->rqkgj", grouped, own_keys, preferred_element_type=jnp.float32)
        * score_scale
    )
    own_peak, own_sum, own_weights = summarize(own_scores, visible[:, :, None, None, :])
    own_acc = jnp.einsum(
        "rqkgj,rjkd->rqkgd", own_weights, own_values, preferred_element_type=jnp.float32
    )

    mine = span_pages[own_spans]
    unused_slots, page_index = local_pages(
        mine[:, :, None, :], jnp.arange(pool_count, dtype=jnp.int32)[:, None], pages_dev, peer_pages
    )
    row_ids = page_index[..., None] * page_rows + jnp.arange(page_rows, dtype=jnp.int32)
    replaced = jnp.any(row_ids[..., None] == own_rows[:, :, None, None, None, :], axis=-1)
    valid = jnp.logical_not(replaced).transpose(0, 2, 1, 3, 4).reshape(req_dev, pool_count, -1)
    valid = valid.astype(jnp.float32)
    angles = own_offsets[..., None] * frequencies(head_dim)
    tables = jnp.stack(
        [
            jnp.concatenate([jnp.cos(angles), jnp.cos(angles)], axis=-1),
            jnp.concatenate([-jnp.sin(angles), jnp.sin(angles)], axis=-1),
        ],
        axis=2,
    ).reshape(req_dev, 2 * n_slots, head_dim)
    local = (fresh_peak, fresh_sum, fresh_acc, own_peak, own_sum, own_acc, valid, tables)

    all_pages = span_pages[req_spans]
    slot_ids, unused_index = local_pages(all_pages, device, pages_dev, peer_pages)
    slot_ids = slot_ids.reshape((pool_count, req_dev) + slot_ids.shape[1:])
    arrivals = []
    for r in range(req_dev):
        outgoing = pool_kv[slot_ids[:, r]]
        if arrivals:
            arrivals[-1], outgoing, local = lax.optimization_barrier((arrivals[-1], outgoing, local))
        arrivals.append(lax.all_to_all(outgoing, "pool", split_axis=0, concat_axis=0, tiled=True))
    fresh_peak, fresh_sum, fresh_acc, own_peak, own_sum, own_acc, valid, tables = local

    tp_count = lax.axis_size("tp")
    out_cols = w_out.shape[1] // tp_count
    rank = lax.axis_index("tp")
    blocks = w_out.reshape(w_out.shape[0], tp_count, out_cols)
    shifted = []
    for k in range(tp_count):
        piece = lax.dynamic_index_in_dim(blocks, (rank + k) % tp_count, axis=1, keepdims=False)
        if k:
            piece = lax.ppermute(
                piece, "tp", [(i, (i + k) % tp_count) for i in range(tp_count)]
            )
        shifted.append(piece)
    columns = jnp.stack(shifted)
    flat_queries = queries.reshape(req_dev, qlen * heads, head_dim)
    outputs = []
    for r in range(req_dev):
        one = slice(r, r + 1)
        arrived = arrivals[r]
        if outputs:
            arrived, outputs[-1] = lax.optimization_barrier((arrived, outputs[-1]))
        cached = cached_attention(
            flat_queries[one],
            arrived.reshape(pool_count, 1, n_slots * peer_pages, 2, page_rows, head_dim),
            valid[one],
            tables[one],
            score_scale,
        )
        cached = (
            cached[0].reshape(1, qlen, kv_heads, group_size),
            cached[1].reshape(1, qlen, kv_heads, group_size),
            cached[2].reshape(1, qlen, kv_heads, group_size, head_dim),
        )
        total = combine(
            combine(cached, (fresh_peak[one], fresh_sum[one], fresh_acc[one])),
            (own_peak[one], own_sum[one], own_acc[one]),
        )
        attn = total[2] / total[1][..., None]
        live = steps_q < own_lengths[r]
        attn = (
            jnp.where(live[None, :, None, None, None], attn, 0.0)
            .astype(jnp.bfloat16)
            .reshape(qlen, heads * head_dim)
        )
        gathered = jnp.stack(
            [attn]
            + [
                lax.ppermute(attn, "tp", [(i, (i + k) % tp_count) for i in range(tp_count)])
                for k in range(1, tp_count)
            ]
        )
        out = jnp.einsum("tqh,thm->qm", gathered, columns, preferred_element_type=jnp.float32)
        outputs.append(out.astype(jnp.bfloat16)[None])
    return jnp.concatenate(outputs, axis=0)


def solution(mesh):
    return jax.shard_map(
        shards,
        mesh=mesh,
        in_specs=(
            P("pool", "tp", None, None, None),
            P(),
            P(),
            P(),
            P(),
            P(),
            P("pool", None, "tp", None),
            P("pool", None, None, "tp", None),
            P("pool", None, None, "tp"),
            P(None, None, "tp", None),
            P("tp", None),
        ),
        out_specs=P("pool", None, "tp"),
        check_vma=False,
    )
```

```python
import functools

import jax
import jax.numpy as jnp
from jax import lax
from jax.experimental import pallas as pl
from jax.experimental.pallas import tpu as pltpu
from jax.sharding import PartitionSpec as P

THETA = 1000000.0
NEGATIVE = -1e30


def rotate(vectors, position):
    halfway = vectors.shape[-1] // 2
    frequency = THETA ** (-(jnp.arange(halfway, dtype=jnp.float32) * 2.0) / vectors.shape[-1])
    angles = position[..., None] * frequency
    cosine_part = jnp.cos(angles)
    sine_part = jnp.sin(angles)
    leading = vectors[..., :halfway]
    trailing = vectors[..., halfway:]
    return jnp.concatenate(
        [
            leading * cosine_part - trailing * sine_part,
            trailing * cosine_part + leading * sine_part,
        ],
        axis=-1,
    )


def summarize(scores, valid):
    masked = jnp.where(valid, scores, NEGATIVE)
    peak = jnp.max(masked, axis=-1)
    powers = jnp.where(valid, jnp.exp(masked - peak[..., None]), 0.0)
    return (peak, jnp.sum(powers, axis=-1), powers.astype(jnp.bfloat16))


def combine(former, latter):
    peak = jnp.maximum(former[0], latter[0])
    former_factor = jnp.exp(former[0] - peak)
    latter_factor = jnp.exp(latter[0] - peak)
    return (
        peak,
        former[1] * former_factor + latter[1] * latter_factor,
        former[2] * former_factor[..., None] + latter[2] * latter_factor[..., None],
    )


def merge_normalised(peaks, sums, normalised, axis):
    merged_peak = jnp.max(peaks, axis=axis)
    weight = sums * jnp.exp(peaks - jnp.expand_dims(merged_peak, axis))
    return (
        merged_peak,
        jnp.sum(weight, axis=axis),
        jnp.sum(normalised.astype(jnp.float32) * weight[..., None], axis=axis),
    )


def local_pages(pages, device, pages_dev, peer_pages):
    here = pages // pages_dev == device
    ranking = jnp.cumsum(here.astype(jnp.int32), axis=-1) - 1
    picks = here[..., None, :] & (
        ranking[..., None, :] == jnp.arange(peer_pages, dtype=jnp.int32)[:, None]
    )
    slot_ids = jnp.sum(jnp.where(picks, (pages % pages_dev)[..., None, :], 0), axis=-1)
    page_index = jnp.sum(jnp.where(picks, jnp.arange(pages.shape[-1], dtype=jnp.int32), 0), axis=-1)
    return (slot_ids, page_index)


def frequencies(head_dim):
    halfway = head_dim // 2
    return THETA ** (-(jnp.arange(halfway, dtype=jnp.float32) * 2.0) / head_dim)


SET_BLOCK = 8


def cached_kernel(scale, q_ref, kv_ref, valid_ref, table_ref, peak_ref, sum_ref, num_ref, m_acc, w_acc, n_acc):
    block = pl.program_id(1)
    n_blocks = pl.num_programs(1)
    n_pages = kv_ref.shape[2]
    page_rows = kv_ref.shape[4]
    head_dim = kv_ref.shape[5]
    n_slots = table_ref.shape[1] // 2
    slot_rows = (n_pages // n_slots) * page_rows

    @pl.when(block == 0)
    def _():
        m_acc[...] = jnp.full(m_acc.shape, NEGATIVE, jnp.float32)
        w_acc[...] = jnp.zeros(w_acc.shape, jnp.float32)
        n_acc[...] = jnp.zeros(n_acc.shape, jnp.float32)

    query = q_ref[0]
    table = table_ref[0]
    cosine = jnp.concatenate(
        [jnp.broadcast_to(table[2 * c : 2 * c + 1], (slot_rows, head_dim)) for c in range(n_slots)], axis=0
    )
    sine = jnp.concatenate(
        [jnp.broadcast_to(table[2 * c + 1 : 2 * c + 2], (slot_rows, head_dim)) for c in range(n_slots)], axis=0
    )

    def one_set(i, carry):
        keys = kv_ref[i, 0, :, 0].reshape(n_pages * page_rows, head_dim).astype(jnp.float32)
        values = kv_ref[i, 0, :, 1].reshape(n_pages * page_rows, head_dim)
        keys = (keys * cosine + pltpu.roll(keys, head_dim // 2, 1) * sine).astype(jnp.bfloat16)
        scores = lax.dot_general(
            keys, query, (((1,), (1,)), ((), ())), preferred_element_type=jnp.float32
        ) * scale
        valid = valid_ref[0, i] > 0.5
        masked = jnp.where(valid, scores, NEGATIVE)
        peak = jnp.max(masked, axis=0, keepdims=True)
        powers = jnp.where(valid, jnp.exp(masked - peak), 0.0)
        total = jnp.sum(powers, axis=0, keepdims=True)
        acc = lax.dot_general(
            values, powers.astype(jnp.bfloat16), (((0,), (0,)), ((), ())),
            preferred_element_type=jnp.float32,
        )
        inverse = 1.0 / jnp.maximum(total, 1.0)
        normalised = (acc * inverse).astype(jnp.bfloat16).astype(jnp.float32)
        old = m_acc[...]
        merged = jnp.maximum(old, peak)
        rescale = jnp.exp(old - merged)
        weight = total * jnp.exp(peak - merged)
        m_acc[...] = merged
        w_acc[...] = w_acc[...] * rescale + weight
        n_acc[...] = n_acc[...] * rescale + normalised * weight
        return carry

    lax.fori_loop(0, kv_ref.shape[0], one_set, 0)

    @pl.when(block == n_blocks - 1)
    def _():
        peak_ref[0] = m_acc[...]
        sum_ref[0] = w_acc[...]
        num_ref[0] = n_acc[...]


def cached_attention(queries, arrived, valid, tables, scale):
    req_dev, rows, head_dim = queries.shape
    pool_count = arrived.shape[0]
    kv_block = (SET_BLOCK,) + (1,) + arrived.shape[2:]
    valid = valid[..., None]
    peak, total, num = pl.pallas_call(
        functools.partial(cached_kernel, scale),
        grid=(req_dev, pool_count // SET_BLOCK),
        in_specs=[
            pl.BlockSpec((1, rows, head_dim), lambda r, j: (r, 0, 0)),
            pl.BlockSpec(kv_block, lambda r, j: (j, r, 0, 0, 0, 0)),
            pl.BlockSpec((1, SET_BLOCK, valid.shape[2], 1), lambda r, j: (r, j, 0, 0)),
            pl.BlockSpec((1,) + tables.shape[1:], lambda r, j: (r, 0, 0)),
        ],
        out_specs=[
            pl.BlockSpec((1, 1, rows), lambda r, j: (r, 0, 0)),
            pl.BlockSpec((1, 1, rows), lambda r, j: (r, 0, 0)),
            pl.BlockSpec((1, head_dim, rows), lambda r, j: (r, 0, 0)),
        ],
        out_shape=[
            jax.ShapeDtypeStruct((req_dev, 1, rows), jnp.float32),
            jax.ShapeDtypeStruct((req_dev, 1, rows), jnp.float32),
            jax.ShapeDtypeStruct((req_dev, head_dim, rows), jnp.float32),
        ],
        scratch_shapes=[
            pltpu.VMEM((1, rows), jnp.float32),
            pltpu.VMEM((1, rows), jnp.float32),
            pltpu.VMEM((head_dim, rows), jnp.float32),
        ],
        compiler_params=pltpu.CompilerParams(dimension_semantics=("parallel", "arbitrary")),
    )(queries, arrived, valid, tables)
    return (peak, total, jnp.swapaxes(num, 1, 2))

def shards(
    pool_kv,
    span_pages,
    req_spans,
    span_offsets,
    recompute_rows,
    question_lengths,
    question_q,
    question_kv,
    recompute_hidden,
    w_kv,
    w_out,
):
    pool_count = lax.axis_size("pool")
    device = lax.axis_index("pool")
    req_dev = question_q.shape[0]
    qlen = question_q.shape[1]
    heads = question_q.shape[2]
    head_dim = question_q.shape[3]
    pages_dev = pool_kv.shape[0]
    kv_heads = pool_kv.shape[1]
    page_rows = pool_kv.shape[3]
    group_size = heads // kv_heads
    n_slots = req_spans.shape[1]
    pages_span = span_pages.shape[1]
    span_rows = pages_span * page_rows
    peer_pages = pages_span // pool_count
    score_scale = head_dim ** (-0.5)
    first_request = device * req_dev
    own_spans = lax.dynamic_slice_in_dim(req_spans, first_request, req_dev, 0)
    own_offsets = lax.dynamic_slice_in_dim(span_offsets, first_request, req_dev, 0).astype(
        jnp.float32
    )
    own_rows = lax.dynamic_slice_in_dim(recompute_rows, first_request, req_dev, 0)
    own_lengths = lax.dynamic_slice_in_dim(question_lengths, first_request, req_dev, 0)
    steps_q = jnp.arange(qlen, dtype=jnp.int32)
    qpos = (n_slots * span_rows + steps_q).astype(jnp.float32)
    queries = rotate(question_q.astype(jnp.float32), qpos[None, :, None]).astype(jnp.bfloat16)
    grouped = queries.reshape(req_dev, qlen, kv_heads, group_size, head_dim)
    own_keys = rotate(question_kv[:, :, 0].astype(jnp.float32), qpos[None, :, None]).astype(
        jnp.bfloat16
    )
    own_values = question_kv[:, :, 1]
    hidden = lax.all_gather(recompute_hidden, "tp", axis=3, tiled=True)
    widened = hidden.astype(jnp.float32)
    normed = (
        widened * lax.rsqrt(jnp.mean(widened * widened, axis=-1, keepdims=True) + 1e-06)
    ).astype(jnp.bfloat16)
    fresh = jnp.einsum("rcnd,dskh->rcnskh", normed, w_kv, preferred_element_type=jnp.float32)
    fresh_pos = own_offsets[:, :, None] + own_rows.astype(jnp.float32)
    fresh_keys = rotate(fresh[:, :, :, 0], fresh_pos[..., None]).astype(jnp.bfloat16)
    fresh_values = fresh[:, :, :, 1].astype(jnp.bfloat16)
    fresh_scores = (
        jnp.einsum("rqkgd,rcnkd->rqkgcn", grouped, fresh_keys, preferred_element_type=jnp.float32)
        * score_scale
    )
    fresh_scores = fresh_scores.reshape(req_dev, qlen, kv_heads, group_size, -1)
    fresh_peak, fresh_sum, fresh_weights = summarize(fresh_scores, True)
    fresh_acc = jnp.einsum(
        "rqkgn,rnkd->rqkgd",
        fresh_weights,
        fresh_values.reshape(req_dev, -1, kv_heads, head_dim),
        preferred_element_type=jnp.float32,
    )
    visible = (steps_q[None, None, :] <= steps_q[None, :, None]) & (
        steps_q[None, None, :] < own_lengths[:, None, None]
    )
    own_scores = (
        jnp.einsum("rqkgd,rjkd->rqkgj", grouped, own_keys, preferred_element_type=jnp.float32)
        * score_scale
    )
    own_peak, own_sum, own_weights = summarize(own_scores, visible[:, :, None, None, :])
    own_acc = jnp.einsum(
        "rqkgj,rjkd->rqkgd", own_weights, own_values, preferred_element_type=jnp.float32
    )
    own_keys = rotate(question_kv[:, :, 0].astype(jnp.float32), qpos[None, :, None]).astype(
        jnp.bfloat16
    )
    own_values = question_kv[:, :, 1]
    hidden = lax.all_gather(recompute_hidden, "tp", axis=3, tiled=True)
    widened = hidden.astype(jnp.float32)
    normed = (
        widened * lax.rsqrt(jnp.mean(widened * widened, axis=-1, keepdims=True) + 1e-06)
    ).astype(jnp.bfloat16)
    fresh = jnp.einsum("rcnd,dskh->rcnskh", normed, w_kv, preferred_element_type=jnp.float32)
    fresh_pos = own_offsets[:, :, None] + own_rows.astype(jnp.float32)
    fresh_keys = rotate(fresh[:, :, :, 0], fresh_pos[..., None]).astype(jnp.bfloat16)
    fresh_values = fresh[:, :, :, 1].astype(jnp.bfloat16)
    fresh_scores = (
        jnp.einsum("rqkgd,rcnkd->rqkgcn", grouped, fresh_keys, preferred_element_type=jnp.float32)
        * score_scale
    )
    fresh_scores = fresh_scores.reshape(req_dev, qlen, kv_heads, group_size, -1)
    fresh_peak, fresh_sum, fresh_weights = summarize(fresh_scores, True)
    fresh_acc = jnp.einsum(
        "rqkgn,rnkd->rqkgd",
        fresh_weights,
        fresh_values.reshape(req_dev, -1, kv_heads, head_dim),
        preferred_element_type=jnp.float32,
    )
    visible = (steps_q[None, None, :] <= steps_q[None, :, None]) & (
        steps_q[None, None, :] < own_lengths[:, None, None]
    )
    own_scores = (
        jnp.einsum("rqkgd,rjkd->rqkgj", grouped, own_keys, preferred_element_type=jnp.float32)
        * score_scale
    )
    own_peak, own_sum, own_weights = summarize(own_scores, visible[:, :, None, None, :])
    own_acc = jnp.einsum(
        "rqkgj,rjkd->rqkgd", own_weights, own_values, preferred_element_type=jnp.float32
    )

    mine = span_pages[own_spans]
    unused_slots, page_index = local_pages(
        mine[:, :, None, :], jnp.arange(pool_count, dtype=jnp.int32)[:, None], pages_dev, peer_pages
    )
    row_ids = page_index[..., None] * page_rows + jnp.arange(page_rows, dtype=jnp.int32)
    replaced = jnp.any(row_ids[..., None] == own_rows[:, :, None, None, None, :], axis=-1)
    valid = jnp.logical_not(replaced).transpose(0, 2, 1, 3, 4).reshape(req_dev, pool_count, -1)
    valid = valid.astype(jnp.float32)
    angles = own_offsets[..., None] * frequencies(head_dim)
    tables = jnp.stack(
        [
            jnp.concatenate([jnp.cos(angles), jnp.cos(angles)], axis=-1),
            jnp.concatenate([-jnp.sin(angles), jnp.sin(angles)], axis=-1),
        ],
        axis=2,
    ).reshape(req_dev, 2 * n_slots, head_dim)
    local = (fresh_peak, fresh_sum, fresh_acc, own_peak, own_sum, own_acc, valid, tables)

    all_pages = span_pages[req_spans]
    slot_ids, unused_index = local_pages(all_pages, device, pages_dev, peer_pages)
    slot_ids = slot_ids.reshape((pool_count, req_dev) + slot_ids.shape[1:])
    arrivals = []
    for r in range(req_dev):
        outgoing = pool_kv[slot_ids[:, r]]
        if arrivals:
            arrivals[-1], outgoing, local = lax.optimization_barrier((arrivals[-1], outgoing, local))
        arrivals.append(lax.all_to_all(outgoing, "pool", split_axis=0, concat_axis=0, tiled=True))
    fresh_peak, fresh_sum, fresh_acc, own_peak, own_sum, own_acc, valid, tables = local

    flat_queries = queries.reshape(req_dev, qlen * heads, head_dim)
    outputs = []
    for r in range(req_dev):
        one = slice(r, r + 1)
        arrived = arrivals[r]
        if outputs:
            arrived, outputs[-1] = lax.optimization_barrier((arrived, outputs[-1]))
        cached = cached_attention(
            flat_queries[one],
            arrived.reshape(pool_count, 1, n_slots * peer_pages, 2, page_rows, head_dim),
            valid[one],
            tables[one],
            score_scale,
        )
        cached = (
            cached[0].reshape(1, qlen, kv_heads, group_size),
            cached[1].reshape(1, qlen, kv_heads, group_size),
            cached[2].reshape(1, qlen, kv_heads, group_size, head_dim),
        )
        total = combine(
            combine(cached, (fresh_peak[one], fresh_sum[one], fresh_acc[one])),
            (own_peak[one], own_sum[one], own_acc[one]),
        )
        attn = total[2] / total[1][..., None]
        live = steps_q < own_lengths[r]
        attn = (
            jnp.where(live[None, :, None, None, None], attn, 0.0)
            .astype(jnp.bfloat16)
            .reshape(1, qlen, heads * head_dim)
        )
        partial_out = jnp.einsum("rqh,hm->rqm", attn, w_out, preferred_element_type=jnp.float32)
        outputs.append(
            lax.psum_scatter(partial_out, "tp", scatter_dimension=2, tiled=True).astype(jnp.bfloat16)
        )
    return jnp.concatenate(outputs, axis=0)


def solution(mesh):
    return jax.shard_map(
        shards,
        mesh=mesh,
        in_specs=(
            P("pool", "tp", None, None, None),
            P(),
            P(),
            P(),
            P(),
            P(),
            P("pool", None, "tp", None),
            P("pool", None, None, "tp", None),
            P("pool", None, None, "tp"),
            P(None, None, "tp", None),
            P("tp", None),
        ),
        out_specs=P("pool", None, "tp"),
        check_vma=False,
    )
```

```python
import functools

import jax
import jax.numpy as jnp
from jax import lax
from jax.experimental import pallas as pl
from jax.experimental.pallas import tpu as pltpu
from jax.sharding import PartitionSpec as P

THETA = 1000000.0
NEGATIVE = -1e30


def rotate(vectors, position):
    halfway = vectors.shape[-1] // 2
    frequency = THETA ** (-(jnp.arange(halfway, dtype=jnp.float32) * 2.0) / vectors.shape[-1])
    angles = position[..., None] * frequency
    cosine_part = jnp.cos(angles)
    sine_part = jnp.sin(angles)
    leading = vectors[..., :halfway]
    trailing = vectors[..., halfway:]
    return jnp.concatenate(
        [
            leading * cosine_part - trailing * sine_part,
            trailing * cosine_part + leading * sine_part,
        ],
        axis=-1,
    )


def summarize(scores, valid):
    masked = jnp.where(valid, scores, NEGATIVE)
    peak = jnp.max(masked, axis=-1)
    powers = jnp.where(valid, jnp.exp(masked - peak[..., None]), 0.0)
    return (peak, jnp.sum(powers, axis=-1), powers.astype(jnp.bfloat16))


def combine(former, latter):
    peak = jnp.maximum(former[0], latter[0])
    former_factor = jnp.exp(former[0] - peak)
    latter_factor = jnp.exp(latter[0] - peak)
    return (
        peak,
        former[1] * former_factor + latter[1] * latter_factor,
        former[2] * former_factor[..., None] + latter[2] * latter_factor[..., None],
    )


def merge_normalised(peaks, sums, normalised, axis):
    merged_peak = jnp.max(peaks, axis=axis)
    weight = sums * jnp.exp(peaks - jnp.expand_dims(merged_peak, axis))
    return (
        merged_peak,
        jnp.sum(weight, axis=axis),
        jnp.sum(normalised.astype(jnp.float32) * weight[..., None], axis=axis),
    )


def local_pages(pages, device, pages_dev, peer_pages):
    here = pages // pages_dev == device
    ranking = jnp.cumsum(here.astype(jnp.int32), axis=-1) - 1
    picks = here[..., None, :] & (
        ranking[..., None, :] == jnp.arange(peer_pages, dtype=jnp.int32)[:, None]
    )
    slot_ids = jnp.sum(jnp.where(picks, (pages % pages_dev)[..., None, :], 0), axis=-1)
    page_index = jnp.sum(jnp.where(picks, jnp.arange(pages.shape[-1], dtype=jnp.int32), 0), axis=-1)
    return (slot_ids, page_index)


def frequencies(head_dim):
    halfway = head_dim // 2
    return THETA ** (-(jnp.arange(halfway, dtype=jnp.float32) * 2.0) / head_dim)


SET_BLOCK = 8


def cached_kernel(scale, q_ref, kv_ref, valid_ref, table_ref, peak_ref, sum_ref, num_ref, m_acc, w_acc, n_acc):
    block = pl.program_id(1)
    n_blocks = pl.num_programs(1)
    n_pages = kv_ref.shape[2]
    page_rows = kv_ref.shape[4]
    head_dim = kv_ref.shape[5]
    n_slots = table_ref.shape[1] // 2
    slot_rows = (n_pages // n_slots) * page_rows

    @pl.when(block == 0)
    def _():
        m_acc[...] = jnp.full(m_acc.shape, NEGATIVE, jnp.float32)
        w_acc[...] = jnp.zeros(w_acc.shape, jnp.float32)
        n_acc[...] = jnp.zeros(n_acc.shape, jnp.float32)

    query = q_ref[0]
    table = table_ref[0]
    cosine = jnp.concatenate(
        [jnp.broadcast_to(table[2 * c : 2 * c + 1], (slot_rows, head_dim)) for c in range(n_slots)], axis=0
    )
    sine = jnp.concatenate(
        [jnp.broadcast_to(table[2 * c + 1 : 2 * c + 2], (slot_rows, head_dim)) for c in range(n_slots)], axis=0
    )

    def one_set(i, carry):
        keys = kv_ref[i, 0, :, 0].reshape(n_pages * page_rows, head_dim).astype(jnp.float32)
        values = kv_ref[i, 0, :, 1].reshape(n_pages * page_rows, head_dim)
        keys = (keys * cosine + pltpu.roll(keys, head_dim // 2, 1) * sine).astype(jnp.bfloat16)
        scores = lax.dot_general(
            keys, query, (((1,), (1,)), ((), ())), preferred_element_type=jnp.float32
        ) * scale
        valid = valid_ref[0, i] > 0.5
        masked = jnp.where(valid, scores, NEGATIVE)
        peak = jnp.max(masked, axis=0, keepdims=True)
        powers = jnp.where(valid, jnp.exp(masked - peak), 0.0)
        total = jnp.sum(powers, axis=0, keepdims=True)
        acc = lax.dot_general(
            values, powers.astype(jnp.bfloat16), (((0,), (0,)), ((), ())),
            preferred_element_type=jnp.float32,
        )
        inverse = 1.0 / jnp.maximum(total, 1.0)
        normalised = (acc * inverse).astype(jnp.bfloat16).astype(jnp.float32)
        old = m_acc[...]
        merged = jnp.maximum(old, peak)
        rescale = jnp.exp(old - merged)
        weight = total * jnp.exp(peak - merged)
        m_acc[...] = merged
        w_acc[...] = w_acc[...] * rescale + weight
        n_acc[...] = n_acc[...] * rescale + normalised * weight
        return carry

    lax.fori_loop(0, kv_ref.shape[0], one_set, 0)

    @pl.when(block == n_blocks - 1)
    def _():
        peak_ref[0] = m_acc[...]
        sum_ref[0] = w_acc[...]
        num_ref[0] = n_acc[...]


def cached_attention(queries, arrived, valid, tables, scale):
    req_dev, rows, head_dim = queries.shape
    pool_count = arrived.shape[0]
    kv_block = (SET_BLOCK,) + (1,) + arrived.shape[2:]
    valid = valid[..., None]
    peak, total, num = pl.pallas_call(
        functools.partial(cached_kernel, scale),
        grid=(req_dev, pool_count // SET_BLOCK),
        in_specs=[
            pl.BlockSpec((1, rows, head_dim), lambda r, j: (r, 0, 0)),
            pl.BlockSpec(kv_block, lambda r, j: (j, r, 0, 0, 0, 0)),
            pl.BlockSpec((1, SET_BLOCK, valid.shape[2], 1), lambda r, j: (r, j, 0, 0)),
            pl.BlockSpec((1,) + tables.shape[1:], lambda r, j: (r, 0, 0)),
        ],
        out_specs=[
            pl.BlockSpec((1, 1, rows), lambda r, j: (r, 0, 0)),
            pl.BlockSpec((1, 1, rows), lambda r, j: (r, 0, 0)),
            pl.BlockSpec((1, head_dim, rows), lambda r, j: (r, 0, 0)),
        ],
        out_shape=[
            jax.ShapeDtypeStruct((req_dev, 1, rows), jnp.float32),
            jax.ShapeDtypeStruct((req_dev, 1, rows), jnp.float32),
            jax.ShapeDtypeStruct((req_dev, head_dim, rows), jnp.float32),
        ],
        scratch_shapes=[
            pltpu.VMEM((1, rows), jnp.float32),
            pltpu.VMEM((1, rows), jnp.float32),
            pltpu.VMEM((head_dim, rows), jnp.float32),
        ],
        compiler_params=pltpu.CompilerParams(dimension_semantics=("parallel", "arbitrary")),
    )(queries, arrived, valid, tables)
    return (peak, total, jnp.swapaxes(num, 1, 2))

def shards(
    pool_kv,
    span_pages,
    req_spans,
    span_offsets,
    recompute_rows,
    question_lengths,
    question_q,
    question_kv,
    recompute_hidden,
    w_kv,
    w_out,
):
    pool_count = lax.axis_size("pool")
    device = lax.axis_index("pool")
    req_dev = question_q.shape[0]
    qlen = question_q.shape[1]
    heads = question_q.shape[2]
    head_dim = question_q.shape[3]
    pages_dev = pool_kv.shape[0]
    kv_heads = pool_kv.shape[1]
    page_rows = pool_kv.shape[3]
    group_size = heads // kv_heads
    n_slots = req_spans.shape[1]
    pages_span = span_pages.shape[1]
    span_rows = pages_span * page_rows
    peer_pages = pages_span // pool_count
    score_scale = head_dim ** (-0.5)
    first_request = device * req_dev
    own_spans = lax.dynamic_slice_in_dim(req_spans, first_request, req_dev, 0)
    own_offsets = lax.dynamic_slice_in_dim(span_offsets, first_request, req_dev, 0).astype(
        jnp.float32
    )
    own_rows = lax.dynamic_slice_in_dim(recompute_rows, first_request, req_dev, 0)
    own_lengths = lax.dynamic_slice_in_dim(question_lengths, first_request, req_dev, 0)
    steps_q = jnp.arange(qlen, dtype=jnp.int32)
    qpos = (n_slots * span_rows + steps_q).astype(jnp.float32)
    queries = rotate(question_q.astype(jnp.float32), qpos[None, :, None]).astype(jnp.bfloat16)
    grouped = queries.reshape(req_dev, qlen, kv_heads, group_size, head_dim)
    own_keys = rotate(question_kv[:, :, 0].astype(jnp.float32), qpos[None, :, None]).astype(
        jnp.bfloat16
    )
    own_values = question_kv[:, :, 1]
    hidden = lax.all_gather(recompute_hidden, "tp", axis=3, tiled=True)
    widened = hidden.astype(jnp.float32)
    normed = (
        widened * lax.rsqrt(jnp.mean(widened * widened, axis=-1, keepdims=True) + 1e-06)
    ).astype(jnp.bfloat16)
    fresh = jnp.einsum("rcnd,dskh->rcnskh", normed, w_kv, preferred_element_type=jnp.float32)
    fresh_pos = own_offsets[:, :, None] + own_rows.astype(jnp.float32)
    fresh_keys = rotate(fresh[:, :, :, 0], fresh_pos[..., None]).astype(jnp.bfloat16)
    fresh_values = fresh[:, :, :, 1].astype(jnp.bfloat16)
    fresh_scores = (
        jnp.einsum("rqkgd,rcnkd->rqkgcn", grouped, fresh_keys, preferred_element_type=jnp.float32)
        * score_scale
    )
    fresh_scores = fresh_scores.reshape(req_dev, qlen, kv_heads, group_size, -1)
    fresh_peak, fresh_sum, fresh_weights = summarize(fresh_scores, True)
    fresh_acc = jnp.einsum(
        "rqkgn,rnkd->rqkgd",
        fresh_weights,
        fresh_values.reshape(req_dev, -1, kv_heads, head_dim),
        preferred_element_type=jnp.float32,
    )
    visible = (steps_q[None, None, :] <= steps_q[None, :, None]) & (
        steps_q[None, None, :] < own_lengths[:, None, None]
    )
    own_scores = (
        jnp.einsum("rqkgd,rjkd->rqkgj", grouped, own_keys, preferred_element_type=jnp.float32)
        * score_scale
    )
    own_peak, own_sum, own_weights = summarize(own_scores, visible[:, :, None, None, :])
    own_acc = jnp.einsum(
        "rqkgj,rjkd->rqkgd", own_weights, own_values, preferred_element_type=jnp.float32
    )
    own_keys = rotate(question_kv[:, :, 0].astype(jnp.float32), qpos[None, :, None]).astype(
        jnp.bfloat16
    )
    own_values = question_kv[:, :, 1]
    hidden = lax.all_gather(recompute_hidden, "tp", axis=3, tiled=True)
    widened = hidden.astype(jnp.float32)
    normed = (
        widened * lax.rsqrt(jnp.mean(widened * widened, axis=-1, keepdims=True) + 1e-06)
    ).astype(jnp.bfloat16)
    fresh = jnp.einsum("rcnd,dskh->rcnskh", normed, w_kv, preferred_element_type=jnp.float32)
    fresh_pos = own_offsets[:, :, None] + own_rows.astype(jnp.float32)
    fresh_keys = rotate(fresh[:, :, :, 0], fresh_pos[..., None]).astype(jnp.bfloat16)
    fresh_values = fresh[:, :, :, 1].astype(jnp.bfloat16)
    fresh_scores = (
        jnp.einsum("rqkgd,rcnkd->rqkgcn", grouped, fresh_keys, preferred_element_type=jnp.float32)
        * score_scale
    )
    fresh_scores = fresh_scores.reshape(req_dev, qlen, kv_heads, group_size, -1)
    fresh_peak, fresh_sum, fresh_weights = summarize(fresh_scores, True)
    fresh_acc = jnp.einsum(
        "rqkgn,rnkd->rqkgd",
        fresh_weights,
        fresh_values.reshape(req_dev, -1, kv_heads, head_dim),
        preferred_element_type=jnp.float32,
    )
    visible = (steps_q[None, None, :] <= steps_q[None, :, None]) & (
        steps_q[None, None, :] < own_lengths[:, None, None]
    )
    own_scores = (
        jnp.einsum("rqkgd,rjkd->rqkgj", grouped, own_keys, preferred_element_type=jnp.float32)
        * score_scale
    )
    own_peak, own_sum, own_weights = summarize(own_scores, visible[:, :, None, None, :])
    own_acc = jnp.einsum(
        "rqkgj,rjkd->rqkgd", own_weights, own_values, preferred_element_type=jnp.float32
    )

    mine = span_pages[own_spans]
    unused_slots, page_index = local_pages(
        mine[:, :, None, :], jnp.arange(pool_count, dtype=jnp.int32)[:, None], pages_dev, peer_pages
    )
    row_ids = page_index[..., None] * page_rows + jnp.arange(page_rows, dtype=jnp.int32)
    replaced = jnp.any(row_ids[..., None] == own_rows[:, :, None, None, None, :], axis=-1)
    valid = jnp.logical_not(replaced).transpose(0, 2, 1, 3, 4).reshape(req_dev, pool_count, -1)
    valid = valid.astype(jnp.float32)
    angles = own_offsets[..., None] * frequencies(head_dim)
    tables = jnp.stack(
        [
            jnp.concatenate([jnp.cos(angles), jnp.cos(angles)], axis=-1),
            jnp.concatenate([-jnp.sin(angles), jnp.sin(angles)], axis=-1),
        ],
        axis=2,
    ).reshape(req_dev, 2 * n_slots, head_dim)
    local = (fresh_peak, fresh_sum, fresh_acc, own_peak, own_sum, own_acc, valid, tables)

    all_pages = span_pages[req_spans]
    slot_ids, unused_index = local_pages(all_pages, device, pages_dev, peer_pages)
    slot_ids = slot_ids.reshape((pool_count, req_dev) + slot_ids.shape[1:])
    arrivals = []
    for r in range(req_dev):
        outgoing = pool_kv[slot_ids[:, r]]
        if arrivals:
            arrivals[-1], outgoing, local = lax.optimization_barrier((arrivals[-1], outgoing, local))
        arrivals.append(lax.all_to_all(outgoing, "pool", split_axis=0, concat_axis=0, tiled=True))
    fresh_peak, fresh_sum, fresh_acc, own_peak, own_sum, own_acc, valid, tables = local

    flat_queries = queries.reshape(req_dev, qlen * heads, head_dim)
    outputs = []
    for r in range(req_dev):
        one = slice(r, r + 1)
        arrived = arrivals[r]
        if outputs:
            arrived, outputs[-1] = lax.optimization_barrier((arrived, outputs[-1]))
        cached = cached_attention(
            flat_queries[one],
            arrived.reshape(pool_count, 1, n_slots * peer_pages, 2, page_rows, head_dim),
            valid[one],
            tables[one],
            score_scale,
        )
        cached = (
            cached[0].reshape(1, qlen, kv_heads, group_size),
            cached[1].reshape(1, qlen, kv_heads, group_size),
            cached[2].reshape(1, qlen, kv_heads, group_size, head_dim),
        )
        total = combine(
            combine(cached, (fresh_peak[one], fresh_sum[one], fresh_acc[one])),
            (own_peak[one], own_sum[one], own_acc[one]),
        )
        attn = total[2] / total[1][..., None]
        live = steps_q < own_lengths[r]
        attn = (
            jnp.where(live[None, :, None, None, None], attn, 0.0)
            .astype(jnp.bfloat16)
            .reshape(1, qlen, heads * head_dim)
        )
        partial_out = jnp.einsum("rqh,hm->rqm", attn, w_out, preferred_element_type=jnp.float32)
        if r < req_dev - 1:
            reduced = lax.psum_scatter(partial_out, "tp", scatter_dimension=2, tiled=True)
        else:
            tp_count = lax.axis_size("tp")
            pieces = partial_out.reshape(1, qlen, tp_count, -1).transpose(2, 0, 1, 3)
            pieces = lax.all_to_all(pieces, "tp", split_axis=0, concat_axis=0, tiled=True)
            reduced = jnp.sum(pieces, axis=0)
        outputs.append(reduced.astype(jnp.bfloat16))
    return jnp.concatenate(outputs, axis=0)


def solution(mesh):
    return jax.shard_map(
        shards,
        mesh=mesh,
        in_specs=(
            P("pool", "tp", None, None, None),
            P(),
            P(),
            P(),
            P(),
            P(),
            P("pool", None, "tp", None),
            P("pool", None, None, "tp", None),
            P("pool", None, None, "tp"),
            P(None, None, "tp", None),
            P("tp", None),
        ),
        out_specs=P("pool", None, "tp"),
        check_vma=False,
    )
```

```python
import functools

import jax
import jax.numpy as jnp
from jax import lax
from jax.experimental import pallas as pl
from jax.experimental.pallas import tpu as pltpu
from jax.sharding import PartitionSpec as P

THETA = 1000000.0
NEGATIVE = -1e30


def rotate(vectors, position):
    halfway = vectors.shape[-1] // 2
    frequency = THETA ** (-(jnp.arange(halfway, dtype=jnp.float32) * 2.0) / vectors.shape[-1])
    angles = position[..., None] * frequency
    cosine_part = jnp.cos(angles)
    sine_part = jnp.sin(angles)
    leading = vectors[..., :halfway]
    trailing = vectors[..., halfway:]
    return jnp.concatenate(
        [
            leading * cosine_part - trailing * sine_part,
            trailing * cosine_part + leading * sine_part,
        ],
        axis=-1,
    )


def summarize(scores, valid):
    masked = jnp.where(valid, scores, NEGATIVE)
    peak = jnp.max(masked, axis=-1)
    powers = jnp.where(valid, jnp.exp(masked - peak[..., None]), 0.0)
    return (peak, jnp.sum(powers, axis=-1), powers.astype(jnp.bfloat16))


def combine(former, latter):
    peak = jnp.maximum(former[0], latter[0])
    former_factor = jnp.exp(former[0] - peak)
    latter_factor = jnp.exp(latter[0] - peak)
    return (
        peak,
        former[1] * former_factor + latter[1] * latter_factor,
        former[2] * former_factor[..., None] + latter[2] * latter_factor[..., None],
    )


def merge_normalised(peaks, sums, normalised, axis):
    merged_peak = jnp.max(peaks, axis=axis)
    weight = sums * jnp.exp(peaks - jnp.expand_dims(merged_peak, axis))
    return (
        merged_peak,
        jnp.sum(weight, axis=axis),
        jnp.sum(normalised.astype(jnp.float32) * weight[..., None], axis=axis),
    )


def local_pages(pages, device, pages_dev, peer_pages):
    here = pages // pages_dev == device
    ranking = jnp.cumsum(here.astype(jnp.int32), axis=-1) - 1
    picks = here[..., None, :] & (
        ranking[..., None, :] == jnp.arange(peer_pages, dtype=jnp.int32)[:, None]
    )
    slot_ids = jnp.sum(jnp.where(picks, (pages % pages_dev)[..., None, :], 0), axis=-1)
    page_index = jnp.sum(jnp.where(picks, jnp.arange(pages.shape[-1], dtype=jnp.int32), 0), axis=-1)
    return (slot_ids, page_index)


def frequencies(head_dim):
    halfway = head_dim // 2
    return THETA ** (-(jnp.arange(halfway, dtype=jnp.float32) * 2.0) / head_dim)


SET_BLOCK = 8


def cached_kernel(scale, q_ref, kv_ref, valid_ref, table_ref, peak_ref, sum_ref, num_ref, m_acc, w_acc, n_acc):
    block = pl.program_id(1)
    n_blocks = pl.num_programs(1)
    n_pages = kv_ref.shape[2]
    page_rows = kv_ref.shape[4]
    head_dim = kv_ref.shape[5]
    n_slots = table_ref.shape[1] // 2
    slot_rows = (n_pages // n_slots) * page_rows

    @pl.when(block == 0)
    def _():
        m_acc[...] = jnp.full(m_acc.shape, NEGATIVE, jnp.float32)
        w_acc[...] = jnp.zeros(w_acc.shape, jnp.float32)
        n_acc[...] = jnp.zeros(n_acc.shape, jnp.float32)

    query = q_ref[0]
    table = table_ref[0]
    cosine = jnp.concatenate(
        [jnp.broadcast_to(table[2 * c : 2 * c + 1], (slot_rows, head_dim)) for c in range(n_slots)], axis=0
    )
    sine = jnp.concatenate(
        [jnp.broadcast_to(table[2 * c + 1 : 2 * c + 2], (slot_rows, head_dim)) for c in range(n_slots)], axis=0
    )

    def one_set(i, carry):
        keys = kv_ref[i, 0, :, 0].reshape(n_pages * page_rows, head_dim).astype(jnp.float32)
        values = kv_ref[i, 0, :, 1].reshape(n_pages * page_rows, head_dim)
        keys = (keys * cosine + pltpu.roll(keys, head_dim // 2, 1) * sine).astype(jnp.bfloat16)
        scores = lax.dot_general(
            keys, query, (((1,), (1,)), ((), ())), preferred_element_type=jnp.float32
        ) * scale
        valid = valid_ref[0, i] > 0.5
        masked = jnp.where(valid, scores, NEGATIVE)
        peak = jnp.max(masked, axis=0, keepdims=True)
        powers = jnp.where(valid, jnp.exp(masked - peak), 0.0)
        total = jnp.sum(powers, axis=0, keepdims=True)
        acc = lax.dot_general(
            values, powers.astype(jnp.bfloat16), (((0,), (0,)), ((), ())),
            preferred_element_type=jnp.float32,
        )
        inverse = 1.0 / jnp.maximum(total, 1.0)
        normalised = (acc * inverse).astype(jnp.bfloat16).astype(jnp.float32)
        old = m_acc[...]
        merged = jnp.maximum(old, peak)
        rescale = jnp.exp(old - merged)
        weight = total * jnp.exp(peak - merged)
        m_acc[...] = merged
        w_acc[...] = w_acc[...] * rescale + weight
        n_acc[...] = n_acc[...] * rescale + normalised * weight
        return carry

    lax.fori_loop(0, kv_ref.shape[0], one_set, 0)

    @pl.when(block == n_blocks - 1)
    def _():
        peak_ref[0] = m_acc[...]
        sum_ref[0] = w_acc[...]
        num_ref[0] = n_acc[...]


def cached_attention(queries, arrived, valid, tables, scale):
    req_dev, rows, head_dim = queries.shape
    pool_count = arrived.shape[0]
    kv_block = (SET_BLOCK,) + (1,) + arrived.shape[2:]
    valid = valid[..., None]
    peak, total, num = pl.pallas_call(
        functools.partial(cached_kernel, scale),
        grid=(req_dev, pool_count // SET_BLOCK),
        in_specs=[
            pl.BlockSpec((1, rows, head_dim), lambda r, j: (r, 0, 0)),
            pl.BlockSpec(kv_block, lambda r, j: (j, r, 0, 0, 0, 0)),
            pl.BlockSpec((1, SET_BLOCK, valid.shape[2], 1), lambda r, j: (r, j, 0, 0)),
            pl.BlockSpec((1,) + tables.shape[1:], lambda r, j: (r, 0, 0)),
        ],
        out_specs=[
            pl.BlockSpec((1, 1, rows), lambda r, j: (r, 0, 0)),
            pl.BlockSpec((1, 1, rows), lambda r, j: (r, 0, 0)),
            pl.BlockSpec((1, head_dim, rows), lambda r, j: (r, 0, 0)),
        ],
        out_shape=[
            jax.ShapeDtypeStruct((req_dev, 1, rows), jnp.float32),
            jax.ShapeDtypeStruct((req_dev, 1, rows), jnp.float32),
            jax.ShapeDtypeStruct((req_dev, head_dim, rows), jnp.float32),
        ],
        scratch_shapes=[
            pltpu.VMEM((1, rows), jnp.float32),
            pltpu.VMEM((1, rows), jnp.float32),
            pltpu.VMEM((head_dim, rows), jnp.float32),
        ],
        compiler_params=pltpu.CompilerParams(dimension_semantics=("parallel", "arbitrary")),
    )(queries, arrived, valid, tables)
    return (peak, total, jnp.swapaxes(num, 1, 2))

def shards(
    pool_kv,
    span_pages,
    req_spans,
    span_offsets,
    recompute_rows,
    question_lengths,
    question_q,
    question_kv,
    recompute_hidden,
    w_kv,
    w_out,
):
    pool_count = lax.axis_size("pool")
    device = lax.axis_index("pool")
    req_dev = question_q.shape[0]
    qlen = question_q.shape[1]
    heads = question_q.shape[2]
    head_dim = question_q.shape[3]
    pages_dev = pool_kv.shape[0]
    kv_heads = pool_kv.shape[1]
    page_rows = pool_kv.shape[3]
    group_size = heads // kv_heads
    n_slots = req_spans.shape[1]
    pages_span = span_pages.shape[1]
    span_rows = pages_span * page_rows
    peer_pages = pages_span // pool_count
    score_scale = head_dim ** (-0.5)
    first_request = device * req_dev
    own_spans = lax.dynamic_slice_in_dim(req_spans, first_request, req_dev, 0)
    own_offsets = lax.dynamic_slice_in_dim(span_offsets, first_request, req_dev, 0).astype(
        jnp.float32
    )
    own_rows = lax.dynamic_slice_in_dim(recompute_rows, first_request, req_dev, 0)
    own_lengths = lax.dynamic_slice_in_dim(question_lengths, first_request, req_dev, 0)
    steps_q = jnp.arange(qlen, dtype=jnp.int32)
    qpos = (n_slots * span_rows + steps_q).astype(jnp.float32)
    queries = rotate(question_q.astype(jnp.float32), qpos[None, :, None]).astype(jnp.bfloat16)
    grouped = queries.reshape(req_dev, qlen, kv_heads, group_size, head_dim)
    own_keys = rotate(question_kv[:, :, 0].astype(jnp.float32), qpos[None, :, None]).astype(
        jnp.bfloat16
    )
    own_values = question_kv[:, :, 1]
    hidden = lax.all_gather(recompute_hidden, "tp", axis=3, tiled=True)
    widened = hidden.astype(jnp.float32)
    normed = (
        widened * lax.rsqrt(jnp.mean(widened * widened, axis=-1, keepdims=True) + 1e-06)
    ).astype(jnp.bfloat16)
    fresh = jnp.einsum("rcnd,dskh->rcnskh", normed, w_kv, preferred_element_type=jnp.float32)
    fresh_pos = own_offsets[:, :, None] + own_rows.astype(jnp.float32)
    fresh_keys = rotate(fresh[:, :, :, 0], fresh_pos[..., None]).astype(jnp.bfloat16)
    fresh_values = fresh[:, :, :, 1].astype(jnp.bfloat16)
    fresh_scores = (
        jnp.einsum("rqkgd,rcnkd->rqkgcn", grouped, fresh_keys, preferred_element_type=jnp.float32)
        * score_scale
    )
    fresh_scores = fresh_scores.reshape(req_dev, qlen, kv_heads, group_size, -1)
    fresh_peak, fresh_sum, fresh_weights = summarize(fresh_scores, True)
    fresh_acc = jnp.einsum(
        "rqkgn,rnkd->rqkgd",
        fresh_weights,
        fresh_values.reshape(req_dev, -1, kv_heads, head_dim),
        preferred_element_type=jnp.float32,
    )
    visible = (steps_q[None, None, :] <= steps_q[None, :, None]) & (
        steps_q[None, None, :] < own_lengths[:, None, None]
    )
    own_scores = (
        jnp.einsum("rqkgd,rjkd->rqkgj", grouped, own_keys, preferred_element_type=jnp.float32)
        * score_scale
    )
    own_peak, own_sum, own_weights = summarize(own_scores, visible[:, :, None, None, :])
    own_acc = jnp.einsum(
        "rqkgj,rjkd->rqkgd", own_weights, own_values, preferred_element_type=jnp.float32
    )
    own_keys = rotate(question_kv[:, :, 0].astype(jnp.float32), qpos[None, :, None]).astype(
        jnp.bfloat16
    )
    own_values = question_kv[:, :, 1]
    hidden = lax.all_gather(recompute_hidden, "tp", axis=3, tiled=True)
    widened = hidden.astype(jnp.float32)
    normed = (
        widened * lax.rsqrt(jnp.mean(widened * widened, axis=-1, keepdims=True) + 1e-06)
    ).astype(jnp.bfloat16)
    fresh = jnp.einsum("rcnd,dskh->rcnskh", normed, w_kv, preferred_element_type=jnp.float32)
    fresh_pos = own_offsets[:, :, None] + own_rows.astype(jnp.float32)
    fresh_keys = rotate(fresh[:, :, :, 0], fresh_pos[..., None]).astype(jnp.bfloat16)
    fresh_values = fresh[:, :, :, 1].astype(jnp.bfloat16)
    fresh_scores = (
        jnp.einsum("rqkgd,rcnkd->rqkgcn", grouped, fresh_keys, preferred_element_type=jnp.float32)
        * score_scale
    )
    fresh_scores = fresh_scores.reshape(req_dev, qlen, kv_heads, group_size, -1)
    fresh_peak, fresh_sum, fresh_weights = summarize(fresh_scores, True)
    fresh_acc = jnp.einsum(
        "rqkgn,rnkd->rqkgd",
        fresh_weights,
        fresh_values.reshape(req_dev, -1, kv_heads, head_dim),
        preferred_element_type=jnp.float32,
    )
    visible = (steps_q[None, None, :] <= steps_q[None, :, None]) & (
        steps_q[None, None, :] < own_lengths[:, None, None]
    )
    own_scores = (
        jnp.einsum("rqkgd,rjkd->rqkgj", grouped, own_keys, preferred_element_type=jnp.float32)
        * score_scale
    )
    own_peak, own_sum, own_weights = summarize(own_scores, visible[:, :, None, None, :])
    own_acc = jnp.einsum(
        "rqkgj,rjkd->rqkgd", own_weights, own_values, preferred_element_type=jnp.float32
    )

    mine = span_pages[own_spans]
    unused_slots, page_index = local_pages(
        mine[:, :, None, :], jnp.arange(pool_count, dtype=jnp.int32)[:, None], pages_dev, peer_pages
    )
    row_ids = page_index[..., None] * page_rows + jnp.arange(page_rows, dtype=jnp.int32)
    replaced = jnp.any(row_ids[..., None] == own_rows[:, :, None, None, None, :], axis=-1)
    valid = jnp.logical_not(replaced).transpose(0, 2, 1, 3, 4).reshape(req_dev, pool_count, -1)
    valid = valid.astype(jnp.float32)
    angles = own_offsets[..., None] * frequencies(head_dim)
    tables = jnp.stack(
        [
            jnp.concatenate([jnp.cos(angles), jnp.cos(angles)], axis=-1),
            jnp.concatenate([-jnp.sin(angles), jnp.sin(angles)], axis=-1),
        ],
        axis=2,
    ).reshape(req_dev, 2 * n_slots, head_dim)
    local = (fresh_peak, fresh_sum, fresh_acc, own_peak, own_sum, own_acc, valid, tables)

    all_pages = span_pages[req_spans]
    slot_ids, unused_index = local_pages(all_pages, device, pages_dev, peer_pages)
    slot_ids = slot_ids.reshape((pool_count, req_dev) + slot_ids.shape[1:])
    arrivals = []
    for r in range(req_dev):
        outgoing = pool_kv[slot_ids[:, r]]
        if arrivals:
            arrivals[-1], outgoing, local = lax.optimization_barrier((arrivals[-1], outgoing, local))
        arrivals.append(lax.all_to_all(outgoing, "pool", split_axis=0, concat_axis=0, tiled=True))
    fresh_peak, fresh_sum, fresh_acc, own_peak, own_sum, own_acc, valid, tables = local

    flat_queries = queries.reshape(req_dev, qlen * heads, head_dim)
    outputs = []
    for r in range(req_dev):
        one = slice(r, r + 1)
        arrived = arrivals[r]
        if outputs:
            arrived, outputs[-1] = lax.optimization_barrier((arrived, outputs[-1]))
        cached = cached_attention(
            flat_queries[one],
            arrived.reshape(pool_count, 1, n_slots * peer_pages, 2, page_rows, head_dim),
            valid[one],
            tables[one],
            score_scale,
        )
        cached = (
            cached[0].reshape(1, qlen, kv_heads, group_size),
            cached[1].reshape(1, qlen, kv_heads, group_size),
            cached[2].reshape(1, qlen, kv_heads, group_size, head_dim),
        )
        total = combine(
            combine(cached, (fresh_peak[one], fresh_sum[one], fresh_acc[one])),
            (own_peak[one], own_sum[one], own_acc[one]),
        )
        attn = total[2] / total[1][..., None]
        live = steps_q < own_lengths[r]
        attn = (
            jnp.where(live[None, :, None, None, None], attn, 0.0)
            .astype(jnp.bfloat16)
            .reshape(1, qlen, heads * head_dim)
        )
        partial_out = jnp.einsum("rqh,hm->rqm", attn, w_out, preferred_element_type=jnp.float32)
        if r < req_dev - 1:
            reduced = lax.psum_scatter(partial_out, "tp", scatter_dimension=2, tiled=True)
        else:
            tp_count = lax.axis_size("tp")
            pieces = partial_out.reshape(1, qlen, tp_count, -1).transpose(2, 0, 1, 3)
            pieces = lax.all_to_all(
                pieces.astype(jnp.bfloat16), "tp", split_axis=0, concat_axis=0, tiled=True
            )
            reduced = jnp.sum(pieces.astype(jnp.float32), axis=0)
        outputs.append(reduced.astype(jnp.bfloat16))
    return jnp.concatenate(outputs, axis=0)


def solution(mesh):
    return jax.shard_map(
        shards,
        mesh=mesh,
        in_specs=(
            P("pool", "tp", None, None, None),
            P(),
            P(),
            P(),
            P(),
            P(),
            P("pool", None, "tp", None),
            P("pool", None, None, "tp", None),
            P("pool", None, None, "tp"),
            P(None, None, "tp", None),
            P("tp", None),
        ),
        out_specs=P("pool", None, "tp"),
        check_vma=False,
    )
```

```python
import functools

import jax
import jax.numpy as jnp
from jax import lax
from jax.experimental import pallas as pl
from jax.experimental.pallas import tpu as pltpu
from jax.sharding import PartitionSpec as P

THETA = 1000000.0
NEGATIVE = -1e30


def rotate(vectors, position):
    halfway = vectors.shape[-1] // 2
    frequency = THETA ** (-(jnp.arange(halfway, dtype=jnp.float32) * 2.0) / vectors.shape[-1])
    angles = position[..., None] * frequency
    cosine_part = jnp.cos(angles)
    sine_part = jnp.sin(angles)
    leading = vectors[..., :halfway]
    trailing = vectors[..., halfway:]
    return jnp.concatenate(
        [
            leading * cosine_part - trailing * sine_part,
            trailing * cosine_part + leading * sine_part,
        ],
        axis=-1,
    )


def summarize(scores, valid):
    masked = jnp.where(valid, scores, NEGATIVE)
    peak = jnp.max(masked, axis=-1)
    powers = jnp.where(valid, jnp.exp(masked - peak[..., None]), 0.0)
    return (peak, jnp.sum(powers, axis=-1), powers.astype(jnp.bfloat16))


def combine(former, latter):
    peak = jnp.maximum(former[0], latter[0])
    former_factor = jnp.exp(former[0] - peak)
    latter_factor = jnp.exp(latter[0] - peak)
    return (
        peak,
        former[1] * former_factor + latter[1] * latter_factor,
        former[2] * former_factor[..., None] + latter[2] * latter_factor[..., None],
    )


def merge_normalised(peaks, sums, normalised, axis):
    merged_peak = jnp.max(peaks, axis=axis)
    weight = sums * jnp.exp(peaks - jnp.expand_dims(merged_peak, axis))
    return (
        merged_peak,
        jnp.sum(weight, axis=axis),
        jnp.sum(normalised.astype(jnp.float32) * weight[..., None], axis=axis),
    )


def local_pages(pages, device, pages_dev, peer_pages):
    here = pages // pages_dev == device
    ranking = jnp.cumsum(here.astype(jnp.int32), axis=-1) - 1
    picks = here[..., None, :] & (
        ranking[..., None, :] == jnp.arange(peer_pages, dtype=jnp.int32)[:, None]
    )
    slot_ids = jnp.sum(jnp.where(picks, (pages % pages_dev)[..., None, :], 0), axis=-1)
    page_index = jnp.sum(jnp.where(picks, jnp.arange(pages.shape[-1], dtype=jnp.int32), 0), axis=-1)
    return (slot_ids, page_index)


def frequencies(head_dim):
    halfway = head_dim // 2
    return THETA ** (-(jnp.arange(halfway, dtype=jnp.float32) * 2.0) / head_dim)


SET_BLOCK = 8


def cached_kernel(scale, q_ref, kv_ref, valid_ref, table_ref, peak_ref, sum_ref, num_ref, m_acc, w_acc, n_acc):
    block = pl.program_id(1)
    n_blocks = pl.num_programs(1)
    n_pages = kv_ref.shape[2]
    page_rows = kv_ref.shape[4]
    head_dim = kv_ref.shape[5]
    n_slots = table_ref.shape[1] // 2
    slot_rows = (n_pages // n_slots) * page_rows

    @pl.when(block == 0)
    def _():
        m_acc[...] = jnp.full(m_acc.shape, NEGATIVE, jnp.float32)
        w_acc[...] = jnp.zeros(w_acc.shape, jnp.float32)
        n_acc[...] = jnp.zeros(n_acc.shape, jnp.float32)

    query = q_ref[0]
    table = table_ref[0]
    cosine = jnp.concatenate(
        [jnp.broadcast_to(table[2 * c : 2 * c + 1], (slot_rows, head_dim)) for c in range(n_slots)], axis=0
    )
    sine = jnp.concatenate(
        [jnp.broadcast_to(table[2 * c + 1 : 2 * c + 2], (slot_rows, head_dim)) for c in range(n_slots)], axis=0
    )

    def one_set(i, carry):
        keys = kv_ref[i, 0, :, 0].reshape(n_pages * page_rows, head_dim).astype(jnp.float32)
        values = kv_ref[i, 0, :, 1].reshape(n_pages * page_rows, head_dim)
        keys = (keys * cosine + pltpu.roll(keys, head_dim // 2, 1) * sine).astype(jnp.bfloat16)
        scores = lax.dot_general(
            keys, query, (((1,), (1,)), ((), ())), preferred_element_type=jnp.float32
        ) * scale
        valid = valid_ref[0, i] > 0.5
        masked = jnp.where(valid, scores, NEGATIVE)
        peak = jnp.max(masked, axis=0, keepdims=True)
        powers = jnp.where(valid, jnp.exp(masked - peak), 0.0)
        total = jnp.sum(powers, axis=0, keepdims=True)
        acc = lax.dot_general(
            values, powers.astype(jnp.bfloat16), (((0,), (0,)), ((), ())),
            preferred_element_type=jnp.float32,
        )
        inverse = 1.0 / jnp.maximum(total, 1.0)
        normalised = (acc * inverse).astype(jnp.bfloat16).astype(jnp.float32)
        old = m_acc[...]
        merged = jnp.maximum(old, peak)
        rescale = jnp.exp(old - merged)
        weight = total * jnp.exp(peak - merged)
        m_acc[...] = merged
        w_acc[...] = w_acc[...] * rescale + weight
        n_acc[...] = n_acc[...] * rescale + normalised * weight
        return carry

    lax.fori_loop(0, kv_ref.shape[0], one_set, 0)

    @pl.when(block == n_blocks - 1)
    def _():
        peak_ref[0] = m_acc[...]
        sum_ref[0] = w_acc[...]
        num_ref[0] = n_acc[...]


def cached_attention(queries, arrived, valid, tables, scale):
    req_dev, rows, head_dim = queries.shape
    pool_count = arrived.shape[0]
    kv_block = (SET_BLOCK,) + (1,) + arrived.shape[2:]
    valid = valid[..., None]
    peak, total, num = pl.pallas_call(
        functools.partial(cached_kernel, scale),
        grid=(req_dev, pool_count // SET_BLOCK),
        in_specs=[
            pl.BlockSpec((1, rows, head_dim), lambda r, j: (r, 0, 0)),
            pl.BlockSpec(kv_block, lambda r, j: (j, r, 0, 0, 0, 0)),
            pl.BlockSpec((1, SET_BLOCK, valid.shape[2], 1), lambda r, j: (r, j, 0, 0)),
            pl.BlockSpec((1,) + tables.shape[1:], lambda r, j: (r, 0, 0)),
        ],
        out_specs=[
            pl.BlockSpec((1, 1, rows), lambda r, j: (r, 0, 0)),
            pl.BlockSpec((1, 1, rows), lambda r, j: (r, 0, 0)),
            pl.BlockSpec((1, head_dim, rows), lambda r, j: (r, 0, 0)),
        ],
        out_shape=[
            jax.ShapeDtypeStruct((req_dev, 1, rows), jnp.float32),
            jax.ShapeDtypeStruct((req_dev, 1, rows), jnp.float32),
            jax.ShapeDtypeStruct((req_dev, head_dim, rows), jnp.float32),
        ],
        scratch_shapes=[
            pltpu.VMEM((1, rows), jnp.float32),
            pltpu.VMEM((1, rows), jnp.float32),
            pltpu.VMEM((head_dim, rows), jnp.float32),
        ],
        compiler_params=pltpu.CompilerParams(dimension_semantics=("parallel", "arbitrary")),
    )(queries, arrived, valid, tables)
    return (peak, total, jnp.swapaxes(num, 1, 2))

def shards(
    pool_kv,
    span_pages,
    req_spans,
    span_offsets,
    recompute_rows,
    question_lengths,
    question_q,
    question_kv,
    recompute_hidden,
    w_kv,
    w_out,
):
    pool_count = lax.axis_size("pool")
    device = lax.axis_index("pool")
    req_dev = question_q.shape[0]
    qlen = question_q.shape[1]
    heads = question_q.shape[2]
    head_dim = question_q.shape[3]
    pages_dev = pool_kv.shape[0]
    kv_heads = pool_kv.shape[1]
    page_rows = pool_kv.shape[3]
    group_size = heads // kv_heads
    n_slots = req_spans.shape[1]
    pages_span = span_pages.shape[1]
    span_rows = pages_span * page_rows
    peer_pages = pages_span // pool_count
    score_scale = head_dim ** (-0.5)
    first_request = device * req_dev
    own_spans = lax.dynamic_slice_in_dim(req_spans, first_request, req_dev, 0)
    own_offsets = lax.dynamic_slice_in_dim(span_offsets, first_request, req_dev, 0).astype(
        jnp.float32
    )
    own_rows = lax.dynamic_slice_in_dim(recompute_rows, first_request, req_dev, 0)
    own_lengths = lax.dynamic_slice_in_dim(question_lengths, first_request, req_dev, 0)
    steps_q = jnp.arange(qlen, dtype=jnp.int32)
    qpos = (n_slots * span_rows + steps_q).astype(jnp.float32)
    queries = rotate(question_q.astype(jnp.float32), qpos[None, :, None]).astype(jnp.bfloat16)
    grouped = queries.reshape(req_dev, qlen, kv_heads, group_size, head_dim)
    own_keys = rotate(question_kv[:, :, 0].astype(jnp.float32), qpos[None, :, None]).astype(
        jnp.bfloat16
    )
    own_values = question_kv[:, :, 1]
    tp_count = lax.axis_size("tp")
    rank = lax.axis_index("tp")
    width = recompute_hidden.shape[3]
    hidden = jnp.stack(
        [recompute_hidden]
        + [
            lax.ppermute(recompute_hidden, "tp", [(i, (i + k) % tp_count) for i in range(tp_count)])
            for k in range(1, tp_count)
        ]
    )
    weights = jnp.stack(
        [
            lax.dynamic_slice_in_dim(w_kv, ((rank - k) % tp_count) * width, width, axis=0)
            for k in range(tp_count)
        ]
    )
    widened = hidden.astype(jnp.float32)
    square_mean = jnp.sum(widened * widened, axis=(0, 4)) / (tp_count * width)
    normed = (widened * lax.rsqrt(square_mean + 1e-06)[None, ..., None]).astype(jnp.bfloat16)
    fresh = jnp.einsum("trcnd,tdskh->rcnskh", normed, weights, preferred_element_type=jnp.float32)
    fresh_pos = own_offsets[:, :, None] + own_rows.astype(jnp.float32)
    fresh_keys = rotate(fresh[:, :, :, 0], fresh_pos[..., None]).astype(jnp.bfloat16)
    fresh_values = fresh[:, :, :, 1].astype(jnp.bfloat16)
    fresh_scores = (
        jnp.einsum("rqkgd,rcnkd->rqkgcn", grouped, fresh_keys, preferred_element_type=jnp.float32)
        * score_scale
    )
    fresh_scores = fresh_scores.reshape(req_dev, qlen, kv_heads, group_size, -1)
    fresh_peak, fresh_sum, fresh_weights = summarize(fresh_scores, True)
    fresh_acc = jnp.einsum(
        "rqkgn,rnkd->rqkgd",
        fresh_weights,
        fresh_values.reshape(req_dev, -1, kv_heads, head_dim),
        preferred_element_type=jnp.float32,
    )
    visible = (steps_q[None, None, :] <= steps_q[None, :, None]) & (
        steps_q[None, None, :] < own_lengths[:, None, None]
    )
    own_scores = (
        jnp.einsum("rqkgd,rjkd->rqkgj", grouped, own_keys, preferred_element_type=jnp.float32)
        * score_scale
    )
    own_peak, own_sum, own_weights = summarize(own_scores, visible[:, :, None, None, :])
    own_acc = jnp.einsum(
        "rqkgj,rjkd->rqkgd", own_weights, own_values, preferred_element_type=jnp.float32
    )
    own_keys = rotate(question_kv[:, :, 0].astype(jnp.float32), qpos[None, :, None]).astype(
        jnp.bfloat16
    )
    own_values = question_kv[:, :, 1]
    tp_count = lax.axis_size("tp")
    rank = lax.axis_index("tp")
    width = recompute_hidden.shape[3]
    hidden = jnp.stack(
        [recompute_hidden]
        + [
            lax.ppermute(recompute_hidden, "tp", [(i, (i + k) % tp_count) for i in range(tp_count)])
            for k in range(1, tp_count)
        ]
    )
    weights = jnp.stack(
        [
            lax.dynamic_slice_in_dim(w_kv, ((rank - k) % tp_count) * width, width, axis=0)
            for k in range(tp_count)
        ]
    )
    widened = hidden.astype(jnp.float32)
    square_mean = jnp.sum(widened * widened, axis=(0, 4)) / (tp_count * width)
    normed = (widened * lax.rsqrt(square_mean + 1e-06)[None, ..., None]).astype(jnp.bfloat16)
    fresh = jnp.einsum("trcnd,tdskh->rcnskh", normed, weights, preferred_element_type=jnp.float32)
    fresh_pos = own_offsets[:, :, None] + own_rows.astype(jnp.float32)
    fresh_keys = rotate(fresh[:, :, :, 0], fresh_pos[..., None]).astype(jnp.bfloat16)
    fresh_values = fresh[:, :, :, 1].astype(jnp.bfloat16)
    fresh_scores = (
        jnp.einsum("rqkgd,rcnkd->rqkgcn", grouped, fresh_keys, preferred_element_type=jnp.float32)
        * score_scale
    )
    fresh_scores = fresh_scores.reshape(req_dev, qlen, kv_heads, group_size, -1)
    fresh_peak, fresh_sum, fresh_weights = summarize(fresh_scores, True)
    fresh_acc = jnp.einsum(
        "rqkgn,rnkd->rqkgd",
        fresh_weights,
        fresh_values.reshape(req_dev, -1, kv_heads, head_dim),
        preferred_element_type=jnp.float32,
    )
    visible = (steps_q[None, None, :] <= steps_q[None, :, None]) & (
        steps_q[None, None, :] < own_lengths[:, None, None]
    )
    own_scores = (
        jnp.einsum("rqkgd,rjkd->rqkgj", grouped, own_keys, preferred_element_type=jnp.float32)
        * score_scale
    )
    own_peak, own_sum, own_weights = summarize(own_scores, visible[:, :, None, None, :])
    own_acc = jnp.einsum(
        "rqkgj,rjkd->rqkgd", own_weights, own_values, preferred_element_type=jnp.float32
    )

    mine = span_pages[own_spans]
    unused_slots, page_index = local_pages(
        mine[:, :, None, :], jnp.arange(pool_count, dtype=jnp.int32)[:, None], pages_dev, peer_pages
    )
    row_ids = page_index[..., None] * page_rows + jnp.arange(page_rows, dtype=jnp.int32)
    replaced = jnp.any(row_ids[..., None] == own_rows[:, :, None, None, None, :], axis=-1)
    valid = jnp.logical_not(replaced).transpose(0, 2, 1, 3, 4).reshape(req_dev, pool_count, -1)
    valid = valid.astype(jnp.float32)
    angles = own_offsets[..., None] * frequencies(head_dim)
    tables = jnp.stack(
        [
            jnp.concatenate([jnp.cos(angles), jnp.cos(angles)], axis=-1),
            jnp.concatenate([-jnp.sin(angles), jnp.sin(angles)], axis=-1),
        ],
        axis=2,
    ).reshape(req_dev, 2 * n_slots, head_dim)
    local = (fresh_peak, fresh_sum, fresh_acc, own_peak, own_sum, own_acc, valid, tables)

    all_pages = span_pages[req_spans]
    slot_ids, unused_index = local_pages(all_pages, device, pages_dev, peer_pages)
    slot_ids = slot_ids.reshape((pool_count, req_dev) + slot_ids.shape[1:])
    arrivals = []
    for r in range(req_dev):
        outgoing = pool_kv[slot_ids[:, r]]
        if arrivals:
            arrivals[-1], outgoing, local = lax.optimization_barrier((arrivals[-1], outgoing, local))
        arrivals.append(lax.all_to_all(outgoing, "pool", split_axis=0, concat_axis=0, tiled=True))
    fresh_peak, fresh_sum, fresh_acc, own_peak, own_sum, own_acc, valid, tables = local

    flat_queries = queries.reshape(req_dev, qlen * heads, head_dim)
    outputs = []
    for r in range(req_dev):
        one = slice(r, r + 1)
        arrived = arrivals[r]
        if outputs:
            arrived, outputs[-1] = lax.optimization_barrier((arrived, outputs[-1]))
        cached = cached_attention(
            flat_queries[one],
            arrived.reshape(pool_count, 1, n_slots * peer_pages, 2, page_rows, head_dim),
            valid[one],
            tables[one],
            score_scale,
        )
        cached = (
            cached[0].reshape(1, qlen, kv_heads, group_size),
            cached[1].reshape(1, qlen, kv_heads, group_size),
            cached[2].reshape(1, qlen, kv_heads, group_size, head_dim),
        )
        total = combine(
            combine(cached, (fresh_peak[one], fresh_sum[one], fresh_acc[one])),
            (own_peak[one], own_sum[one], own_acc[one]),
        )
        attn = total[2] / total[1][..., None]
        live = steps_q < own_lengths[r]
        attn = (
            jnp.where(live[None, :, None, None, None], attn, 0.0)
            .astype(jnp.bfloat16)
            .reshape(1, qlen, heads * head_dim)
        )
        partial_out = jnp.einsum("rqh,hm->rqm", attn, w_out, preferred_element_type=jnp.float32)
        outputs.append(partial_out.astype(jnp.bfloat16))
    pieces = jnp.concatenate(outputs, axis=0).reshape(req_dev, qlen, tp_count, -1).transpose(2, 0, 1, 3)
    pieces = lax.all_to_all(pieces, "tp", split_axis=0, concat_axis=0, tiled=True)
    return jnp.sum(pieces.astype(jnp.float32), axis=0).astype(jnp.bfloat16)


def solution(mesh):
    return jax.shard_map(
        shards,
        mesh=mesh,
        in_specs=(
            P("pool", "tp", None, None, None),
            P(),
            P(),
            P(),
            P(),
            P(),
            P("pool", None, "tp", None),
            P("pool", None, None, "tp", None),
            P("pool", None, None, "tp"),
            P(None, None, "tp", None),
            P("tp", None),
        ),
        out_specs=P("pool", None, "tp"),
        check_vma=False,
    )
```

```python
import functools

import jax
import jax.numpy as jnp
from jax import lax
from jax.experimental import pallas as pl
from jax.experimental.pallas import tpu as pltpu
from jax.sharding import PartitionSpec as P

THETA = 1000000.0
NEGATIVE = -1e30


def rotate(vectors, position):
    halfway = vectors.shape[-1] // 2
    frequency = THETA ** (-(jnp.arange(halfway, dtype=jnp.float32) * 2.0) / vectors.shape[-1])
    angles = position[..., None] * frequency
    cosine_part = jnp.cos(angles)
    sine_part = jnp.sin(angles)
    leading = vectors[..., :halfway]
    trailing = vectors[..., halfway:]
    return jnp.concatenate(
        [
            leading * cosine_part - trailing * sine_part,
            trailing * cosine_part + leading * sine_part,
        ],
        axis=-1,
    )


def summarize(scores, valid):
    masked = jnp.where(valid, scores, NEGATIVE)
    peak = jnp.max(masked, axis=-1)
    powers = jnp.where(valid, jnp.exp(masked - peak[..., None]), 0.0)
    return (peak, jnp.sum(powers, axis=-1), powers.astype(jnp.bfloat16))


def combine(former, latter):
    peak = jnp.maximum(former[0], latter[0])
    former_factor = jnp.exp(former[0] - peak)
    latter_factor = jnp.exp(latter[0] - peak)
    return (
        peak,
        former[1] * former_factor + latter[1] * latter_factor,
        former[2] * former_factor[..., None] + latter[2] * latter_factor[..., None],
    )


def merge_normalised(peaks, sums, normalised, axis):
    merged_peak = jnp.max(peaks, axis=axis)
    weight = sums * jnp.exp(peaks - jnp.expand_dims(merged_peak, axis))
    return (
        merged_peak,
        jnp.sum(weight, axis=axis),
        jnp.sum(normalised.astype(jnp.float32) * weight[..., None], axis=axis),
    )


def local_pages(pages, device, pages_dev, peer_pages):
    here = pages // pages_dev == device
    ranking = jnp.cumsum(here.astype(jnp.int32), axis=-1) - 1
    picks = here[..., None, :] & (
        ranking[..., None, :] == jnp.arange(peer_pages, dtype=jnp.int32)[:, None]
    )
    slot_ids = jnp.sum(jnp.where(picks, (pages % pages_dev)[..., None, :], 0), axis=-1)
    page_index = jnp.sum(jnp.where(picks, jnp.arange(pages.shape[-1], dtype=jnp.int32), 0), axis=-1)
    return (slot_ids, page_index)


def frequencies(head_dim):
    halfway = head_dim // 2
    return THETA ** (-(jnp.arange(halfway, dtype=jnp.float32) * 2.0) / head_dim)


SET_BLOCK = 8


def cached_kernel(scale, q_ref, kv_ref, valid_ref, table_ref, peak_ref, sum_ref, num_ref, m_acc, w_acc, n_acc):
    block = pl.program_id(1)
    n_blocks = pl.num_programs(1)
    n_pages = kv_ref.shape[2]
    page_rows = kv_ref.shape[4]
    head_dim = kv_ref.shape[5]
    n_slots = table_ref.shape[1] // 2
    slot_rows = (n_pages // n_slots) * page_rows

    @pl.when(block == 0)
    def _():
        m_acc[...] = jnp.full(m_acc.shape, NEGATIVE, jnp.float32)
        w_acc[...] = jnp.zeros(w_acc.shape, jnp.float32)
        n_acc[...] = jnp.zeros(n_acc.shape, jnp.float32)

    query = q_ref[0]
    table = table_ref[0]
    cosine = jnp.concatenate(
        [jnp.broadcast_to(table[2 * c : 2 * c + 1], (slot_rows, head_dim)) for c in range(n_slots)], axis=0
    )
    sine = jnp.concatenate(
        [jnp.broadcast_to(table[2 * c + 1 : 2 * c + 2], (slot_rows, head_dim)) for c in range(n_slots)], axis=0
    )

    def one_set(i, carry):
        keys = kv_ref[i, 0, :, 0].reshape(n_pages * page_rows, head_dim).astype(jnp.float32)
        values = kv_ref[i, 0, :, 1].reshape(n_pages * page_rows, head_dim)
        keys = (keys * cosine + pltpu.roll(keys, head_dim // 2, 1) * sine).astype(jnp.bfloat16)
        scores = lax.dot_general(
            keys, query, (((1,), (1,)), ((), ())), preferred_element_type=jnp.float32
        ) * scale
        valid = valid_ref[0, i] > 0.5
        masked = jnp.where(valid, scores, NEGATIVE)
        peak = jnp.max(masked, axis=0, keepdims=True)
        powers = jnp.exp(masked - jnp.maximum(peak, 0.1 * NEGATIVE))
        total = jnp.sum(powers, axis=0, keepdims=True)
        acc = lax.dot_general(
            values, powers.astype(jnp.bfloat16), (((0,), (0,)), ((), ())),
            preferred_element_type=jnp.float32,
        )
        inverse = 1.0 / jnp.maximum(total, 1.0)
        normalised = (acc * inverse).astype(jnp.bfloat16).astype(jnp.float32)
        old = m_acc[...]
        merged = jnp.maximum(old, peak)
        rescale = jnp.exp(old - merged)
        weight = total * jnp.exp(peak - merged)
        m_acc[...] = merged
        w_acc[...] = w_acc[...] * rescale + weight
        n_acc[...] = n_acc[...] * rescale + normalised * weight
        return carry

    lax.fori_loop(0, kv_ref.shape[0], one_set, 0)

    @pl.when(block == n_blocks - 1)
    def _():
        peak_ref[0] = m_acc[...]
        sum_ref[0] = w_acc[...]
        num_ref[0] = n_acc[...]


def cached_attention(queries, arrived, valid, tables, scale):
    req_dev, rows, head_dim = queries.shape
    pool_count = arrived.shape[0]
    kv_block = (SET_BLOCK,) + (1,) + arrived.shape[2:]
    valid = valid[..., None]
    peak, total, num = pl.pallas_call(
        functools.partial(cached_kernel, scale),
        grid=(req_dev, pool_count // SET_BLOCK),
        in_specs=[
            pl.BlockSpec((1, rows, head_dim), lambda r, j: (r, 0, 0)),
            pl.BlockSpec(kv_block, lambda r, j: (j, r, 0, 0, 0, 0)),
            pl.BlockSpec((1, SET_BLOCK, valid.shape[2], 1), lambda r, j: (r, j, 0, 0)),
            pl.BlockSpec((1,) + tables.shape[1:], lambda r, j: (r, 0, 0)),
        ],
        out_specs=[
            pl.BlockSpec((1, 1, rows), lambda r, j: (r, 0, 0)),
            pl.BlockSpec((1, 1, rows), lambda r, j: (r, 0, 0)),
            pl.BlockSpec((1, head_dim, rows), lambda r, j: (r, 0, 0)),
        ],
        out_shape=[
            jax.ShapeDtypeStruct((req_dev, 1, rows), jnp.float32),
            jax.ShapeDtypeStruct((req_dev, 1, rows), jnp.float32),
            jax.ShapeDtypeStruct((req_dev, head_dim, rows), jnp.float32),
        ],
        scratch_shapes=[
            pltpu.VMEM((1, rows), jnp.float32),
            pltpu.VMEM((1, rows), jnp.float32),
            pltpu.VMEM((head_dim, rows), jnp.float32),
        ],
        compiler_params=pltpu.CompilerParams(dimension_semantics=("parallel", "arbitrary")),
    )(queries, arrived, valid, tables)
    return (peak, total, jnp.swapaxes(num, 1, 2))

def shards(
    pool_kv,
    span_pages,
    req_spans,
    span_offsets,
    recompute_rows,
    question_lengths,
    question_q,
    question_kv,
    recompute_hidden,
    w_kv,
    w_out,
):
    pool_count = lax.axis_size("pool")
    device = lax.axis_index("pool")
    req_dev = question_q.shape[0]
    qlen = question_q.shape[1]
    heads = question_q.shape[2]
    head_dim = question_q.shape[3]
    pages_dev = pool_kv.shape[0]
    kv_heads = pool_kv.shape[1]
    page_rows = pool_kv.shape[3]
    group_size = heads // kv_heads
    n_slots = req_spans.shape[1]
    pages_span = span_pages.shape[1]
    span_rows = pages_span * page_rows
    peer_pages = pages_span // pool_count
    score_scale = head_dim ** (-0.5)
    first_request = device * req_dev
    own_spans = lax.dynamic_slice_in_dim(req_spans, first_request, req_dev, 0)
    own_offsets = lax.dynamic_slice_in_dim(span_offsets, first_request, req_dev, 0).astype(
        jnp.float32
    )
    own_rows = lax.dynamic_slice_in_dim(recompute_rows, first_request, req_dev, 0)
    own_lengths = lax.dynamic_slice_in_dim(question_lengths, first_request, req_dev, 0)
    steps_q = jnp.arange(qlen, dtype=jnp.int32)
    qpos = (n_slots * span_rows + steps_q).astype(jnp.float32)
    queries = rotate(question_q.astype(jnp.float32), qpos[None, :, None]).astype(jnp.bfloat16)
    grouped = queries.reshape(req_dev, qlen, kv_heads, group_size, head_dim)
    own_keys = rotate(question_kv[:, :, 0].astype(jnp.float32), qpos[None, :, None]).astype(
        jnp.bfloat16
    )
    own_values = question_kv[:, :, 1]
    tp_count = lax.axis_size("tp")
    rank = lax.axis_index("tp")
    width = recompute_hidden.shape[3]
    hidden = jnp.stack(
        [recompute_hidden]
        + [
            lax.ppermute(recompute_hidden, "tp", [(i, (i + k) % tp_count) for i in range(tp_count)])
            for k in range(1, tp_count)
        ]
    )
    weights = jnp.stack(
        [
            lax.dynamic_slice_in_dim(w_kv, ((rank - k) % tp_count) * width, width, axis=0)
            for k in range(tp_count)
        ]
    )
    widened = hidden.astype(jnp.float32)
    square_mean = jnp.sum(widened * widened, axis=(0, 4)) / (tp_count * width)
    normed = (widened * lax.rsqrt(square_mean + 1e-06)[None, ..., None]).astype(jnp.bfloat16)
    fresh = jnp.einsum("trcnd,tdskh->rcnskh", normed, weights, preferred_element_type=jnp.float32)
    fresh_pos = own_offsets[:, :, None] + own_rows.astype(jnp.float32)
    fresh_keys = rotate(fresh[:, :, :, 0], fresh_pos[..., None]).astype(jnp.bfloat16)
    fresh_values = fresh[:, :, :, 1].astype(jnp.bfloat16)
    fresh_scores = (
        jnp.einsum("rqkgd,rcnkd->rqkgcn", grouped, fresh_keys, preferred_element_type=jnp.float32)
        * score_scale
    )
    fresh_scores = fresh_scores.reshape(req_dev, qlen, kv_heads, group_size, -1)
    fresh_peak, fresh_sum, fresh_weights = summarize(fresh_scores, True)
    fresh_acc = jnp.einsum(
        "rqkgn,rnkd->rqkgd",
        fresh_weights,
        fresh_values.reshape(req_dev, -1, kv_heads, head_dim),
        preferred_element_type=jnp.float32,
    )
    visible = (steps_q[None, None, :] <= steps_q[None, :, None]) & (
        steps_q[None, None, :] < own_lengths[:, None, None]
    )
    own_scores = (
        jnp.einsum("rqkgd,rjkd->rqkgj", grouped, own_keys, preferred_element_type=jnp.float32)
        * score_scale
    )
    own_peak, own_sum, own_weights = summarize(own_scores, visible[:, :, None, None, :])
    own_acc = jnp.einsum(
        "rqkgj,rjkd->rqkgd", own_weights, own_values, preferred_element_type=jnp.float32
    )
    own_keys = rotate(question_kv[:, :, 0].astype(jnp.float32), qpos[None, :, None]).astype(
        jnp.bfloat16
    )
    own_values = question_kv[:, :, 1]
    tp_count = lax.axis_size("tp")
    rank = lax.axis_index("tp")
    width = recompute_hidden.shape[3]
    hidden = jnp.stack(
        [recompute_hidden]
        + [
            lax.ppermute(recompute_hidden, "tp", [(i, (i + k) % tp_count) for i in range(tp_count)])
            for k in range(1, tp_count)
        ]
    )
    weights = jnp.stack(
        [
            lax.dynamic_slice_in_dim(w_kv, ((rank - k) % tp_count) * width, width, axis=0)
            for k in range(tp_count)
        ]
    )
    widened = hidden.astype(jnp.float32)
    square_mean = jnp.sum(widened * widened, axis=(0, 4)) / (tp_count * width)
    normed = (widened * lax.rsqrt(square_mean + 1e-06)[None, ..., None]).astype(jnp.bfloat16)
    fresh = jnp.einsum("trcnd,tdskh->rcnskh", normed, weights, preferred_element_type=jnp.float32)
    fresh_pos = own_offsets[:, :, None] + own_rows.astype(jnp.float32)
    fresh_keys = rotate(fresh[:, :, :, 0], fresh_pos[..., None]).astype(jnp.bfloat16)
    fresh_values = fresh[:, :, :, 1].astype(jnp.bfloat16)
    fresh_scores = (
        jnp.einsum("rqkgd,rcnkd->rqkgcn", grouped, fresh_keys, preferred_element_type=jnp.float32)
        * score_scale
    )
    fresh_scores = fresh_scores.reshape(req_dev, qlen, kv_heads, group_size, -1)
    fresh_peak, fresh_sum, fresh_weights = summarize(fresh_scores, True)
    fresh_acc = jnp.einsum(
        "rqkgn,rnkd->rqkgd",
        fresh_weights,
        fresh_values.reshape(req_dev, -1, kv_heads, head_dim),
        preferred_element_type=jnp.float32,
    )
    visible = (steps_q[None, None, :] <= steps_q[None, :, None]) & (
        steps_q[None, None, :] < own_lengths[:, None, None]
    )
    own_scores = (
        jnp.einsum("rqkgd,rjkd->rqkgj", grouped, own_keys, preferred_element_type=jnp.float32)
        * score_scale
    )
    own_peak, own_sum, own_weights = summarize(own_scores, visible[:, :, None, None, :])
    own_acc = jnp.einsum(
        "rqkgj,rjkd->rqkgd", own_weights, own_values, preferred_element_type=jnp.float32
    )

    mine = span_pages[own_spans]
    unused_slots, page_index = local_pages(
        mine[:, :, None, :], jnp.arange(pool_count, dtype=jnp.int32)[:, None], pages_dev, peer_pages
    )
    row_ids = page_index[..., None] * page_rows + jnp.arange(page_rows, dtype=jnp.int32)
    replaced = jnp.any(row_ids[..., None] == own_rows[:, :, None, None, None, :], axis=-1)
    valid = jnp.logical_not(replaced).transpose(0, 2, 1, 3, 4).reshape(req_dev, pool_count, -1)
    valid = valid.astype(jnp.float32)
    angles = own_offsets[..., None] * frequencies(head_dim)
    tables = jnp.stack(
        [
            jnp.concatenate([jnp.cos(angles), jnp.cos(angles)], axis=-1),
            jnp.concatenate([-jnp.sin(angles), jnp.sin(angles)], axis=-1),
        ],
        axis=2,
    ).reshape(req_dev, 2 * n_slots, head_dim)
    local = (fresh_peak, fresh_sum, fresh_acc, own_peak, own_sum, own_acc, valid, tables)

    all_pages = span_pages[req_spans]
    slot_ids, unused_index = local_pages(all_pages, device, pages_dev, peer_pages)
    slot_ids = slot_ids.reshape((pool_count, req_dev) + slot_ids.shape[1:])
    arrivals = []
    for r in range(req_dev):
        outgoing = pool_kv[slot_ids[:, r]]
        if arrivals:
            arrivals[-1], outgoing, local = lax.optimization_barrier((arrivals[-1], outgoing, local))
        arrivals.append(lax.all_to_all(outgoing, "pool", split_axis=0, concat_axis=0, tiled=True))
    fresh_peak, fresh_sum, fresh_acc, own_peak, own_sum, own_acc, valid, tables = local

    flat_queries = queries.reshape(req_dev, qlen * heads, head_dim)
    outputs = []
    for r in range(req_dev):
        one = slice(r, r + 1)
        arrived = arrivals[r]
        if outputs:
            arrived, outputs[-1] = lax.optimization_barrier((arrived, outputs[-1]))
        cached = cached_attention(
            flat_queries[one],
            arrived.reshape(pool_count, 1, n_slots * peer_pages, 2, page_rows, head_dim),
            valid[one],
            tables[one],
            score_scale,
        )
        cached = (
            cached[0].reshape(1, qlen, kv_heads, group_size),
            cached[1].reshape(1, qlen, kv_heads, group_size),
            cached[2].reshape(1, qlen, kv_heads, group_size, head_dim),
        )
        total = combine(
            combine(cached, (fresh_peak[one], fresh_sum[one], fresh_acc[one])),
            (own_peak[one], own_sum[one], own_acc[one]),
        )
        attn = total[2] / total[1][..., None]
        live = steps_q < own_lengths[r]
        attn = (
            jnp.where(live[None, :, None, None, None], attn, 0.0)
            .astype(jnp.bfloat16)
            .reshape(1, qlen, heads * head_dim)
        )
        partial_out = jnp.einsum("rqh,hm->rqm", attn, w_out, preferred_element_type=jnp.float32)
        pieces = partial_out.astype(jnp.bfloat16).reshape(1, qlen, tp_count, -1)
        if r < req_dev - 1:
            own = lax.dynamic_index_in_dim(pieces, rank, axis=2, keepdims=False)
            received = [own] + [
                lax.ppermute(
                    lax.dynamic_index_in_dim(pieces, (rank + k) % tp_count, axis=2, keepdims=False),
                    "tp",
                    [(i, (i + k) % tp_count) for i in range(tp_count)],
                )
                for k in range(1, tp_count)
            ]
            reduced = jnp.sum(jnp.stack(received).astype(jnp.float32), axis=0)
        else:
            pieces = lax.all_to_all(
                pieces.transpose(2, 0, 1, 3), "tp", split_axis=0, concat_axis=0, tiled=True
            )
            reduced = jnp.sum(pieces.astype(jnp.float32), axis=0)
        outputs.append(reduced.astype(jnp.bfloat16))
    return jnp.concatenate(outputs, axis=0)


def solution(mesh):
    return jax.shard_map(
        shards,
        mesh=mesh,
        in_specs=(
            P("pool", "tp", None, None, None),
            P(),
            P(),
            P(),
            P(),
            P(),
            P("pool", None, "tp", None),
            P("pool", None, None, "tp", None),
            P("pool", None, None, "tp"),
            P(None, None, "tp", None),
            P("tp", None),
        ),
        out_specs=P("pool", None, "tp"),
        check_vma=False,
    )
```

```python
import functools

import jax
import jax.numpy as jnp
from jax import lax
from jax.experimental import pallas as pl
from jax.experimental.pallas import tpu as pltpu
from jax.sharding import PartitionSpec as P

THETA = 1000000.0
NEGATIVE = -1e30


def rotate(vectors, position):
    halfway = vectors.shape[-1] // 2
    frequency = THETA ** (-(jnp.arange(halfway, dtype=jnp.float32) * 2.0) / vectors.shape[-1])
    angles = position[..., None] * frequency
    cosine_part = jnp.cos(angles)
    sine_part = jnp.sin(angles)
    leading = vectors[..., :halfway]
    trailing = vectors[..., halfway:]
    return jnp.concatenate(
        [
            leading * cosine_part - trailing * sine_part,
            trailing * cosine_part + leading * sine_part,
        ],
        axis=-1,
    )


def summarize(scores, valid):
    masked = jnp.where(valid, scores, NEGATIVE)
    peak = jnp.max(masked, axis=-1)
    powers = jnp.where(valid, jnp.exp(masked - peak[..., None]), 0.0)
    return (peak, jnp.sum(powers, axis=-1), powers.astype(jnp.bfloat16))


def combine(former, latter):
    peak = jnp.maximum(former[0], latter[0])
    former_factor = jnp.exp(former[0] - peak)
    latter_factor = jnp.exp(latter[0] - peak)
    return (
        peak,
        former[1] * former_factor + latter[1] * latter_factor,
        former[2] * former_factor[..., None] + latter[2] * latter_factor[..., None],
    )


def merge_normalised(peaks, sums, normalised, axis):
    merged_peak = jnp.max(peaks, axis=axis)
    weight = sums * jnp.exp(peaks - jnp.expand_dims(merged_peak, axis))
    return (
        merged_peak,
        jnp.sum(weight, axis=axis),
        jnp.sum(normalised.astype(jnp.float32) * weight[..., None], axis=axis),
    )


def local_pages(pages, device, pages_dev, peer_pages):
    here = pages // pages_dev == device
    ranking = jnp.cumsum(here.astype(jnp.int32), axis=-1) - 1
    picks = here[..., None, :] & (
        ranking[..., None, :] == jnp.arange(peer_pages, dtype=jnp.int32)[:, None]
    )
    slot_ids = jnp.sum(jnp.where(picks, (pages % pages_dev)[..., None, :], 0), axis=-1)
    page_index = jnp.sum(jnp.where(picks, jnp.arange(pages.shape[-1], dtype=jnp.int32), 0), axis=-1)
    return (slot_ids, page_index)


def frequencies(head_dim):
    halfway = head_dim // 2
    return THETA ** (-(jnp.arange(halfway, dtype=jnp.float32) * 2.0) / head_dim)


SET_BLOCK = 8


def cached_kernel(scale, q_ref, kv_ref, valid_ref, table_ref, peak_ref, sum_ref, num_ref, m_acc, w_acc, n_acc):
    block = pl.program_id(1)
    n_blocks = pl.num_programs(1)
    n_pages = kv_ref.shape[2]
    page_rows = kv_ref.shape[4]
    head_dim = kv_ref.shape[5]
    n_slots = table_ref.shape[1] // 2
    slot_rows = (n_pages // n_slots) * page_rows

    @pl.when(block == 0)
    def _():
        m_acc[...] = jnp.full(m_acc.shape, NEGATIVE, jnp.float32)
        w_acc[...] = jnp.zeros(w_acc.shape, jnp.float32)
        n_acc[...] = jnp.zeros(n_acc.shape, jnp.float32)

    query = q_ref[0]
    table = table_ref[0]
    cosine = jnp.concatenate(
        [jnp.broadcast_to(table[2 * c : 2 * c + 1], (slot_rows, head_dim)) for c in range(n_slots)], axis=0
    )
    sine = jnp.concatenate(
        [jnp.broadcast_to(table[2 * c + 1 : 2 * c + 2], (slot_rows, head_dim)) for c in range(n_slots)], axis=0
    )

    def one_set(i, carry):
        keys = kv_ref[i, 0, :, 0].reshape(n_pages * page_rows, head_dim).astype(jnp.float32)
        values = kv_ref[i, 0, :, 1].reshape(n_pages * page_rows, head_dim)
        keys = (keys * cosine + pltpu.roll(keys, head_dim // 2, 1) * sine).astype(jnp.bfloat16)
        scores = lax.dot_general(
            keys, query, (((1,), (1,)), ((), ())), preferred_element_type=jnp.float32
        ) * scale
        valid = valid_ref[0, i] > 0.5
        masked = jnp.where(valid, scores, NEGATIVE)
        peak = jnp.max(masked, axis=0, keepdims=True)
        powers = jnp.exp(masked - jnp.maximum(peak, 0.1 * NEGATIVE))
        total = jnp.sum(powers, axis=0, keepdims=True)
        acc = lax.dot_general(
            values, powers.astype(jnp.bfloat16), (((0,), (0,)), ((), ())),
            preferred_element_type=jnp.float32,
        )
        inverse = 1.0 / jnp.maximum(total, 1.0)
        normalised = (acc * inverse).astype(jnp.bfloat16).astype(jnp.float32)
        old = m_acc[...]
        merged = jnp.maximum(old, peak)
        rescale = jnp.exp(old - merged)
        weight = total * jnp.exp(peak - merged)
        m_acc[...] = merged
        w_acc[...] = w_acc[...] * rescale + weight
        n_acc[...] = n_acc[...] * rescale + normalised * weight
        return carry

    lax.fori_loop(0, kv_ref.shape[0], one_set, 0)

    @pl.when(block == n_blocks - 1)
    def _():
        peak_ref[0] = m_acc[...]
        sum_ref[0] = w_acc[...]
        num_ref[0] = n_acc[...]


def cached_attention(queries, arrived, valid, tables, scale):
    req_dev, rows, head_dim = queries.shape
    pool_count = arrived.shape[0]
    kv_block = (SET_BLOCK,) + (1,) + arrived.shape[2:]
    valid = valid[..., None]
    peak, total, num = pl.pallas_call(
        functools.partial(cached_kernel, scale),
        grid=(req_dev, pool_count // SET_BLOCK),
        in_specs=[
            pl.BlockSpec((1, rows, head_dim), lambda r, j: (r, 0, 0)),
            pl.BlockSpec(kv_block, lambda r, j: (j, r, 0, 0, 0, 0)),
            pl.BlockSpec((1, SET_BLOCK, valid.shape[2], 1), lambda r, j: (r, j, 0, 0)),
            pl.BlockSpec((1,) + tables.shape[1:], lambda r, j: (r, 0, 0)),
        ],
        out_specs=[
            pl.BlockSpec((1, 1, rows), lambda r, j: (r, 0, 0)),
            pl.BlockSpec((1, 1, rows), lambda r, j: (r, 0, 0)),
            pl.BlockSpec((1, head_dim, rows), lambda r, j: (r, 0, 0)),
        ],
        out_shape=[
            jax.ShapeDtypeStruct((req_dev, 1, rows), jnp.float32),
            jax.ShapeDtypeStruct((req_dev, 1, rows), jnp.float32),
            jax.ShapeDtypeStruct((req_dev, head_dim, rows), jnp.float32),
        ],
        scratch_shapes=[
            pltpu.VMEM((1, rows), jnp.float32),
            pltpu.VMEM((1, rows), jnp.float32),
            pltpu.VMEM((head_dim, rows), jnp.float32),
        ],
        compiler_params=pltpu.CompilerParams(dimension_semantics=("parallel", "arbitrary")),
    )(queries, arrived, valid, tables)
    return (peak, total, jnp.swapaxes(num, 1, 2))

def shards(
    pool_kv,
    span_pages,
    req_spans,
    span_offsets,
    recompute_rows,
    question_lengths,
    question_q,
    question_kv,
    recompute_hidden,
    w_kv,
    w_out,
):
    pool_count = lax.axis_size("pool")
    device = lax.axis_index("pool")
    req_dev = question_q.shape[0]
    qlen = question_q.shape[1]
    heads = question_q.shape[2]
    head_dim = question_q.shape[3]
    pages_dev = pool_kv.shape[0]
    kv_heads = pool_kv.shape[1]
    page_rows = pool_kv.shape[3]
    group_size = heads // kv_heads
    n_slots = req_spans.shape[1]
    pages_span = span_pages.shape[1]
    span_rows = pages_span * page_rows
    peer_pages = pages_span // pool_count
    score_scale = head_dim ** (-0.5)
    first_request = device * req_dev
    own_spans = lax.dynamic_slice_in_dim(req_spans, first_request, req_dev, 0)
    own_offsets = lax.dynamic_slice_in_dim(span_offsets, first_request, req_dev, 0).astype(
        jnp.float32
    )
    own_rows = lax.dynamic_slice_in_dim(recompute_rows, first_request, req_dev, 0)
    own_lengths = lax.dynamic_slice_in_dim(question_lengths, first_request, req_dev, 0)
    steps_q = jnp.arange(qlen, dtype=jnp.int32)
    qpos = (n_slots * span_rows + steps_q).astype(jnp.float32)
    queries = rotate(question_q.astype(jnp.float32), qpos[None, :, None]).astype(jnp.bfloat16)
    grouped = queries.reshape(req_dev, qlen, kv_heads, group_size, head_dim)
    own_keys = rotate(question_kv[:, :, 0].astype(jnp.float32), qpos[None, :, None]).astype(
        jnp.bfloat16
    )
    own_values = question_kv[:, :, 1]
    tp_count = lax.axis_size("tp")
    rank = lax.axis_index("tp")
    width = recompute_hidden.shape[3]
    hidden = jnp.stack(
        [recompute_hidden]
        + [
            lax.ppermute(recompute_hidden, "tp", [(i, (i + k) % tp_count) for i in range(tp_count)])
            for k in range(1, tp_count)
        ]
    )
    weights = jnp.take(
        w_kv.reshape((tp_count, width) + w_kv.shape[1:]),
        (rank - jnp.arange(tp_count, dtype=jnp.int32)) % tp_count,
        axis=0,
    )
    widened = hidden.astype(jnp.float32)
    square_mean = jnp.sum(widened * widened, axis=(0, 4)) / (tp_count * width)
    normed = (widened * lax.rsqrt(square_mean + 1e-06)[None, ..., None]).astype(jnp.bfloat16)
    fresh = jnp.einsum("trcnd,tdskh->rcnskh", normed, weights, preferred_element_type=jnp.float32)
    fresh_pos = own_offsets[:, :, None] + own_rows.astype(jnp.float32)
    fresh_keys = rotate(fresh[:, :, :, 0], fresh_pos[..., None]).astype(jnp.bfloat16)
    fresh_values = fresh[:, :, :, 1].astype(jnp.bfloat16)
    fresh_scores = (
        jnp.einsum("rqkgd,rcnkd->rqkgcn", grouped, fresh_keys, preferred_element_type=jnp.float32)
        * score_scale
    )
    fresh_scores = fresh_scores.reshape(req_dev, qlen, kv_heads, group_size, -1)
    fresh_peak, fresh_sum, fresh_weights = summarize(fresh_scores, True)
    fresh_acc = jnp.einsum(
        "rqkgn,rnkd->rqkgd",
        fresh_weights,
        fresh_values.reshape(req_dev, -1, kv_heads, head_dim),
        preferred_element_type=jnp.float32,
    )
    visible = (steps_q[None, None, :] <= steps_q[None, :, None]) & (
        steps_q[None, None, :] < own_lengths[:, None, None]
    )
    own_scores = (
        jnp.einsum("rqkgd,rjkd->rqkgj", grouped, own_keys, preferred_element_type=jnp.float32)
        * score_scale
    )
    own_peak, own_sum, own_weights = summarize(own_scores, visible[:, :, None, None, :])
    own_acc = jnp.einsum(
        "rqkgj,rjkd->rqkgd", own_weights, own_values, preferred_element_type=jnp.float32
    )
    own_keys = rotate(question_kv[:, :, 0].astype(jnp.float32), qpos[None, :, None]).astype(
        jnp.bfloat16
    )
    own_values = question_kv[:, :, 1]
    tp_count = lax.axis_size("tp")
    rank = lax.axis_index("tp")
    width = recompute_hidden.shape[3]
    hidden = jnp.stack(
        [recompute_hidden]
        + [
            lax.ppermute(recompute_hidden, "tp", [(i, (i + k) % tp_count) for i in range(tp_count)])
            for k in range(1, tp_count)
        ]
    )
    weights = jnp.take(
        w_kv.reshape((tp_count, width) + w_kv.shape[1:]),
        (rank - jnp.arange(tp_count, dtype=jnp.int32)) % tp_count,
        axis=0,
    )
    widened = hidden.astype(jnp.float32)
    square_mean = jnp.sum(widened * widened, axis=(0, 4)) / (tp_count * width)
    normed = (widened * lax.rsqrt(square_mean + 1e-06)[None, ..., None]).astype(jnp.bfloat16)
    fresh = jnp.einsum("trcnd,tdskh->rcnskh", normed, weights, preferred_element_type=jnp.float32)
    fresh_pos = own_offsets[:, :, None] + own_rows.astype(jnp.float32)
    fresh_keys = rotate(fresh[:, :, :, 0], fresh_pos[..., None]).astype(jnp.bfloat16)
    fresh_values = fresh[:, :, :, 1].astype(jnp.bfloat16)
    fresh_scores = (
        jnp.einsum("rqkgd,rcnkd->rqkgcn", grouped, fresh_keys, preferred_element_type=jnp.float32)
        * score_scale
    )
    fresh_scores = fresh_scores.reshape(req_dev, qlen, kv_heads, group_size, -1)
    fresh_peak, fresh_sum, fresh_weights = summarize(fresh_scores, True)
    fresh_acc = jnp.einsum(
        "rqkgn,rnkd->rqkgd",
        fresh_weights,
        fresh_values.reshape(req_dev, -1, kv_heads, head_dim),
        preferred_element_type=jnp.float32,
    )
    visible = (steps_q[None, None, :] <= steps_q[None, :, None]) & (
        steps_q[None, None, :] < own_lengths[:, None, None]
    )
    own_scores = (
        jnp.einsum("rqkgd,rjkd->rqkgj", grouped, own_keys, preferred_element_type=jnp.float32)
        * score_scale
    )
    own_peak, own_sum, own_weights = summarize(own_scores, visible[:, :, None, None, :])
    own_acc = jnp.einsum(
        "rqkgj,rjkd->rqkgd", own_weights, own_values, preferred_element_type=jnp.float32
    )

    mine = span_pages[own_spans]
    unused_slots, page_index = local_pages(
        mine[:, :, None, :], jnp.arange(pool_count, dtype=jnp.int32)[:, None], pages_dev, peer_pages
    )
    row_ids = page_index[..., None] * page_rows + jnp.arange(page_rows, dtype=jnp.int32)
    replaced = jnp.any(row_ids[..., None] == own_rows[:, :, None, None, None, :], axis=-1)
    valid = jnp.logical_not(replaced).transpose(0, 2, 1, 3, 4).reshape(req_dev, pool_count, -1)
    valid = valid.astype(jnp.float32)
    angles = own_offsets[..., None] * frequencies(head_dim)
    tables = jnp.stack(
        [
            jnp.concatenate([jnp.cos(angles), jnp.cos(angles)], axis=-1),
            jnp.concatenate([-jnp.sin(angles), jnp.sin(angles)], axis=-1),
        ],
        axis=2,
    ).reshape(req_dev, 2 * n_slots, head_dim)
    local = (fresh_peak, fresh_sum, fresh_acc, own_peak, own_sum, own_acc, valid, tables)

    all_pages = span_pages[req_spans]
    slot_ids, unused_index = local_pages(all_pages, device, pages_dev, peer_pages)
    slot_ids = slot_ids.reshape((pool_count, req_dev) + slot_ids.shape[1:])
    arrivals = []
    for r in range(req_dev):
        outgoing = pool_kv[slot_ids[:, r]]
        if arrivals:
            arrivals[-1], outgoing, local = lax.optimization_barrier((arrivals[-1], outgoing, local))
        arrivals.append(lax.all_to_all(outgoing, "pool", split_axis=0, concat_axis=0, tiled=True))
    fresh_peak, fresh_sum, fresh_acc, own_peak, own_sum, own_acc, valid, tables = local

    flat_queries = queries.reshape(req_dev, qlen * heads, head_dim)
    outputs = []
    for r in range(req_dev):
        one = slice(r, r + 1)
        arrived = arrivals[r]
        if outputs:
            arrived, outputs[-1] = lax.optimization_barrier((arrived, outputs[-1]))
        cached = cached_attention(
            flat_queries[one],
            arrived.reshape(pool_count, 1, n_slots * peer_pages, 2, page_rows, head_dim),
            valid[one],
            tables[one],
            score_scale,
        )
        cached = (
            cached[0].reshape(1, qlen, kv_heads, group_size),
            cached[1].reshape(1, qlen, kv_heads, group_size),
            cached[2].reshape(1, qlen, kv_heads, group_size, head_dim),
        )
        total = combine(
            combine(cached, (fresh_peak[one], fresh_sum[one], fresh_acc[one])),
            (own_peak[one], own_sum[one], own_acc[one]),
        )
        attn = total[2] / total[1][..., None]
        live = steps_q < own_lengths[r]
        attn = (
            jnp.where(live[None, :, None, None, None], attn, 0.0)
            .astype(jnp.bfloat16)
            .reshape(1, qlen, heads * head_dim)
        )
        partial_out = jnp.einsum("rqh,hm->rqm", attn, w_out, preferred_element_type=jnp.float32)
        pieces = partial_out.astype(jnp.bfloat16).reshape(1, qlen, tp_count, -1)
        if r < req_dev - 1:
            rolled = jnp.take(
                pieces, (rank + jnp.arange(tp_count, dtype=jnp.int32)) % tp_count, axis=2
            )
            received = [rolled[:, :, 0]] + [
                lax.ppermute(
                    rolled[:, :, k], "tp", [(i, (i + k) % tp_count) for i in range(tp_count)]
                )
                for k in range(1, tp_count)
            ]
            reduced = jnp.sum(jnp.stack(received).astype(jnp.float32), axis=0)
        else:
            pieces = lax.all_to_all(
                pieces.transpose(2, 0, 1, 3), "tp", split_axis=0, concat_axis=0, tiled=True
            )
            reduced = jnp.sum(pieces.astype(jnp.float32), axis=0)
        outputs.append(reduced.astype(jnp.bfloat16))
    return jnp.concatenate(outputs, axis=0)


def solution(mesh):
    return jax.shard_map(
        shards,
        mesh=mesh,
        in_specs=(
            P("pool", "tp", None, None, None),
            P(),
            P(),
            P(),
            P(),
            P(),
            P("pool", None, "tp", None),
            P("pool", None, None, "tp", None),
            P("pool", None, None, "tp"),
            P(None, None, "tp", None),
            P("tp", None),
        ),
        out_specs=P("pool", None, "tp"),
        check_vma=False,
    )
```

```python
import functools

import jax
import jax.numpy as jnp
from jax import lax
from jax.experimental import pallas as pl
from jax.experimental.pallas import tpu as pltpu
from jax.sharding import PartitionSpec as P

THETA = 1000000.0
NEGATIVE = -1e30


def rotate(vectors, position):
    halfway = vectors.shape[-1] // 2
    frequency = THETA ** (-(jnp.arange(halfway, dtype=jnp.float32) * 2.0) / vectors.shape[-1])
    angles = position[..., None] * frequency
    cosine_part = jnp.cos(angles)
    sine_part = jnp.sin(angles)
    leading = vectors[..., :halfway]
    trailing = vectors[..., halfway:]
    return jnp.concatenate(
        [
            leading * cosine_part - trailing * sine_part,
            trailing * cosine_part + leading * sine_part,
        ],
        axis=-1,
    )


def summarize(scores, valid):
    masked = jnp.where(valid, scores, NEGATIVE)
    peak = jnp.max(masked, axis=-1)
    powers = jnp.where(valid, jnp.exp(masked - peak[..., None]), 0.0)
    return (peak, jnp.sum(powers, axis=-1), powers.astype(jnp.bfloat16))


def combine(former, latter):
    peak = jnp.maximum(former[0], latter[0])
    former_factor = jnp.exp(former[0] - peak)
    latter_factor = jnp.exp(latter[0] - peak)
    return (
        peak,
        former[1] * former_factor + latter[1] * latter_factor,
        former[2] * former_factor[..., None] + latter[2] * latter_factor[..., None],
    )


def merge_normalised(peaks, sums, normalised, axis):
    merged_peak = jnp.max(peaks, axis=axis)
    weight = sums * jnp.exp(peaks - jnp.expand_dims(merged_peak, axis))
    return (
        merged_peak,
        jnp.sum(weight, axis=axis),
        jnp.sum(normalised.astype(jnp.float32) * weight[..., None], axis=axis),
    )


def local_pages(pages, device, pages_dev, peer_pages):
    here = pages // pages_dev == device
    ranking = jnp.cumsum(here.astype(jnp.int32), axis=-1) - 1
    picks = here[..., None, :] & (
        ranking[..., None, :] == jnp.arange(peer_pages, dtype=jnp.int32)[:, None]
    )
    slot_ids = jnp.sum(jnp.where(picks, (pages % pages_dev)[..., None, :], 0), axis=-1)
    page_index = jnp.sum(jnp.where(picks, jnp.arange(pages.shape[-1], dtype=jnp.int32), 0), axis=-1)
    return (slot_ids, page_index)


def frequencies(head_dim):
    halfway = head_dim // 2
    return THETA ** (-(jnp.arange(halfway, dtype=jnp.float32) * 2.0) / head_dim)


SET_BLOCK = 8


def cached_kernel(scale, q_ref, kv_ref, valid_ref, table_ref, peak_ref, sum_ref, num_ref, m_acc, w_acc, n_acc):
    block = pl.program_id(1)
    n_blocks = pl.num_programs(1)
    n_pages = kv_ref.shape[2]
    page_rows = kv_ref.shape[4]
    head_dim = kv_ref.shape[5]
    n_slots = table_ref.shape[1] // 2
    slot_rows = (n_pages // n_slots) * page_rows

    @pl.when(block == 0)
    def _():
        m_acc[...] = jnp.full(m_acc.shape, NEGATIVE, jnp.float32)
        w_acc[...] = jnp.zeros(w_acc.shape, jnp.float32)
        n_acc[...] = jnp.zeros(n_acc.shape, jnp.float32)

    query = q_ref[0]
    table = table_ref[0]
    cosine = jnp.concatenate(
        [jnp.broadcast_to(table[2 * c : 2 * c + 1], (slot_rows, head_dim)) for c in range(n_slots)], axis=0
    )
    sine = jnp.concatenate(
        [jnp.broadcast_to(table[2 * c + 1 : 2 * c + 2], (slot_rows, head_dim)) for c in range(n_slots)], axis=0
    )

    def one_set(i, carry):
        keys = kv_ref[i, 0, :, 0].reshape(n_pages * page_rows, head_dim).astype(jnp.float32)
        values = kv_ref[i, 0, :, 1].reshape(n_pages * page_rows, head_dim)
        keys = (keys * cosine + pltpu.roll(keys, head_dim // 2, 1) * sine).astype(jnp.bfloat16)
        scores = lax.dot_general(
            keys, query, (((1,), (1,)), ((), ())), preferred_element_type=jnp.float32
        ) * scale
        valid = valid_ref[0, i] > 0.5
        masked = jnp.where(valid, scores, NEGATIVE)
        peak = jnp.max(masked, axis=0, keepdims=True)
        powers = jnp.exp(masked - jnp.maximum(peak, 0.1 * NEGATIVE))
        total = jnp.sum(powers, axis=0, keepdims=True)
        acc = lax.dot_general(
            values, powers.astype(jnp.bfloat16), (((0,), (0,)), ((), ())),
            preferred_element_type=jnp.float32,
        )
        inverse = 1.0 / jnp.maximum(total, 1.0)
        normalised = (acc * inverse).astype(jnp.bfloat16).astype(jnp.float32)
        old = m_acc[...]
        merged = jnp.maximum(old, peak)
        rescale = jnp.exp(old - merged)
        weight = total * jnp.exp(peak - merged)
        m_acc[...] = merged
        w_acc[...] = w_acc[...] * rescale + weight
        n_acc[...] = n_acc[...] * rescale + normalised * weight
        return carry

    lax.fori_loop(0, kv_ref.shape[0], one_set, 0)

    @pl.when(block == n_blocks - 1)
    def _():
        peak_ref[0] = m_acc[...]
        sum_ref[0] = w_acc[...]
        num_ref[0] = n_acc[...]


def cached_attention(queries, arrived, valid, tables, scale):
    req_dev, rows, head_dim = queries.shape
    pool_count = arrived.shape[0]
    kv_block = (SET_BLOCK,) + (1,) + arrived.shape[2:]
    valid = valid[..., None]
    peak, total, num = pl.pallas_call(
        functools.partial(cached_kernel, scale),
        grid=(req_dev, pool_count // SET_BLOCK),
        in_specs=[
            pl.BlockSpec((1, rows, head_dim), lambda r, j: (r, 0, 0)),
            pl.BlockSpec(kv_block, lambda r, j: (j, r, 0, 0, 0, 0)),
            pl.BlockSpec((1, SET_BLOCK, valid.shape[2], 1), lambda r, j: (r, j, 0, 0)),
            pl.BlockSpec((1,) + tables.shape[1:], lambda r, j: (r, 0, 0)),
        ],
        out_specs=[
            pl.BlockSpec((1, 1, rows), lambda r, j: (r, 0, 0)),
            pl.BlockSpec((1, 1, rows), lambda r, j: (r, 0, 0)),
            pl.BlockSpec((1, head_dim, rows), lambda r, j: (r, 0, 0)),
        ],
        out_shape=[
            jax.ShapeDtypeStruct((req_dev, 1, rows), jnp.float32),
            jax.ShapeDtypeStruct((req_dev, 1, rows), jnp.float32),
            jax.ShapeDtypeStruct((req_dev, head_dim, rows), jnp.float32),
        ],
        scratch_shapes=[
            pltpu.VMEM((1, rows), jnp.float32),
            pltpu.VMEM((1, rows), jnp.float32),
            pltpu.VMEM((head_dim, rows), jnp.float32),
        ],
        compiler_params=pltpu.CompilerParams(dimension_semantics=("parallel", "arbitrary")),
    )(queries, arrived, valid, tables)
    return (peak, total, jnp.swapaxes(num, 1, 2))

def shards(
    pool_kv,
    span_pages,
    req_spans,
    span_offsets,
    recompute_rows,
    question_lengths,
    question_q,
    question_kv,
    recompute_hidden,
    w_kv,
    w_out,
):
    pool_count = lax.axis_size("pool")
    device = lax.axis_index("pool")
    req_dev = question_q.shape[0]
    qlen = question_q.shape[1]
    heads = question_q.shape[2]
    head_dim = question_q.shape[3]
    pages_dev = pool_kv.shape[0]
    kv_heads = pool_kv.shape[1]
    page_rows = pool_kv.shape[3]
    group_size = heads // kv_heads
    n_slots = req_spans.shape[1]
    pages_span = span_pages.shape[1]
    span_rows = pages_span * page_rows
    peer_pages = pages_span // pool_count
    score_scale = head_dim ** (-0.5)
    first_request = device * req_dev
    own_spans = lax.dynamic_slice_in_dim(req_spans, first_request, req_dev, 0)
    own_offsets = lax.dynamic_slice_in_dim(span_offsets, first_request, req_dev, 0).astype(
        jnp.float32
    )
    own_rows = lax.dynamic_slice_in_dim(recompute_rows, first_request, req_dev, 0)
    own_lengths = lax.dynamic_slice_in_dim(question_lengths, first_request, req_dev, 0)
    steps_q = jnp.arange(qlen, dtype=jnp.int32)
    qpos = (n_slots * span_rows + steps_q).astype(jnp.float32)
    queries = rotate(question_q.astype(jnp.float32), qpos[None, :, None]).astype(jnp.bfloat16)
    grouped = queries.reshape(req_dev, qlen, kv_heads, group_size, head_dim)
    own_keys = rotate(question_kv[:, :, 0].astype(jnp.float32), qpos[None, :, None]).astype(
        jnp.bfloat16
    )
    own_values = question_kv[:, :, 1]
    tp_count = lax.axis_size("tp")
    rank = lax.axis_index("tp")
    width = recompute_hidden.shape[3]
    partner = lax.ppermute(recompute_hidden, "tp", [(i, i ^ 1) for i in range(tp_count)])
    pair = jnp.stack([recompute_hidden, partner])
    shifts = range(0, tp_count, 2)
    hidden = jnp.concatenate(
        [pair]
        + [
            lax.ppermute(pair, "tp", [(i, (i + k) % tp_count) for i in range(tp_count)])
            for k in shifts[1:]
        ]
    )
    sources = jnp.stack(
        [jnp.stack([(rank - k) % tp_count, ((rank - k) % tp_count) ^ 1]) for k in shifts]
    ).reshape(-1)
    weights = jnp.take(w_kv.reshape((tp_count, width) + w_kv.shape[1:]), sources, axis=0)
    widened = hidden.astype(jnp.float32)
    square_mean = jnp.sum(widened * widened, axis=(0, 4)) / (tp_count * width)
    normed = (widened * lax.rsqrt(square_mean + 1e-06)[None, ..., None]).astype(jnp.bfloat16)
    fresh = jnp.einsum("trcnd,tdskh->rcnskh", normed, weights, preferred_element_type=jnp.float32)
    fresh_pos = own_offsets[:, :, None] + own_rows.astype(jnp.float32)
    fresh_keys = rotate(fresh[:, :, :, 0], fresh_pos[..., None]).astype(jnp.bfloat16)
    fresh_values = fresh[:, :, :, 1].astype(jnp.bfloat16)
    fresh_scores = (
        jnp.einsum("rqkgd,rcnkd->rqkgcn", grouped, fresh_keys, preferred_element_type=jnp.float32)
        * score_scale
    )
    fresh_scores = fresh_scores.reshape(req_dev, qlen, kv_heads, group_size, -1)
    fresh_peak, fresh_sum, fresh_weights = summarize(fresh_scores, True)
    fresh_acc = jnp.einsum(
        "rqkgn,rnkd->rqkgd",
        fresh_weights,
        fresh_values.reshape(req_dev, -1, kv_heads, head_dim),
        preferred_element_type=jnp.float32,
    )
    visible = (steps_q[None, None, :] <= steps_q[None, :, None]) & (
        steps_q[None, None, :] < own_lengths[:, None, None]
    )
    own_scores = (
        jnp.einsum("rqkgd,rjkd->rqkgj", grouped, own_keys, preferred_element_type=jnp.float32)
        * score_scale
    )
    own_peak, own_sum, own_weights = summarize(own_scores, visible[:, :, None, None, :])
    own_acc = jnp.einsum(
        "rqkgj,rjkd->rqkgd", own_weights, own_values, preferred_element_type=jnp.float32
    )
    own_keys = rotate(question_kv[:, :, 0].astype(jnp.float32), qpos[None, :, None]).astype(
        jnp.bfloat16
    )
    own_values = question_kv[:, :, 1]
    tp_count = lax.axis_size("tp")
    rank = lax.axis_index("tp")
    width = recompute_hidden.shape[3]
    partner = lax.ppermute(recompute_hidden, "tp", [(i, i ^ 1) for i in range(tp_count)])
    pair = jnp.stack([recompute_hidden, partner])
    shifts = range(0, tp_count, 2)
    hidden = jnp.concatenate(
        [pair]
        + [
            lax.ppermute(pair, "tp", [(i, (i + k) % tp_count) for i in range(tp_count)])
            for k in shifts[1:]
        ]
    )
    sources = jnp.stack(
        [jnp.stack([(rank - k) % tp_count, ((rank - k) % tp_count) ^ 1]) for k in shifts]
    ).reshape(-1)
    weights = jnp.take(w_kv.reshape((tp_count, width) + w_kv.shape[1:]), sources, axis=0)
    widened = hidden.astype(jnp.float32)
    square_mean = jnp.sum(widened * widened, axis=(0, 4)) / (tp_count * width)
    normed = (widened * lax.rsqrt(square_mean + 1e-06)[None, ..., None]).astype(jnp.bfloat16)
    fresh = jnp.einsum("trcnd,tdskh->rcnskh", normed, weights, preferred_element_type=jnp.float32)
    fresh_pos = own_offsets[:, :, None] + own_rows.astype(jnp.float32)
    fresh_keys = rotate(fresh[:, :, :, 0], fresh_pos[..., None]).astype(jnp.bfloat16)
    fresh_values = fresh[:, :, :, 1].astype(jnp.bfloat16)
    fresh_scores = (
        jnp.einsum("rqkgd,rcnkd->rqkgcn", grouped, fresh_keys, preferred_element_type=jnp.float32)
        * score_scale
    )
    fresh_scores = fresh_scores.reshape(req_dev, qlen, kv_heads, group_size, -1)
    fresh_peak, fresh_sum, fresh_weights = summarize(fresh_scores, True)
    fresh_acc = jnp.einsum(
        "rqkgn,rnkd->rqkgd",
        fresh_weights,
        fresh_values.reshape(req_dev, -1, kv_heads, head_dim),
        preferred_element_type=jnp.float32,
    )
    visible = (steps_q[None, None, :] <= steps_q[None, :, None]) & (
        steps_q[None, None, :] < own_lengths[:, None, None]
    )
    own_scores = (
        jnp.einsum("rqkgd,rjkd->rqkgj", grouped, own_keys, preferred_element_type=jnp.float32)
        * score_scale
    )
    own_peak, own_sum, own_weights = summarize(own_scores, visible[:, :, None, None, :])
    own_acc = jnp.einsum(
        "rqkgj,rjkd->rqkgd", own_weights, own_values, preferred_element_type=jnp.float32
    )

    mine = span_pages[own_spans]
    unused_slots, page_index = local_pages(
        mine[:, :, None, :], jnp.arange(pool_count, dtype=jnp.int32)[:, None], pages_dev, peer_pages
    )
    row_ids = page_index[..., None] * page_rows + jnp.arange(page_rows, dtype=jnp.int32)
    replaced = jnp.any(row_ids[..., None] == own_rows[:, :, None, None, None, :], axis=-1)
    valid = jnp.logical_not(replaced).transpose(0, 2, 1, 3, 4).reshape(req_dev, pool_count, -1)
    valid = valid.astype(jnp.float32)
    angles = own_offsets[..., None] * frequencies(head_dim)
    tables = jnp.stack(
        [
            jnp.concatenate([jnp.cos(angles), jnp.cos(angles)], axis=-1),
            jnp.concatenate([-jnp.sin(angles), jnp.sin(angles)], axis=-1),
        ],
        axis=2,
    ).reshape(req_dev, 2 * n_slots, head_dim)
    local = (fresh_peak, fresh_sum, fresh_acc, own_peak, own_sum, own_acc, valid, tables)

    all_pages = span_pages[req_spans]
    slot_ids, unused_index = local_pages(all_pages, device, pages_dev, peer_pages)
    slot_ids = slot_ids.reshape((pool_count, req_dev) + slot_ids.shape[1:])
    arrivals = []
    for r in range(req_dev):
        outgoing = pool_kv[slot_ids[:, r]]
        if arrivals:
            arrivals[-1], outgoing, local = lax.optimization_barrier((arrivals[-1], outgoing, local))
        arrivals.append(lax.all_to_all(outgoing, "pool", split_axis=0, concat_axis=0, tiled=True))
    fresh_peak, fresh_sum, fresh_acc, own_peak, own_sum, own_acc, valid, tables = local

    flat_queries = queries.reshape(req_dev, qlen * heads, head_dim)
    outputs = []
    for r in range(req_dev):
        one = slice(r, r + 1)
        arrived = arrivals[r]
        if outputs:
            arrived, outputs[-1] = lax.optimization_barrier((arrived, outputs[-1]))
        cached = cached_attention(
            flat_queries[one],
            arrived.reshape(pool_count, 1, n_slots * peer_pages, 2, page_rows, head_dim),
            valid[one],
            tables[one],
            score_scale,
        )
        cached = (
            cached[0].reshape(1, qlen, kv_heads, group_size),
            cached[1].reshape(1, qlen, kv_heads, group_size),
            cached[2].reshape(1, qlen, kv_heads, group_size, head_dim),
        )
        total = combine(
            combine(cached, (fresh_peak[one], fresh_sum[one], fresh_acc[one])),
            (own_peak[one], own_sum[one], own_acc[one]),
        )
        attn = total[2] / total[1][..., None]
        live = steps_q < own_lengths[r]
        attn = (
            jnp.where(live[None, :, None, None, None], attn, 0.0)
            .astype(jnp.bfloat16)
            .reshape(1, qlen, heads * head_dim)
        )
        partial_out = jnp.einsum("rqh,hm->rqm", attn, w_out, preferred_element_type=jnp.float32)
        pieces = partial_out.astype(jnp.bfloat16).reshape(1, qlen, tp_count, -1)
        if r < req_dev - 1:
            rolled = jnp.take(
                pieces, (rank + jnp.arange(tp_count, dtype=jnp.int32)) % tp_count, axis=2
            )
            received = [rolled[:, :, 0]] + [
                lax.ppermute(
                    rolled[:, :, k], "tp", [(i, (i + k) % tp_count) for i in range(tp_count)]
                )
                for k in range(1, tp_count)
            ]
            reduced = jnp.sum(jnp.stack(received).astype(jnp.float32), axis=0)
        else:
            pieces = lax.all_to_all(
                pieces.transpose(2, 0, 1, 3), "tp", split_axis=0, concat_axis=0, tiled=True
            )
            reduced = jnp.sum(pieces.astype(jnp.float32), axis=0)
        outputs.append(reduced.astype(jnp.bfloat16))
    return jnp.concatenate(outputs, axis=0)


def solution(mesh):
    return jax.shard_map(
        shards,
        mesh=mesh,
        in_specs=(
            P("pool", "tp", None, None, None),
            P(),
            P(),
            P(),
            P(),
            P(),
            P("pool", None, "tp", None),
            P("pool", None, None, "tp", None),
            P("pool", None, None, "tp"),
            P(None, None, "tp", None),
            P("tp", None),
        ),
        out_specs=P("pool", None, "tp"),
        check_vma=False,
    )
```

```python
import functools

import jax
import jax.numpy as jnp
from jax import lax
from jax.experimental import pallas as pl
from jax.experimental.pallas import tpu as pltpu
from jax.sharding import PartitionSpec as P

THETA = 1000000.0
NEGATIVE = -1e30


def rotate(vectors, position):
    halfway = vectors.shape[-1] // 2
    frequency = THETA ** (-(jnp.arange(halfway, dtype=jnp.float32) * 2.0) / vectors.shape[-1])
    angles = position[..., None] * frequency
    cosine_part = jnp.cos(angles)
    sine_part = jnp.sin(angles)
    leading = vectors[..., :halfway]
    trailing = vectors[..., halfway:]
    return jnp.concatenate(
        [
            leading * cosine_part - trailing * sine_part,
            trailing * cosine_part + leading * sine_part,
        ],
        axis=-1,
    )


def summarize(scores, valid):
    masked = jnp.where(valid, scores, NEGATIVE)
    peak = jnp.max(masked, axis=-1)
    powers = jnp.where(valid, jnp.exp(masked - peak[..., None]), 0.0)
    return (peak, jnp.sum(powers, axis=-1), powers.astype(jnp.bfloat16))


def combine(former, latter):
    peak = jnp.maximum(former[0], latter[0])
    former_factor = jnp.exp(former[0] - peak)
    latter_factor = jnp.exp(latter[0] - peak)
    return (
        peak,
        former[1] * former_factor + latter[1] * latter_factor,
        former[2] * former_factor[..., None] + latter[2] * latter_factor[..., None],
    )


def merge_normalised(peaks, sums, normalised, axis):
    merged_peak = jnp.max(peaks, axis=axis)
    weight = sums * jnp.exp(peaks - jnp.expand_dims(merged_peak, axis))
    return (
        merged_peak,
        jnp.sum(weight, axis=axis),
        jnp.sum(normalised.astype(jnp.float32) * weight[..., None], axis=axis),
    )


def local_pages(pages, device, pages_dev, peer_pages):
    here = pages // pages_dev == device
    ranking = jnp.cumsum(here.astype(jnp.int32), axis=-1) - 1
    picks = here[..., None, :] & (
        ranking[..., None, :] == jnp.arange(peer_pages, dtype=jnp.int32)[:, None]
    )
    slot_ids = jnp.sum(jnp.where(picks, (pages % pages_dev)[..., None, :], 0), axis=-1)
    page_index = jnp.sum(jnp.where(picks, jnp.arange(pages.shape[-1], dtype=jnp.int32), 0), axis=-1)
    return (slot_ids, page_index)


def frequencies(head_dim):
    halfway = head_dim // 2
    return THETA ** (-(jnp.arange(halfway, dtype=jnp.float32) * 2.0) / head_dim)


SET_BLOCK = 16


def cached_kernel(scale, q_ref, kv_ref, valid_ref, table_ref, peak_ref, sum_ref, num_ref, m_acc, w_acc, n_acc):
    block = pl.program_id(1)
    n_blocks = pl.num_programs(1)
    n_pages = kv_ref.shape[2]
    page_rows = kv_ref.shape[4]
    head_dim = kv_ref.shape[5]
    n_slots = table_ref.shape[1] // 2
    slot_rows = (n_pages // n_slots) * page_rows

    @pl.when(block == 0)
    def _():
        m_acc[...] = jnp.full(m_acc.shape, NEGATIVE, jnp.float32)
        w_acc[...] = jnp.zeros(w_acc.shape, jnp.float32)
        n_acc[...] = jnp.zeros(n_acc.shape, jnp.float32)

    query = q_ref[0]
    table = table_ref[0]
    cosine = jnp.concatenate(
        [jnp.broadcast_to(table[2 * c : 2 * c + 1], (slot_rows, head_dim)) for c in range(n_slots)], axis=0
    )
    sine = jnp.concatenate(
        [jnp.broadcast_to(table[2 * c + 1 : 2 * c + 2], (slot_rows, head_dim)) for c in range(n_slots)], axis=0
    )

    def one_set(i, carry):
        keys = kv_ref[i, 0, :, 0].reshape(n_pages * page_rows, head_dim).astype(jnp.float32)
        values = kv_ref[i, 0, :, 1].reshape(n_pages * page_rows, head_dim)
        keys = (keys * cosine + pltpu.roll(keys, head_dim // 2, 1) * sine).astype(jnp.bfloat16)
        scores = lax.dot_general(
            keys, query, (((1,), (1,)), ((), ())), preferred_element_type=jnp.float32
        ) * scale
        valid = valid_ref[0, i] > 0.5
        masked = jnp.where(valid, scores, NEGATIVE)
        peak = jnp.max(masked, axis=0, keepdims=True)
        powers = jnp.exp(masked - jnp.maximum(peak, 0.1 * NEGATIVE))
        total = jnp.sum(powers, axis=0, keepdims=True)
        acc = lax.dot_general(
            values, powers.astype(jnp.bfloat16), (((0,), (0,)), ((), ())),
            preferred_element_type=jnp.float32,
        )
        inverse = 1.0 / jnp.maximum(total, 1.0)
        normalised = (acc * inverse).astype(jnp.bfloat16).astype(jnp.float32)
        old = m_acc[...]
        merged = jnp.maximum(old, peak)
        rescale = jnp.exp(old - merged)
        weight = total * jnp.exp(peak - merged)
        m_acc[...] = merged
        w_acc[...] = w_acc[...] * rescale + weight
        n_acc[...] = n_acc[...] * rescale + normalised * weight
        return carry

    lax.fori_loop(0, kv_ref.shape[0], one_set, 0)

    @pl.when(block == n_blocks - 1)
    def _():
        peak_ref[0] = m_acc[...]
        sum_ref[0] = w_acc[...]
        num_ref[0] = n_acc[...]


def cached_attention(queries, arrived, valid, tables, scale):
    req_dev, rows, head_dim = queries.shape
    pool_count = arrived.shape[0]
    kv_block = (SET_BLOCK,) + (1,) + arrived.shape[2:]
    valid = valid[..., None]
    peak, total, num = pl.pallas_call(
        functools.partial(cached_kernel, scale),
        grid=(req_dev, pool_count // SET_BLOCK),
        in_specs=[
            pl.BlockSpec((1, rows, head_dim), lambda r, j: (r, 0, 0)),
            pl.BlockSpec(kv_block, lambda r, j: (j, r, 0, 0, 0, 0)),
            pl.BlockSpec((1, SET_BLOCK, valid.shape[2], 1), lambda r, j: (r, j, 0, 0)),
            pl.BlockSpec((1,) + tables.shape[1:], lambda r, j: (r, 0, 0)),
        ],
        out_specs=[
            pl.BlockSpec((1, 1, rows), lambda r, j: (r, 0, 0)),
            pl.BlockSpec((1, 1, rows), lambda r, j: (r, 0, 0)),
            pl.BlockSpec((1, head_dim, rows), lambda r, j: (r, 0, 0)),
        ],
        out_shape=[
            jax.ShapeDtypeStruct((req_dev, 1, rows), jnp.float32),
            jax.ShapeDtypeStruct((req_dev, 1, rows), jnp.float32),
            jax.ShapeDtypeStruct((req_dev, head_dim, rows), jnp.float32),
        ],
        scratch_shapes=[
            pltpu.VMEM((1, rows), jnp.float32),
            pltpu.VMEM((1, rows), jnp.float32),
            pltpu.VMEM((head_dim, rows), jnp.float32),
        ],
        compiler_params=pltpu.CompilerParams(dimension_semantics=("parallel", "arbitrary")),
    )(queries, arrived, valid, tables)
    return (peak, total, jnp.swapaxes(num, 1, 2))

def shards(
    pool_kv,
    span_pages,
    req_spans,
    span_offsets,
    recompute_rows,
    question_lengths,
    question_q,
    question_kv,
    recompute_hidden,
    w_kv,
    w_out,
):
    pool_count = lax.axis_size("pool")
    device = lax.axis_index("pool")
    req_dev = question_q.shape[0]
    qlen = question_q.shape[1]
    heads = question_q.shape[2]
    head_dim = question_q.shape[3]
    pages_dev = pool_kv.shape[0]
    kv_heads = pool_kv.shape[1]
    page_rows = pool_kv.shape[3]
    group_size = heads // kv_heads
    n_slots = req_spans.shape[1]
    pages_span = span_pages.shape[1]
    span_rows = pages_span * page_rows
    peer_pages = pages_span // pool_count
    score_scale = head_dim ** (-0.5)
    first_request = device * req_dev
    own_spans = lax.dynamic_slice_in_dim(req_spans, first_request, req_dev, 0)
    own_offsets = lax.dynamic_slice_in_dim(span_offsets, first_request, req_dev, 0).astype(
        jnp.float32
    )
    own_rows = lax.dynamic_slice_in_dim(recompute_rows, first_request, req_dev, 0)
    own_lengths = lax.dynamic_slice_in_dim(question_lengths, first_request, req_dev, 0)
    steps_q = jnp.arange(qlen, dtype=jnp.int32)
    qpos = (n_slots * span_rows + steps_q).astype(jnp.float32)
    queries = rotate(question_q.astype(jnp.float32), qpos[None, :, None]).astype(jnp.bfloat16)
    grouped = queries.reshape(req_dev, qlen, kv_heads, group_size, head_dim)
    own_keys = rotate(question_kv[:, :, 0].astype(jnp.float32), qpos[None, :, None]).astype(
        jnp.bfloat16
    )
    own_values = question_kv[:, :, 1]
    tp_count = lax.axis_size("tp")
    rank = lax.axis_index("tp")
    width = recompute_hidden.shape[3]
    hidden = jnp.stack(
        [recompute_hidden]
        + [
            lax.ppermute(recompute_hidden, "tp", [(i, (i + k) % tp_count) for i in range(tp_count)])
            for k in range(1, tp_count)
        ]
    )
    weights = jnp.take(
        w_kv.reshape((tp_count, width) + w_kv.shape[1:]),
        (rank - jnp.arange(tp_count, dtype=jnp.int32)) % tp_count,
        axis=0,
    )
    widened = hidden.astype(jnp.float32)
    square_mean = jnp.sum(widened * widened, axis=(0, 4)) / (tp_count * width)
    normed = (widened * lax.rsqrt(square_mean + 1e-06)[None, ..., None]).astype(jnp.bfloat16)
    fresh = jnp.einsum("trcnd,tdskh->rcnskh", normed, weights, preferred_element_type=jnp.float32)
    fresh_pos = own_offsets[:, :, None] + own_rows.astype(jnp.float32)
    fresh_keys = rotate(fresh[:, :, :, 0], fresh_pos[..., None]).astype(jnp.bfloat16)
    fresh_values = fresh[:, :, :, 1].astype(jnp.bfloat16)
    fresh_scores = (
        jnp.einsum("rqkgd,rcnkd->rqkgcn", grouped, fresh_keys, preferred_element_type=jnp.float32)
        * score_scale
    )
    fresh_scores = fresh_scores.reshape(req_dev, qlen, kv_heads, group_size, -1)
    fresh_peak, fresh_sum, fresh_weights = summarize(fresh_scores, True)
    fresh_acc = jnp.einsum(
        "rqkgn,rnkd->rqkgd",
        fresh_weights,
        fresh_values.reshape(req_dev, -1, kv_heads, head_dim),
        preferred_element_type=jnp.float32,
    )
    visible = (steps_q[None, None, :] <= steps_q[None, :, None]) & (
        steps_q[None, None, :] < own_lengths[:, None, None]
    )
    own_scores = (
        jnp.einsum("rqkgd,rjkd->rqkgj", grouped, own_keys, preferred_element_type=jnp.float32)
        * score_scale
    )
    own_peak, own_sum, own_weights = summarize(own_scores, visible[:, :, None, None, :])
    own_acc = jnp.einsum(
        "rqkgj,rjkd->rqkgd", own_weights, own_values, preferred_element_type=jnp.float32
    )
    own_keys = rotate(question_kv[:, :, 0].astype(jnp.float32), qpos[None, :, None]).astype(
        jnp.bfloat16
    )
    own_values = question_kv[:, :, 1]
    tp_count = lax.axis_size("tp")
    rank = lax.axis_index("tp")
    width = recompute_hidden.shape[3]
    hidden = jnp.stack(
        [recompute_hidden]
        + [
            lax.ppermute(recompute_hidden, "tp", [(i, (i + k) % tp_count) for i in range(tp_count)])
            for k in range(1, tp_count)
        ]
    )
    weights = jnp.take(
        w_kv.reshape((tp_count, width) + w_kv.shape[1:]),
        (rank - jnp.arange(tp_count, dtype=jnp.int32)) % tp_count,
        axis=0,
    )
    widened = hidden.astype(jnp.float32)
    square_mean = jnp.sum(widened * widened, axis=(0, 4)) / (tp_count * width)
    normed = (widened * lax.rsqrt(square_mean + 1e-06)[None, ..., None]).astype(jnp.bfloat16)
    fresh = jnp.einsum("trcnd,tdskh->rcnskh", normed, weights, preferred_element_type=jnp.float32)
    fresh_pos = own_offsets[:, :, None] + own_rows.astype(jnp.float32)
    fresh_keys = rotate(fresh[:, :, :, 0], fresh_pos[..., None]).astype(jnp.bfloat16)
    fresh_values = fresh[:, :, :, 1].astype(jnp.bfloat16)
    fresh_scores = (
        jnp.einsum("rqkgd,rcnkd->rqkgcn", grouped, fresh_keys, preferred_element_type=jnp.float32)
        * score_scale
    )
    fresh_scores = fresh_scores.reshape(req_dev, qlen, kv_heads, group_size, -1)
    fresh_peak, fresh_sum, fresh_weights = summarize(fresh_scores, True)
    fresh_acc = jnp.einsum(
        "rqkgn,rnkd->rqkgd",
        fresh_weights,
        fresh_values.reshape(req_dev, -1, kv_heads, head_dim),
        preferred_element_type=jnp.float32,
    )
    visible = (steps_q[None, None, :] <= steps_q[None, :, None]) & (
        steps_q[None, None, :] < own_lengths[:, None, None]
    )
    own_scores = (
        jnp.einsum("rqkgd,rjkd->rqkgj", grouped, own_keys, preferred_element_type=jnp.float32)
        * score_scale
    )
    own_peak, own_sum, own_weights = summarize(own_scores, visible[:, :, None, None, :])
    own_acc = jnp.einsum(
        "rqkgj,rjkd->rqkgd", own_weights, own_values, preferred_element_type=jnp.float32
    )

    mine = span_pages[own_spans]
    unused_slots, page_index = local_pages(
        mine[:, :, None, :], jnp.arange(pool_count, dtype=jnp.int32)[:, None], pages_dev, peer_pages
    )
    row_ids = page_index[..., None] * page_rows + jnp.arange(page_rows, dtype=jnp.int32)
    replaced = jnp.any(row_ids[..., None] == own_rows[:, :, None, None, None, :], axis=-1)
    valid = jnp.logical_not(replaced).transpose(0, 2, 1, 3, 4).reshape(req_dev, pool_count, -1)
    valid = valid.astype(jnp.float32)
    angles = own_offsets[..., None] * frequencies(head_dim)
    tables = jnp.stack(
        [
            jnp.concatenate([jnp.cos(angles), jnp.cos(angles)], axis=-1),
            jnp.concatenate([-jnp.sin(angles), jnp.sin(angles)], axis=-1),
        ],
        axis=2,
    ).reshape(req_dev, 2 * n_slots, head_dim)
    local = (fresh_peak, fresh_sum, fresh_acc, own_peak, own_sum, own_acc, valid, tables)

    all_pages = span_pages[req_spans]
    slot_ids, unused_index = local_pages(all_pages, device, pages_dev, peer_pages)
    slot_ids = slot_ids.reshape((pool_count, req_dev) + slot_ids.shape[1:])
    arrivals = []
    for r in range(req_dev):
        outgoing = pool_kv[slot_ids[:, r]]
        if arrivals:
            arrivals[-1], outgoing, local = lax.optimization_barrier((arrivals[-1], outgoing, local))
        arrivals.append(lax.all_to_all(outgoing, "pool", split_axis=0, concat_axis=0, tiled=True))
    fresh_peak, fresh_sum, fresh_acc, own_peak, own_sum, own_acc, valid, tables = local

    flat_queries = queries.reshape(req_dev, qlen * heads, head_dim)
    outputs = []
    for r in range(req_dev):
        one = slice(r, r + 1)
        arrived = arrivals[r]
        if outputs:
            arrived, outputs[-1] = lax.optimization_barrier((arrived, outputs[-1]))
        cached = cached_attention(
            flat_queries[one],
            arrived.reshape(pool_count, 1, n_slots * peer_pages, 2, page_rows, head_dim),
            valid[one],
            tables[one],
            score_scale,
        )
        cached = (
            cached[0].reshape(1, qlen, kv_heads, group_size),
            cached[1].reshape(1, qlen, kv_heads, group_size),
            cached[2].reshape(1, qlen, kv_heads, group_size, head_dim),
        )
        total = combine(
            combine(cached, (fresh_peak[one], fresh_sum[one], fresh_acc[one])),
            (own_peak[one], own_sum[one], own_acc[one]),
        )
        attn = total[2] / total[1][..., None]
        live = steps_q < own_lengths[r]
        attn = (
            jnp.where(live[None, :, None, None, None], attn, 0.0)
            .astype(jnp.bfloat16)
            .reshape(1, qlen, heads * head_dim)
        )
        partial_out = jnp.einsum("rqh,hm->rqm", attn, w_out, preferred_element_type=jnp.float32)
        pieces = partial_out.astype(jnp.bfloat16).reshape(1, qlen, tp_count, -1)
        if r < req_dev - 1:
            rolled = jnp.take(
                pieces, (rank + jnp.arange(tp_count, dtype=jnp.int32)) % tp_count, axis=2
            )
            received = [rolled[:, :, 0]] + [
                lax.ppermute(
                    rolled[:, :, k], "tp", [(i, (i + k) % tp_count) for i in range(tp_count)]
                )
                for k in range(1, tp_count)
            ]
            reduced = jnp.sum(jnp.stack(received).astype(jnp.float32), axis=0)
        else:
            pieces = lax.all_to_all(
                pieces.transpose(2, 0, 1, 3), "tp", split_axis=0, concat_axis=0, tiled=True
            )
            reduced = jnp.sum(pieces.astype(jnp.float32), axis=0)
        outputs.append(reduced.astype(jnp.bfloat16))
    return jnp.concatenate(outputs, axis=0)


def solution(mesh):
    return jax.shard_map(
        shards,
        mesh=mesh,
        in_specs=(
            P("pool", "tp", None, None, None),
            P(),
            P(),
            P(),
            P(),
            P(),
            P("pool", None, "tp", None),
            P("pool", None, None, "tp", None),
            P("pool", None, None, "tp"),
            P(None, None, "tp", None),
            P("tp", None),
        ),
        out_specs=P("pool", None, "tp"),
        check_vma=False,
    )
```

```python
import functools

import jax
import jax.numpy as jnp
from jax import lax
from jax.experimental import pallas as pl
from jax.experimental.pallas import tpu as pltpu
from jax.sharding import PartitionSpec as P

THETA = 1000000.0
NEGATIVE = -1e30


def rotate(vectors, position):
    halfway = vectors.shape[-1] // 2
    frequency = THETA ** (-(jnp.arange(halfway, dtype=jnp.float32) * 2.0) / vectors.shape[-1])
    angles = position[..., None] * frequency
    cosine_part = jnp.cos(angles)
    sine_part = jnp.sin(angles)
    leading = vectors[..., :halfway]
    trailing = vectors[..., halfway:]
    return jnp.concatenate(
        [
            leading * cosine_part - trailing * sine_part,
            trailing * cosine_part + leading * sine_part,
        ],
        axis=-1,
    )


def summarize(scores, valid):
    masked = jnp.where(valid, scores, NEGATIVE)
    peak = jnp.max(masked, axis=-1)
    powers = jnp.where(valid, jnp.exp(masked - peak[..., None]), 0.0)
    return (peak, jnp.sum(powers, axis=-1), powers.astype(jnp.bfloat16))


def combine(former, latter):
    peak = jnp.maximum(former[0], latter[0])
    former_factor = jnp.exp(former[0] - peak)
    latter_factor = jnp.exp(latter[0] - peak)
    return (
        peak,
        former[1] * former_factor + latter[1] * latter_factor,
        former[2] * former_factor[..., None] + latter[2] * latter_factor[..., None],
    )


def merge_normalised(peaks, sums, normalised, axis):
    merged_peak = jnp.max(peaks, axis=axis)
    weight = sums * jnp.exp(peaks - jnp.expand_dims(merged_peak, axis))
    return (
        merged_peak,
        jnp.sum(weight, axis=axis),
        jnp.sum(normalised.astype(jnp.float32) * weight[..., None], axis=axis),
    )


def local_pages(pages, device, pages_dev, peer_pages):
    here = pages // pages_dev == device
    ranking = jnp.cumsum(here.astype(jnp.int32), axis=-1) - 1
    picks = here[..., None, :] & (
        ranking[..., None, :] == jnp.arange(peer_pages, dtype=jnp.int32)[:, None]
    )
    slot_ids = jnp.sum(jnp.where(picks, (pages % pages_dev)[..., None, :], 0), axis=-1)
    page_index = jnp.sum(jnp.where(picks, jnp.arange(pages.shape[-1], dtype=jnp.int32), 0), axis=-1)
    return (slot_ids, page_index)


def frequencies(head_dim):
    halfway = head_dim // 2
    return THETA ** (-(jnp.arange(halfway, dtype=jnp.float32) * 2.0) / head_dim)


SET_BLOCK = 8


def cached_kernel(scale, q_ref, kv_ref, valid_ref, table_ref, peak_ref, sum_ref, num_ref, m_acc, w_acc, n_acc):
    block = pl.program_id(1)
    n_blocks = pl.num_programs(1)
    n_pages = kv_ref.shape[2]
    page_rows = kv_ref.shape[4]
    head_dim = kv_ref.shape[5]
    n_slots = table_ref.shape[1] // 2
    slot_rows = (n_pages // n_slots) * page_rows

    @pl.when(block == 0)
    def _():
        m_acc[...] = jnp.full(m_acc.shape, NEGATIVE, jnp.float32)
        w_acc[...] = jnp.zeros(w_acc.shape, jnp.float32)
        n_acc[...] = jnp.zeros(n_acc.shape, jnp.float32)

    query = q_ref[0]
    table = table_ref[0]
    cosine = jnp.concatenate(
        [jnp.broadcast_to(table[2 * c : 2 * c + 1], (slot_rows, head_dim)) for c in range(n_slots)], axis=0
    )
    sine = jnp.concatenate(
        [jnp.broadcast_to(table[2 * c + 1 : 2 * c + 2], (slot_rows, head_dim)) for c in range(n_slots)], axis=0
    )

    def one_set(i, carry):
        keys = kv_ref[i, 0, :, 0].reshape(n_pages * page_rows, head_dim).astype(jnp.float32)
        values = kv_ref[i, 0, :, 1].reshape(n_pages * page_rows, head_dim)
        keys = (keys * cosine + pltpu.roll(keys, head_dim // 2, 1) * sine).astype(jnp.bfloat16)
        scores = lax.dot_general(
            keys, query, (((1,), (1,)), ((), ())), preferred_element_type=jnp.float32
        ) * scale
        valid = valid_ref[0, i] > 0.5
        masked = jnp.where(valid, scores, NEGATIVE)
        peak = jnp.max(masked, axis=0, keepdims=True)
        powers = jnp.exp(masked - jnp.maximum(peak, 0.1 * NEGATIVE))
        total = jnp.sum(powers, axis=0, keepdims=True)
        acc = lax.dot_general(
            values, powers.astype(jnp.bfloat16), (((0,), (0,)), ((), ())),
            preferred_element_type=jnp.float32,
        )
        inverse = 1.0 / jnp.maximum(total, 1.0)
        normalised = (acc * inverse).astype(jnp.bfloat16).astype(jnp.float32)
        old = m_acc[...]
        merged = jnp.maximum(old, peak)
        rescale = jnp.exp(old - merged)
        weight = total * jnp.exp(peak - merged)
        m_acc[...] = merged
        w_acc[...] = w_acc[...] * rescale + weight
        n_acc[...] = n_acc[...] * rescale + normalised * weight
        return carry

    lax.fori_loop(0, kv_ref.shape[0], one_set, 0)

    @pl.when(block == n_blocks - 1)
    def _():
        peak_ref[0] = m_acc[...]
        sum_ref[0] = w_acc[...]
        num_ref[0] = n_acc[...].T


def cached_attention(queries, arrived, valid, tables, scale):
    req_dev, rows, head_dim = queries.shape
    pool_count = arrived.shape[0]
    kv_block = (SET_BLOCK,) + (1,) + arrived.shape[2:]
    valid = valid[..., None]
    peak, total, num = pl.pallas_call(
        functools.partial(cached_kernel, scale),
        grid=(req_dev, pool_count // SET_BLOCK),
        in_specs=[
            pl.BlockSpec((1, rows, head_dim), lambda r, j: (r, 0, 0)),
            pl.BlockSpec(kv_block, lambda r, j: (j, r, 0, 0, 0, 0)),
            pl.BlockSpec((1, SET_BLOCK, valid.shape[2], 1), lambda r, j: (r, j, 0, 0)),
            pl.BlockSpec((1,) + tables.shape[1:], lambda r, j: (r, 0, 0)),
        ],
        out_specs=[
            pl.BlockSpec((1, 1, rows), lambda r, j: (r, 0, 0)),
            pl.BlockSpec((1, 1, rows), lambda r, j: (r, 0, 0)),
            pl.BlockSpec((1, rows, head_dim), lambda r, j: (r, 0, 0)),
        ],
        out_shape=[
            jax.ShapeDtypeStruct((req_dev, 1, rows), jnp.float32),
            jax.ShapeDtypeStruct((req_dev, 1, rows), jnp.float32),
            jax.ShapeDtypeStruct((req_dev, rows, head_dim), jnp.float32),
        ],
        scratch_shapes=[
            pltpu.VMEM((1, rows), jnp.float32),
            pltpu.VMEM((1, rows), jnp.float32),
            pltpu.VMEM((head_dim, rows), jnp.float32),
        ],
        compiler_params=pltpu.CompilerParams(dimension_semantics=("parallel", "arbitrary")),
    )(queries, arrived, valid, tables)
    return (peak, total, num)

def shards(
    pool_kv,
    span_pages,
    req_spans,
    span_offsets,
    recompute_rows,
    question_lengths,
    question_q,
    question_kv,
    recompute_hidden,
    w_kv,
    w_out,
):
    pool_count = lax.axis_size("pool")
    device = lax.axis_index("pool")
    req_dev = question_q.shape[0]
    qlen = question_q.shape[1]
    heads = question_q.shape[2]
    head_dim = question_q.shape[3]
    pages_dev = pool_kv.shape[0]
    kv_heads = pool_kv.shape[1]
    page_rows = pool_kv.shape[3]
    group_size = heads // kv_heads
    n_slots = req_spans.shape[1]
    pages_span = span_pages.shape[1]
    span_rows = pages_span * page_rows
    peer_pages = pages_span // pool_count
    score_scale = head_dim ** (-0.5)
    first_request = device * req_dev
    own_spans = lax.dynamic_slice_in_dim(req_spans, first_request, req_dev, 0)
    own_offsets = lax.dynamic_slice_in_dim(span_offsets, first_request, req_dev, 0).astype(
        jnp.float32
    )
    own_rows = lax.dynamic_slice_in_dim(recompute_rows, first_request, req_dev, 0)
    own_lengths = lax.dynamic_slice_in_dim(question_lengths, first_request, req_dev, 0)
    steps_q = jnp.arange(qlen, dtype=jnp.int32)
    qpos = (n_slots * span_rows + steps_q).astype(jnp.float32)
    queries = rotate(question_q.astype(jnp.float32), qpos[None, :, None]).astype(jnp.bfloat16)
    grouped = queries.reshape(req_dev, qlen, kv_heads, group_size, head_dim)
    own_keys = rotate(question_kv[:, :, 0].astype(jnp.float32), qpos[None, :, None]).astype(
        jnp.bfloat16
    )
    own_values = question_kv[:, :, 1]
    tp_count = lax.axis_size("tp")
    rank = lax.axis_index("tp")
    width = recompute_hidden.shape[3]
    hidden = jnp.stack(
        [recompute_hidden]
        + [
            lax.ppermute(recompute_hidden, "tp", [(i, (i + k) % tp_count) for i in range(tp_count)])
            for k in range(1, tp_count)
        ]
    )
    weights = jnp.take(
        w_kv.reshape((tp_count, width) + w_kv.shape[1:]),
        (rank - jnp.arange(tp_count, dtype=jnp.int32)) % tp_count,
        axis=0,
    )
    widened = hidden.astype(jnp.float32)
    square_mean = jnp.sum(widened * widened, axis=(0, 4)) / (tp_count * width)
    normed = (widened * lax.rsqrt(square_mean + 1e-06)[None, ..., None]).astype(jnp.bfloat16)
    fresh = jnp.einsum("trcnd,tdskh->rcnskh", normed, weights, preferred_element_type=jnp.float32)
    fresh_pos = own_offsets[:, :, None] + own_rows.astype(jnp.float32)
    fresh_keys = rotate(fresh[:, :, :, 0], fresh_pos[..., None]).astype(jnp.bfloat16)
    fresh_values = fresh[:, :, :, 1].astype(jnp.bfloat16)
    fresh_scores = (
        jnp.einsum("rqkgd,rcnkd->rqkgcn", grouped, fresh_keys, preferred_element_type=jnp.float32)
        * score_scale
    )
    fresh_scores = fresh_scores.reshape(req_dev, qlen, kv_heads, group_size, -1)
    fresh_peak, fresh_sum, fresh_weights = summarize(fresh_scores, True)
    fresh_acc = jnp.einsum(
        "rqkgn,rnkd->rqkgd",
        fresh_weights,
        fresh_values.reshape(req_dev, -1, kv_heads, head_dim),
        preferred_element_type=jnp.float32,
    )
    visible = (steps_q[None, None, :] <= steps_q[None, :, None]) & (
        steps_q[None, None, :] < own_lengths[:, None, None]
    )
    own_scores = (
        jnp.einsum("rqkgd,rjkd->rqkgj", grouped, own_keys, preferred_element_type=jnp.float32)
        * score_scale
    )
    own_peak, own_sum, own_weights = summarize(own_scores, visible[:, :, None, None, :])
    own_acc = jnp.einsum(
        "rqkgj,rjkd->rqkgd", own_weights, own_values, preferred_element_type=jnp.float32
    )
    own_keys = rotate(question_kv[:, :, 0].astype(jnp.float32), qpos[None, :, None]).astype(
        jnp.bfloat16
    )
    own_values = question_kv[:, :, 1]
    tp_count = lax.axis_size("tp")
    rank = lax.axis_index("tp")
    width = recompute_hidden.shape[3]
    hidden = jnp.stack(
        [recompute_hidden]
        + [
            lax.ppermute(recompute_hidden, "tp", [(i, (i + k) % tp_count) for i in range(tp_count)])
            for k in range(1, tp_count)
        ]
    )
    weights = jnp.take(
        w_kv.reshape((tp_count, width) + w_kv.shape[1:]),
        (rank - jnp.arange(tp_count, dtype=jnp.int32)) % tp_count,
        axis=0,
    )
    widened = hidden.astype(jnp.float32)
    square_mean = jnp.sum(widened * widened, axis=(0, 4)) / (tp_count * width)
    normed = (widened * lax.rsqrt(square_mean + 1e-06)[None, ..., None]).astype(jnp.bfloat16)
    fresh = jnp.einsum("trcnd,tdskh->rcnskh", normed, weights, preferred_element_type=jnp.float32)
    fresh_pos = own_offsets[:, :, None] + own_rows.astype(jnp.float32)
    fresh_keys = rotate(fresh[:, :, :, 0], fresh_pos[..., None]).astype(jnp.bfloat16)
    fresh_values = fresh[:, :, :, 1].astype(jnp.bfloat16)
    fresh_scores = (
        jnp.einsum("rqkgd,rcnkd->rqkgcn", grouped, fresh_keys, preferred_element_type=jnp.float32)
        * score_scale
    )
    fresh_scores = fresh_scores.reshape(req_dev, qlen, kv_heads, group_size, -1)
    fresh_peak, fresh_sum, fresh_weights = summarize(fresh_scores, True)
    fresh_acc = jnp.einsum(
        "rqkgn,rnkd->rqkgd",
        fresh_weights,
        fresh_values.reshape(req_dev, -1, kv_heads, head_dim),
        preferred_element_type=jnp.float32,
    )
    visible = (steps_q[None, None, :] <= steps_q[None, :, None]) & (
        steps_q[None, None, :] < own_lengths[:, None, None]
    )
    own_scores = (
        jnp.einsum("rqkgd,rjkd->rqkgj", grouped, own_keys, preferred_element_type=jnp.float32)
        * score_scale
    )
    own_peak, own_sum, own_weights = summarize(own_scores, visible[:, :, None, None, :])
    own_acc = jnp.einsum(
        "rqkgj,rjkd->rqkgd", own_weights, own_values, preferred_element_type=jnp.float32
    )

    mine = span_pages[own_spans]
    unused_slots, page_index = local_pages(
        mine[:, :, None, :], jnp.arange(pool_count, dtype=jnp.int32)[:, None], pages_dev, peer_pages
    )
    row_ids = page_index[..., None] * page_rows + jnp.arange(page_rows, dtype=jnp.int32)
    replaced = jnp.any(row_ids[..., None] == own_rows[:, :, None, None, None, :], axis=-1)
    valid = jnp.logical_not(replaced).transpose(0, 2, 1, 3, 4).reshape(req_dev, pool_count, -1)
    valid = valid.astype(jnp.float32)
    angles = own_offsets[..., None] * frequencies(head_dim)
    tables = jnp.stack(
        [
            jnp.concatenate([jnp.cos(angles), jnp.cos(angles)], axis=-1),
            jnp.concatenate([-jnp.sin(angles), jnp.sin(angles)], axis=-1),
        ],
        axis=2,
    ).reshape(req_dev, 2 * n_slots, head_dim)
    local = (fresh_peak, fresh_sum, fresh_acc, own_peak, own_sum, own_acc, valid, tables)

    all_pages = span_pages[req_spans]
    slot_ids, unused_index = local_pages(all_pages, device, pages_dev, peer_pages)
    slot_ids = slot_ids.reshape((pool_count, req_dev) + slot_ids.shape[1:])
    arrivals = []
    for r in range(req_dev):
        outgoing = pool_kv[slot_ids[:, r]]
        if arrivals:
            arrivals[-1], outgoing, local = lax.optimization_barrier((arrivals[-1], outgoing, local))
        arrivals.append(lax.all_to_all(outgoing, "pool", split_axis=0, concat_axis=0, tiled=True))
    fresh_peak, fresh_sum, fresh_acc, own_peak, own_sum, own_acc, valid, tables = local

    flat_queries = queries.reshape(req_dev, qlen * heads, head_dim)
    outputs = []
    for r in range(req_dev):
        one = slice(r, r + 1)
        arrived = arrivals[r]
        if outputs:
            arrived, outputs[-1] = lax.optimization_barrier((arrived, outputs[-1]))
        cached = cached_attention(
            flat_queries[one],
            arrived.reshape(pool_count, 1, n_slots * peer_pages, 2, page_rows, head_dim),
            valid[one],
            tables[one],
            score_scale,
        )
        cached = (
            cached[0].reshape(1, qlen, kv_heads, group_size),
            cached[1].reshape(1, qlen, kv_heads, group_size),
            cached[2].reshape(1, qlen, kv_heads, group_size, head_dim),
        )
        total = combine(
            combine(cached, (fresh_peak[one], fresh_sum[one], fresh_acc[one])),
            (own_peak[one], own_sum[one], own_acc[one]),
        )
        attn = total[2] / total[1][..., None]
        live = steps_q < own_lengths[r]
        attn = (
            jnp.where(live[None, :, None, None, None], attn, 0.0)
            .astype(jnp.bfloat16)
            .reshape(1, qlen, heads * head_dim)
        )
        partial_out = jnp.einsum("rqh,hm->rqm", attn, w_out, preferred_element_type=jnp.float32)
        pieces = partial_out.astype(jnp.bfloat16).reshape(1, qlen, tp_count, -1)
        if r < req_dev - 1:
            rolled = jnp.take(
                pieces, (rank + jnp.arange(tp_count, dtype=jnp.int32)) % tp_count, axis=2
            )
            received = [rolled[:, :, 0]] + [
                lax.ppermute(
                    rolled[:, :, k], "tp", [(i, (i + k) % tp_count) for i in range(tp_count)]
                )
                for k in range(1, tp_count)
            ]
            reduced = jnp.sum(jnp.stack(received).astype(jnp.float32), axis=0)
        else:
            pieces = lax.all_to_all(
                pieces.transpose(2, 0, 1, 3), "tp", split_axis=0, concat_axis=0, tiled=True
            )
            reduced = jnp.sum(pieces.astype(jnp.float32), axis=0)
        outputs.append(reduced.astype(jnp.bfloat16))
    return jnp.concatenate(outputs, axis=0)


def solution(mesh):
    return jax.shard_map(
        shards,
        mesh=mesh,
        in_specs=(
            P("pool", "tp", None, None, None),
            P(),
            P(),
            P(),
            P(),
            P(),
            P("pool", None, "tp", None),
            P("pool", None, None, "tp", None),
            P("pool", None, None, "tp"),
            P(None, None, "tp", None),
            P("tp", None),
        ),
        out_specs=P("pool", None, "tp"),
        check_vma=False,
    )
```
